32 devices in a mesh: section: 4 (over y, x), tp: 4 (over z), mirror: 2 (over core).
Axes of the slice: x: 2, y: 2, z: 4, core: 2. Of those that a mesh axis runs over, the one named last changes fastest.
Arguments:
- feats: bfloat16 [2, 2, 128, 5120], P('mirror', None, 'tp'), may hold values from -16 to 16
- types: int32 [2, 2, 128], P('mirror', None, 'tp'), may hold values from 0 to 63
- segs: int32 [2, 2, 5, 128], P('mirror'), may hold values from 0 to 3, never falling along the last dimension, each value on 1 to 64 neighbouring positions
- type_table: bfloat16 [64, 5120], replicated, may hold values from -3 to 3
- gains: float32 [2, 4, 5120], P('mirror', 'section'), may hold values from 0.25 to 1.75, as said below
- w_qkv: bfloat16 [2, 4, 3, 5120, 512], P('mirror', 'section', None, None, 'tp'), may hold values from -8 to 8, as said below
- w_out: bfloat16 [2, 4, 512, 5120], P('mirror', 'section', 'tp'), as said below
- carry_acts: bfloat16 [2, 4, 128, 5120], P('mirror', 'section', 'tp'), may hold values from -16 to 16
- grad_in: bfloat16 [2, 4, 128, 5120], P('mirror', 'section', 'tp'), may hold values from -6 to 6
- saved: bfloat16 [2, 4, 2, 128, 5120], P('mirror', 'section', None, 'tp'), may hold values from -16 to 16
- cotangent: bfloat16 [2, 2, 128, 5120], P('mirror', None, 'tp'), may hold values from -6 to 6
Outputs:
- acts: bfloat16 [2, 4, 2, 128, 5120], P('mirror', 'section', None, 'tp')
- grad_acts: bfloat16 [2, 4, 2, 128, 5120], P('mirror', 'section', None, 'tp')
- grad_qkv: bfloat16 [2, 4, 3, 5120, 512], P('mirror', 'section', None, None, 'tp')
- grad_out: bfloat16 [2, 4, 512, 5120], P('mirror', 'section', 'tp')
The draws below stay inside these ranges and needn't reach their ends.
Inputs may be any that keep to these rules, and one draw needn't show every extreme that they name: w_qkv[1, k] equals w_qkv[0, 3 - k]. w_out[1, k] equals w_out[0, 3 - k]. gains[1, k] equals gains[0, 3 - k]. `segs`: segment numbers never fall along a micro-batch; each segment holds at most half of 128 tokens, and one holds exactly that many.
All inputs are finite; a program needn't handle non-finite values.
Results may differ from the reference program's by a relative error of at most 0.015.
Values may be sent and summed in bfloat16 or wider, within the bound.
No kernel may reach another device: no remote copies, remote signals or barrier semaphores. Data moves between devices by JAX's collectives and lax.ppermute only.
A program may use at most 128 MiB of HBM per device.

```python
import math
import jax
import jax.numpy as jnp
import numpy as np
from jax import lax

D = 5120
HD = 128
NTYPES = 64
SEQ = 128
STEPS = 2
HEADS = 4
INNER = 512
LAYERS = 4
PIPES = 2
WINDOW_MB = 5
N_TP = 4


def paired_rows(key, leading):
    first_key = jax.random.fold_in(key, 0)
    values = jnp.clip(jax.random.normal(first_key, leading + (SEQ, D), jnp.float32), -4.0, 4.0)
    return values.astype(jnp.bfloat16)


def stacked_replicas(values):
    return jnp.stack([values, jnp.flip(values, axis=0)])


def draw_feats(key, part):
    return paired_rows(jax.random.fold_in(key, 1), (PIPES, STEPS))


def draw_carry_acts(key, part):
    return paired_rows(jax.random.fold_in(key, 2), (PIPES, LAYERS))


def draw_saved(key, part):
    return paired_rows(jax.random.fold_in(key, 3), (PIPES, LAYERS, STEPS))


def draw_w_qkv(key, part):
    first_key = jax.random.fold_in(jax.random.fold_in(key, 4), 0)
    spread = 1.0 / math.sqrt(D)
    values = jnp.clip(jax.random.normal(first_key, (LAYERS, 3, D, INNER), jnp.float32), -6.0, 6.0) * spread
    return stacked_replicas(values.astype(jnp.bfloat16))


def draw_w_out(key, part):
    base_key = jax.random.fold_in(key, 5)
    values = jnp.clip(jax.random.normal(base_key, (LAYERS, INNER, D), jnp.float32), -6.0, 6.0) / math.sqrt(4.0 * HD)
    return stacked_replicas(values.astype(jnp.bfloat16))


def draw_gains(key, part):
    base_key = jax.random.fold_in(key, 6)
    values = 1.0 + 0.15 * jnp.clip(jax.random.normal(base_key, (LAYERS, D), jnp.float32), -5.0, 5.0)
    return stacked_replicas(values)


def set_ends(drawn, rng, low, largest):
    longest = drawn.shape.index(max(drawn.shape))
    spots = []
    for shift in (0, 1):
        where = [jax.random.randint(jax.random.fold_in(rng, axis), (), 0, length) for axis, length in enumerate(drawn.shape)]
        where[longest] = (where[longest] + shift) % drawn.shape[longest]
        spots.append(tuple(where))
    return drawn.at[spots[0]].set(low).at[spots[1]].set(largest)


def level_of(stream_key, shape, cuts, low, largest):
    gain = 1.0
    for dim, blocks in cuts:
        draws = jax.random.uniform(jax.random.fold_in(jax.random.fold_in(stream_key, 6), dim), (blocks,), jnp.float32, low / len(cuts), largest / len(cuts))
        gain = gain * jnp.repeat(jnp.exp(draws), shape[dim] // blocks).reshape((-1,) + (1,) * (len(shape) - 1 - dim))
    return gain


def cumulative_ranks(count, slope):
    weights = [(1 << 20) // math.isqrt(grade ** slope) + 1 for grade in range(1, count + 1)]
    scale = 1 + sum(weights) // (1 << 30)
    return np.cumsum(np.array([max(1, weight // scale) for weight in weights]))


def ranked_ids(key, dims, amount, skew):
    grid = cumulative_ranks(amount, skew)
    pick = jax.random.randint(jax.random.fold_in(key, 1), dims, 0, int(grid[amount - 1]))
    standing = jnp.searchsorted(jnp.asarray(grid, jnp.int32), pick, side="right")
    return jax.random.permutation(jax.random.fold_in(key, 2), amount)[standing].astype(jnp.int32)


def profile(count, total, limit, skew):
    portions = [(1 << 20) // math.isqrt(grade ** skew) + 1 for grade in range(2, count + 1)]
    spare, given = total - limit - (count - 1), [1] * (count - 1)
    while spare > 0:
        candidates = [i for i in range(count - 1) if given[i] < limit]
        pool, remaining = sum([portions[i] for i in candidates]), spare
        for i in candidates:
            more = min(limit - given[i], max(1, remaining * portions[i] // pool), spare)
            given[i] = given[i] + more
            spare = spare - more
    return np.array([limit] + given)


def ragged_sizes(stream_key, amount, total, limit, slope):
    if amount == 2:
        one = jax.random.randint(stream_key, (), max(1, total - limit), min(limit, total - 1) + 1)
        return jnp.stack([one, total - one])
    sizes = jnp.asarray(profile(amount, total, limit, slope), jnp.int32)
    couples = (amount - 1) // 2
    source_of, receiver = sizes[1:1 + 2 * couples:2], sizes[2:2 + 2 * couples:2]
    margin = jnp.minimum(source_of - 1, limit - receiver)
    moved = jax.random.randint(jax.random.fold_in(stream_key, 1), (couples,), 0, 1 << 20) % (margin + 1)
    sizes = sizes.at[1:1 + 2 * couples:2].set(source_of - moved).at[2:2 + 2 * couples:2].set(receiver + moved)
    return sizes[jax.random.permutation(jax.random.fold_in(stream_key, 2), amount)]


def centred(key, extent, scale, reach, shards=(), held_as=jnp.bfloat16):
    loudness = level_of(key, extent, shards, -0.22, 0.18) if shards else 1.0
    result = jax.random.normal(key, extent, jnp.float32) * scale * loudness
    return jnp.minimum(jnp.maximum(result, -reach), reach).astype(held_as)


def setup_inputs(seed: int = 0) -> dict:
    key_list = jax.random.split(jax.random.key(seed), 12)
    feats = draw_feats(jax.random.fold_in(key_list[11], 71), 0)
    types = set_ends(ranked_ids(key_list[1], (PIPES, STEPS, SEQ), NTYPES, 2), jax.random.fold_in(key_list[1], 3), 0, NTYPES - 1).astype(jnp.int32)
    segs = jax.vmap(lambda own: jnp.searchsorted(jnp.cumsum(ragged_sizes(own, 4, SEQ, SEQ // 2, 1)), jnp.arange(SEQ), side="right"))(jax.random.split(key_list[2], PIPES * 2 * WINDOW_MB)).reshape((PIPES, 2, WINDOW_MB, SEQ)).astype(jnp.int32)
    type_table = centred(key_list[3], (NTYPES, D), 0.5, 3.0)
    gains = draw_gains(jax.random.fold_in(key_list[11], 71), 0)
    w_qkv = draw_w_qkv(jax.random.fold_in(key_list[11], 71), 0)
    w_out = draw_w_out(jax.random.fold_in(key_list[11], 71), 0)
    carry_acts = draw_carry_acts(jax.random.fold_in(key_list[11], 71), 0)
    grad_in = centred(key_list[8], (PIPES, LAYERS, SEQ, D), 1.0, 6.0, ((0, 2), (1, 4), (2, 4)))
    saved = draw_saved(jax.random.fold_in(key_list[11], 71), 0)
    cotangent = centred(key_list[10], (PIPES, STEPS, SEQ, D), 1.0, 6.0, ((0, 2), (2, 4)))
    return dict(feats=feats, types=types, segs=segs, type_table=type_table, gains=gains, w_qkv=w_qkv, w_out=w_out, carry_acts=carry_acts, grad_in=grad_in, saved=saved, cotangent=cotangent)


def normalize(values, gain_row):
    mean_square = lax.optimization_barrier(jnp.mean(values * values, axis=-1, keepdims=True))
    return values * lax.rsqrt(mean_square + 1e-05) * gain_row

def segment_mask(segment_ids):
    position = jnp.arange(segment_ids.shape[0], dtype=jnp.int32)
    causal = position[None, :] <= position[:, None]
    return causal & (segment_ids[:, None] == segment_ids[None, :])

def attend(queries, keys_all, values_all, seg_mask):
    scores = jnp.einsum('ihd,jhd->hij', queries, keys_all, preferred_element_type=jnp.float32) / math.sqrt(queries.shape[-1])
    scores = jnp.where(seg_mask[None], scores, -1e+30)
    highest = lax.stop_gradient(lax.optimization_barrier(jnp.max(scores, axis=-1, keepdims=True)))
    expo = jnp.exp(scores - highest)
    probs = (expo / lax.optimization_barrier(jnp.sum(expo, axis=-1, keepdims=True))).astype(values_all.dtype)
    return jnp.einsum('hij,jhd->ihd', probs, values_all, preferred_element_type=jnp.float32)

def embedding(feat_rows, type_rows, type_table):
    onehot = (type_rows[:, None] == jnp.arange(type_table.shape[0], dtype=jnp.int32)[None, :]).astype(jnp.bfloat16)
    looked = jnp.dot(onehot, type_table, preferred_element_type=jnp.float32)
    return (feat_rows.astype(jnp.float32) + looked).astype(jnp.bfloat16)

def section_of(pipe_number, position):
    if pipe_number == 0:
        return position
    return LAYERS - 1 - position

def front(current, gain_row, qkv_weight, seg_mask):
    normed = normalize(current.astype(jnp.float32), gain_row).astype(jnp.bfloat16)
    projected = jnp.einsum('sd,cdn->csn', normed.astype(jnp.float32), qkv_weight.astype(jnp.float32)).astype(jnp.bfloat16)
    heads_view = projected.reshape(3, SEQ, HEADS, HD)
    mixed = attend(heads_view[0], heads_view[1], heads_view[2], seg_mask).reshape(SEQ, INNER).astype(jnp.bfloat16)
    return (normed, projected, mixed)

def layer_forward(current, gain_row, qkv_weight, out_weight, seg_mask):
    group_width = INNER // N_TP
    normed, projected, mixed = front(current, gain_row, qkv_weight, seg_mask)
    group_terms = jnp.einsum('sgn,gnd->gsd', mixed.reshape(SEQ, N_TP, group_width).astype(jnp.float32), out_weight.reshape(N_TP, group_width, D).astype(jnp.float32)).astype(jnp.bfloat16)
    group_terms = lax.optimization_barrier(group_terms).astype(jnp.float32)
    attn = lax.optimization_barrier(jnp.sum(group_terms, axis=0))
    return (current.astype(jnp.float32) + attn).astype(jnp.bfloat16)

def layer_backward(layer_in, upstream, gain_row, qkv_weight, out_weight, seg_mask):
    group_width = INNER // N_TP
    normed, projected, mixed = front(layer_in, gain_row, qkv_weight, seg_mask)
    d_mixed = jnp.dot(upstream, out_weight.T, preferred_element_type=jnp.float32).astype(jnp.bfloat16)
    heads_view = projected.reshape(3, SEQ, HEADS, HD)
    unused, pull_attend = jax.vjp(lambda query_part, key_part, value_part: attend(query_part, key_part, value_part, seg_mask), heads_view[0], heads_view[1], heads_view[2])
    pulled = pull_attend(d_mixed.astype(jnp.float32).reshape(SEQ, HEADS, HD))
    d_projected = jnp.stack(pulled).reshape(3, SEQ, INNER).astype(jnp.bfloat16)
    input_terms = jnp.einsum('csgn,cdgn->gsd', d_projected.reshape(3, SEQ, N_TP, group_width).astype(jnp.float32), qkv_weight.reshape(3, D, N_TP, group_width).astype(jnp.float32)).astype(jnp.bfloat16)
    input_terms = lax.optimization_barrier(input_terms).astype(jnp.float32)
    d_normed = lax.optimization_barrier(jnp.sum(input_terms, axis=0)).astype(jnp.bfloat16)
    unused_norm, pull_norm = jax.vjp(lambda inputs: normalize(inputs, gain_row), layer_in.astype(jnp.float32))
    d_input = pull_norm(d_normed.astype(jnp.float32))[0]
    fresh_grad = (upstream.astype(jnp.float32) + d_input).astype(jnp.bfloat16)
    qkv_term = jnp.einsum('sd,csn->cdn', normed.astype(jnp.float32), d_projected.astype(jnp.float32))
    out_term = jnp.dot(mixed.T, upstream, preferred_element_type=jnp.float32)
    return (fresh_grad, qkv_term, out_term)

def reference(feats, types, segs, type_table, gains, w_qkv, w_out, carry_acts, grad_in, saved, cotangent):
    acts_list = [[[None] * STEPS for section in range(LAYERS)] for pipe_number in range(PIPES)]
    grads_list = [[[None] * STEPS for section in range(LAYERS)] for pipe_number in range(PIPES)]
    qkv_sums = [[jnp.zeros((3, D, INNER), jnp.float32) for layer in range(LAYERS)] for pipe_number in range(PIPES)]
    out_sums = [[jnp.zeros((INNER, D), jnp.float32) for layer in range(LAYERS)] for pipe_number in range(PIPES)]
    for pipe_number in range(PIPES):
        for step_index in range(STEPS):
            for position in range(LAYERS):
                section = section_of(pipe_number, position)
                if position == 0:
                    current = embedding(feats[pipe_number, step_index], types[pipe_number, step_index], type_table)
                elif step_index == 0:
                    current = carry_acts[pipe_number, section]
                else:
                    current = acts_list[pipe_number][section_of(pipe_number, position - 1)][step_index - 1]
                seg_mask = segment_mask(segs[pipe_number, 0, step_index - position + LAYERS - 1])
                acts_list[pipe_number][section][step_index] = layer_forward(current, gains[pipe_number, section], w_qkv[pipe_number, section], w_out[pipe_number, section], seg_mask)
            for position in reversed(range(LAYERS)):
                section = section_of(pipe_number, position)
                if position == LAYERS - 1:
                    upstream = cotangent[pipe_number, step_index]
                elif step_index == 0:
                    upstream = grad_in[pipe_number, section]
                else:
                    upstream = grads_list[pipe_number][section_of(pipe_number, position + 1)][step_index - 1]
                seg_mask = segment_mask(segs[pipe_number, 1, step_index + position])
                fresh_grad, qkv_term, out_term = layer_backward(saved[pipe_number, section, step_index], upstream, gains[pipe_number, section], w_qkv[pipe_number, section], w_out[pipe_number, section], seg_mask)
                grads_list[pipe_number][section][step_index] = fresh_grad
                qkv_sums[pipe_number][position] = qkv_sums[pipe_number][position] + qkv_term
                out_sums[pipe_number][position] = out_sums[pipe_number][position] + out_term
    acts = jnp.stack([jnp.stack([jnp.stack(acts_list[p][k]) for k in range(LAYERS)]) for p in range(PIPES)])
    grad_acts = jnp.stack([jnp.stack([jnp.stack(grads_list[p][k]) for k in range(LAYERS)]) for p in range(PIPES)])
    qkv_rows = []
    out_rows = []
    for replica in range(PIPES):
        qkv_sections = []
        out_sections = []
        for section in range(LAYERS):
            layer = section_of(replica, section)
            qkv_parts = [lax.optimization_barrier(qkv_sums[p][layer].astype(jnp.bfloat16)).astype(jnp.float32) for p in range(PIPES)]
            out_parts = [lax.optimization_barrier(out_sums[p][layer].astype(jnp.bfloat16)).astype(jnp.float32) for p in range(PIPES)]
            qkv_sections.append((qkv_parts[0] + qkv_parts[1]).astype(jnp.bfloat16))
            out_sections.append((out_parts[0] + out_parts[1]).astype(jnp.bfloat16))
        qkv_rows.append(jnp.stack(qkv_sections))
        out_rows.append(jnp.stack(out_sections))
    grad_qkv = jnp.stack(qkv_rows)
    grad_out = jnp.stack(out_rows)
    return (acts, grad_acts, grad_qkv, grad_out)
```

```python
import math

import numpy as np

import jax
import jax.numpy as jnp
from jax import lax
from jax.sharding import PartitionSpec as P

HD = 128


def passed_along(block, axis, distance):
    devices = range(lax.axis_size(axis))
    route = [(i - distance, i) for i in devices if i - distance in devices]
    return lax.ppermute(block, axis, route)


def flipped(value, axis, mask):
    return lax.ppermute(value, axis, [(i, i ^ mask) for i in range(lax.axis_size(axis))])


def normalize(values, gain_row):
    mean_square = jnp.mean(values * values, axis=-1, keepdims=True)
    return values * lax.rsqrt(mean_square + 1e-05) * gain_row


def segment_mask(segment_ids):
    position = jnp.arange(segment_ids.shape[0], dtype=jnp.int32)
    causal = position[None, :] <= position[:, None]
    return causal & (segment_ids[:, None] == segment_ids[None, :])


def attend(queries, keys_all, values_all, seg_mask):
    scores = jnp.einsum(
        "ihd,jhd->hij", queries, keys_all, preferred_element_type=jnp.float32
    ) / math.sqrt(queries.shape[-1])
    scores = jnp.where(seg_mask[None], scores, -1e30)
    highest = lax.stop_gradient(jnp.max(scores, axis=-1, keepdims=True))
    expo = jnp.exp(scores - highest)
    probs = (expo / jnp.sum(expo, axis=-1, keepdims=True)).astype(values_all.dtype)
    return jnp.einsum("hij,jhd->ihd", probs, values_all, preferred_element_type=jnp.float32)


def embedding(feat_rows, type_rows, type_table):
    onehot = (
        type_rows[:, None] == jnp.arange(type_table.shape[0], dtype=jnp.int32)[None, :]
    ).astype(jnp.bfloat16)
    looked = jnp.dot(onehot, type_table, preferred_element_type=jnp.float32)
    return (feat_rows.astype(jnp.float32) + looked).astype(jnp.bfloat16)


def gathered(blocks):
    full = lax.all_gather(jnp.stack(blocks), "tp", axis=1, tiled=True)
    return [full[i] for i in range(len(blocks))]


def scattered(blocks):
    part = lax.psum_scatter(jnp.stack(blocks), "tp", scatter_dimension=1, tiled=True)
    return [part[i] for i in range(len(blocks))]


def shards(
    feats, types, segs, type_table, gains, w_qkv, w_out, carry_acts, grad_in, saved, cotangent
):
    sections = lax.axis_size("section")
    section_index = lax.axis_index("section")
    on_first_pipe = lax.axis_index("mirror") == 0
    position = jnp.where(on_first_pipe, section_index, sections - 1 - section_index)
    gain_row = gains[0, 0]
    qkv_weight = w_qkv[0, 0]
    out_weight = w_out[0, 0]
    window_steps = feats.shape[1]
    seq_len = segs.shape[3]
    model_width = qkv_weight.shape[1]
    inner_here = qkv_weight.shape[-1]
    heads_here = inner_here // HD

    def mask_for(which, index):
        return segment_mask(lax.dynamic_index_in_dim(segs[0, which], index, 0, keepdims=False))

    def normed_rows(rows):
        return normalize(rows.astype(jnp.float32), gain_row).astype(jnp.bfloat16)

    def heads_of(normed_full):
        projected = jnp.einsum(
            "sd,cdn->csn", normed_full, qkv_weight, preferred_element_type=jnp.float32
        ).astype(jnp.bfloat16)
        return projected.reshape(3, seq_len, heads_here, HD)

    def forward_part(normed_full, seg_mask):
        heads_view = heads_of(normed_full)
        mixed = (
            attend(heads_view[0], heads_view[1], heads_view[2], seg_mask)
            .reshape(seq_len, inner_here)
            .astype(jnp.bfloat16)
        )
        return jnp.dot(mixed, out_weight, preferred_element_type=jnp.float32).astype(jnp.bfloat16)

    def backward_part(normed_full, upstream_full, seg_mask):
        heads_view = heads_of(normed_full)
        primal, pull_attend = jax.vjp(
            lambda query_part, key_part, value_part: attend(
                query_part, key_part, value_part, seg_mask
            ),
            heads_view[0],
            heads_view[1],
            heads_view[2],
        )
        mixed = primal.reshape(seq_len, inner_here).astype(jnp.bfloat16)
        d_mixed = jnp.einsum(
            "sd,nd->sn", upstream_full, out_weight, preferred_element_type=jnp.float32
        ).astype(jnp.bfloat16)
        pulled = pull_attend(d_mixed.astype(jnp.float32).reshape(seq_len, heads_here, HD))
        d_projected = jnp.stack(pulled).reshape(3, seq_len, inner_here)
        d_normed_part = jnp.einsum(
            "csn,cdn->sd", d_projected, qkv_weight, preferred_element_type=jnp.float32
        ).astype(jnp.bfloat16)
        qkv_term = jnp.einsum(
            "sd,csn->cdn", normed_full, d_projected, preferred_element_type=jnp.float32
        )
        out_term = jnp.einsum("sn,sd->nd", mixed, upstream_full, preferred_element_type=jnp.float32)
        return d_normed_part, qkv_term, out_term

    def input_grad(layer_in, upstream, d_normed):
        unused_norm, pull_norm = jax.vjp(
            lambda inputs: normalize(inputs, gain_row), layer_in.astype(jnp.float32)
        )
        d_input = pull_norm(d_normed.astype(jnp.float32))[0]
        return (upstream.astype(jnp.float32) + d_input).astype(jnp.bfloat16)

    saved_normed = [normed_rows(saved[0, 0, t]) for t in range(window_steps)]
    saved_full = [None] + [gathered([saved_normed[t]])[0] for t in range(1, window_steps)]

    forward_in = carry_acts[0, 0]
    backward_in = grad_in[0, 0]
    forward_outs = []
    backward_outs = []
    qkv_total = jnp.zeros(qkv_weight.shape, jnp.float32)
    out_total = jnp.zeros(out_weight.shape, jnp.float32)
    for step_index in range(window_steps):
        embedded = embedding(feats[0, step_index], types[0, step_index], type_table)
        current = jnp.where(position == 0, embedded, forward_in)
        upstream = jnp.where(position == sections - 1, cotangent[0, step_index], backward_in)
        to_gather = [normed_rows(current), upstream]
        if step_index == 0:
            to_gather.append(saved_normed[0])
        gathered_rows = gathered(to_gather)
        forward_normed_full, upstream_full = gathered_rows[0], gathered_rows[1]
        backward_normed_full = gathered_rows[2] if step_index == 0 else saved_full[step_index]
        attn_part = forward_part(
            forward_normed_full, mask_for(0, step_index - position + sections - 1)
        )
        d_normed_part, qkv_term, out_term = backward_part(
            backward_normed_full, upstream_full, mask_for(1, step_index + position)
        )
        attn_rows, d_normed = scattered([attn_part, d_normed_part])
        forward_out = (current.astype(jnp.float32) + attn_rows.astype(jnp.float32)).astype(
            jnp.bfloat16
        )
        backward_out = input_grad(saved[0, 0, step_index], upstream, d_normed)
        qkv_total = qkv_total + qkv_term
        out_total = out_total + out_term
        forward_outs.append(forward_out)
        backward_outs.append(backward_out)
        if step_index + 1 < window_steps:
            toward_higher = jnp.where(on_first_pipe, forward_out, backward_out)
            toward_lower = jnp.where(on_first_pipe, backward_out, forward_out)
            from_lower = passed_along(toward_higher, "section", 1)
            from_upper = passed_along(toward_lower, "section", -1)
            forward_in = jnp.where(on_first_pipe, from_lower, from_upper)
            backward_in = jnp.where(on_first_pipe, from_upper, from_lower)

    own_qkv = qkv_total.astype(jnp.bfloat16)
    own_out = out_total.astype(jnp.bfloat16)
    pair_axes = ("section", "mirror")
    bit_count = lax.axis_size(pair_axes).bit_length() - 1
    section_bits = list(range(1, bit_count))
    if section_bits:
        routes = []
        for start in range(len(section_bits)):
            order = section_bits[start:] + section_bits[:start]
            routes.append([1 | (1 << order[0])] + [1 << bit for bit in order[1:]])
    else:
        routes = [[1]]
    cuts = np.linspace(0, model_width, len(routes) + 1).astype(int)
    qkv_sums = []
    out_sums = []
    for route_index, hops in enumerate(routes):
        low, high = int(cuts[route_index]), int(cuts[route_index + 1])
        piece = (own_qkv[:, low:high, :], own_out[:, low:high])
        for mask in hops:
            piece = flipped(piece, pair_axes, mask)
        qkv_sums.append(
            (own_qkv[:, low:high, :].astype(jnp.float32) + piece[0].astype(jnp.float32)).astype(
                jnp.bfloat16
            )
        )
        out_sums.append(
            (own_out[:, low:high].astype(jnp.float32) + piece[1].astype(jnp.float32)).astype(
                jnp.bfloat16
            )
        )
    grad_qkv = jnp.concatenate(qkv_sums, axis=1)
    grad_out = jnp.concatenate(out_sums, axis=1)
    acts_block = jnp.stack(forward_outs)[None, None]
    grads_block = jnp.stack(backward_outs)[None, None]
    return (acts_block, grads_block, grad_qkv[None, None], grad_out[None, None])


def solution(mesh):
    in_specs = (
        P("mirror", None, "tp", None),
        P("mirror", None, "tp"),
        P("mirror", None, None, None),
        P(),
        P("mirror", "section", None),
        P("mirror", "section", None, None, "tp"),
        P("mirror", "section", "tp", None),
        P("mirror", "section", "tp", None),
        P("mirror", "section", "tp", None),
        P("mirror", "section", None, "tp", None),
        P("mirror", None, "tp", None),
    )
    out_specs = (
        P("mirror", "section", None, "tp", None),
        P("mirror", "section", None, "tp", None),
        P("mirror", "section", None, None, "tp"),
        P("mirror", "section", "tp", None),
    )
    return jax.shard_map(shards, mesh=mesh, in_specs=in_specs, out_specs=out_specs, check_vma=False)
```

```python
import math

import numpy as np

import jax
import jax.numpy as jnp
from jax import lax
from jax.sharding import PartitionSpec as P

HD = 128


def passed_along(block, axis, distance):
    devices = range(lax.axis_size(axis))
    route = [(i - distance, i) for i in devices if i - distance in devices]
    return lax.ppermute(block, axis, route)


def flipped(value, axis, mask):
    return lax.ppermute(value, axis, [(i, i ^ mask) for i in range(lax.axis_size(axis))])


def normalize(values, gain_row):
    mean_square = jnp.mean(values * values, axis=-1, keepdims=True)
    return values * lax.rsqrt(mean_square + 1e-05) * gain_row


def segment_mask(segment_ids):
    position = jnp.arange(segment_ids.shape[0], dtype=jnp.int32)
    causal = position[None, :] <= position[:, None]
    return causal & (segment_ids[:, None] == segment_ids[None, :])


def attend(queries, keys_all, values_all, seg_mask):
    scores = jnp.einsum(
        "ihd,jhd->hij", queries, keys_all, preferred_element_type=jnp.float32
    ) / math.sqrt(queries.shape[-1])
    scores = jnp.where(seg_mask[None], scores, -1e30)
    highest = lax.stop_gradient(jnp.max(scores, axis=-1, keepdims=True))
    expo = jnp.exp(scores - highest)
    probs = (expo / jnp.sum(expo, axis=-1, keepdims=True)).astype(values_all.dtype)
    return jnp.einsum("hij,jhd->ihd", probs, values_all, preferred_element_type=jnp.float32)


def embedding(feat_rows, type_rows, type_table):
    onehot = (
        type_rows[:, None] == jnp.arange(type_table.shape[0], dtype=jnp.int32)[None, :]
    ).astype(jnp.bfloat16)
    looked = jnp.dot(onehot, type_table, preferred_element_type=jnp.float32)
    return (feat_rows.astype(jnp.float32) + looked).astype(jnp.bfloat16)


def gathered(blocks):
    full = lax.all_gather(jnp.stack(blocks), "tp", axis=1, tiled=True)
    return [full[i] for i in range(len(blocks))]


def scattered(blocks):
    part = lax.psum_scatter(jnp.stack(blocks), "tp", scatter_dimension=1, tiled=True)
    return [part[i] for i in range(len(blocks))]


def shards(
    feats, types, segs, type_table, gains, w_qkv, w_out, carry_acts, grad_in, saved, cotangent
):
    sections = lax.axis_size("section")
    section_index = lax.axis_index("section")
    on_first_pipe = lax.axis_index("mirror") == 0
    position = jnp.where(on_first_pipe, section_index, sections - 1 - section_index)
    gain_row = gains[0, 0]
    qkv_weight = w_qkv[0, 0]
    out_weight = w_out[0, 0]
    window_steps = feats.shape[1]
    seq_len = segs.shape[3]
    model_width = qkv_weight.shape[1]
    inner_here = qkv_weight.shape[-1]
    heads_here = inner_here // HD

    def mask_for(which, index):
        return segment_mask(lax.dynamic_index_in_dim(segs[0, which], index, 0, keepdims=False))

    def normed_rows(rows):
        return normalize(rows.astype(jnp.float32), gain_row).astype(jnp.bfloat16)

    def heads_of(normed_full):
        projected = jnp.einsum(
            "sd,cdn->csn", normed_full, qkv_weight, preferred_element_type=jnp.float32
        ).astype(jnp.bfloat16)
        return projected.reshape(3, seq_len, heads_here, HD)

    def forward_part(normed_full, seg_mask):
        heads_view = heads_of(normed_full)
        mixed = (
            attend(heads_view[0], heads_view[1], heads_view[2], seg_mask)
            .reshape(seq_len, inner_here)
            .astype(jnp.bfloat16)
        )
        return jnp.dot(mixed, out_weight, preferred_element_type=jnp.float32).astype(jnp.bfloat16)

    def backward_part(normed_full, upstream_full, seg_mask):
        heads_view = heads_of(normed_full)
        primal, pull_attend = jax.vjp(
            lambda query_part, key_part, value_part: attend(
                query_part, key_part, value_part, seg_mask
            ),
            heads_view[0],
            heads_view[1],
            heads_view[2],
        )
        mixed = primal.reshape(seq_len, inner_here).astype(jnp.bfloat16)
        d_mixed = jnp.einsum(
            "sd,nd->sn", upstream_full, out_weight, preferred_element_type=jnp.float32
        ).astype(jnp.bfloat16)
        pulled = pull_attend(d_mixed.astype(jnp.float32).reshape(seq_len, heads_here, HD))
        d_projected = jnp.stack(pulled).reshape(3, seq_len, inner_here)
        d_normed_part = jnp.einsum(
            "csn,cdn->sd", d_projected, qkv_weight, preferred_element_type=jnp.float32
        ).astype(jnp.bfloat16)
        qkv_term = jnp.einsum(
            "sd,csn->cdn", normed_full, d_projected, preferred_element_type=jnp.float32
        )
        out_term = jnp.einsum("sn,sd->nd", mixed, upstream_full, preferred_element_type=jnp.float32)
        return d_normed_part, qkv_term, out_term

    def input_grad(layer_in, upstream, d_normed):
        unused_norm, pull_norm = jax.vjp(
            lambda inputs: normalize(inputs, gain_row), layer_in.astype(jnp.float32)
        )
        d_input = pull_norm(d_normed.astype(jnp.float32))[0]
        return (upstream.astype(jnp.float32) + d_input).astype(jnp.bfloat16)

    pair_axes = ("section", "mirror")
    mirror_size = lax.axis_size("mirror")
    up_pairs = []
    down_pairs = []
    for section in range(sections):
        for mirror in range(mirror_size):
            ahead = 1 if mirror == 0 else -1
            if 0 <= section + ahead < sections:
                up_pairs.append((section * mirror_size + mirror, (section + ahead) * mirror_size + mirror))
            if 0 <= section - ahead < sections:
                down_pairs.append((section * mirror_size + mirror, (section - ahead) * mirror_size + mirror))

    saved_normed = [normed_rows(saved[0, 0, t]) for t in range(window_steps)]
    forward_in = carry_acts[0, 0]
    backward_in = grad_in[0, 0]
    forward_outs = []
    backward_outs = []
    qkv_total = jnp.zeros(qkv_weight.shape, jnp.float32)
    out_total = jnp.zeros(out_weight.shape, jnp.float32)
    for step_index in range(window_steps):
        embedded = embedding(feats[0, step_index], types[0, step_index], type_table)
        current = jnp.where(position == 0, embedded, forward_in)
        upstream = jnp.where(position == sections - 1, cotangent[0, step_index], backward_in)
        if step_index == 0:
            upstream_full, backward_normed_full, forward_normed_full = gathered(
                [upstream, saved_normed[0], normed_rows(current)]
            )
        else:
            upstream_full, backward_normed_full = gathered([upstream, saved_normed[step_index]])
        if step_index > 0:
            forward_normed, backward_normed_full = lax.optimization_barrier(
                (normed_rows(current), backward_normed_full)
            )
            forward_normed_full = gathered([forward_normed])[0]
        d_normed_part, qkv_term, out_term = backward_part(
            backward_normed_full, upstream_full, mask_for(1, step_index + position)
        )
        qkv_total = qkv_total + qkv_term
        out_total = out_total + out_term
        attn_part = forward_part(
            forward_normed_full, mask_for(0, step_index - position + sections - 1)
        )
        d_normed, attn_rows = scattered([d_normed_part, attn_part])
        forward_out = (current.astype(jnp.float32) + attn_rows.astype(jnp.float32)).astype(
            jnp.bfloat16
        )
        backward_out = input_grad(saved[0, 0, step_index], upstream, d_normed)
        forward_outs.append(forward_out)
        backward_outs.append(backward_out)
        if step_index + 1 < window_steps:
            forward_in = lax.ppermute(forward_out, pair_axes, up_pairs)
            backward_in = lax.ppermute(backward_out, pair_axes, down_pairs)

    own_qkv = qkv_total.astype(jnp.bfloat16)
    own_out = out_total.astype(jnp.bfloat16)
    bit_count = lax.axis_size(pair_axes).bit_length() - 1
    section_bits = list(range(1, bit_count))
    if section_bits:
        routes = []
        for start in range(len(section_bits)):
            order = section_bits[start:] + section_bits[:start]
            routes.append([1 | (1 << order[0])] + [1 << bit for bit in order[1:]])
    else:
        routes = [[1]]
    cuts = np.linspace(0, model_width, len(routes) + 1).astype(int)
    qkv_sums = []
    out_sums = []
    for route_index, hops in enumerate(routes):
        low, high = int(cuts[route_index]), int(cuts[route_index + 1])
        piece = (own_qkv[:, low:high, :], own_out[:, low:high])
        for mask in hops:
            piece = flipped(piece, pair_axes, mask)
        qkv_sums.append(
            (own_qkv[:, low:high, :].astype(jnp.float32) + piece[0].astype(jnp.float32)).astype(
                jnp.bfloat16
            )
        )
        out_sums.append(
            (own_out[:, low:high].astype(jnp.float32) + piece[1].astype(jnp.float32)).astype(
                jnp.bfloat16
            )
        )
    grad_qkv = jnp.concatenate(qkv_sums, axis=1)
    grad_out = jnp.concatenate(out_sums, axis=1)
    acts_block = jnp.stack(forward_outs)[None, None]
    grads_block = jnp.stack(backward_outs)[None, None]
    return (acts_block, grads_block, grad_qkv[None, None], grad_out[None, None])


def solution(mesh):
    in_specs = (
        P("mirror", None, "tp", None),
        P("mirror", None, "tp"),
        P("mirror", None, None, None),
        P(),
        P("mirror", "section", None),
        P("mirror", "section", None, None, "tp"),
        P("mirror", "section", "tp", None),
        P("mirror", "section", "tp", None),
        P("mirror", "section", "tp", None),
        P("mirror", "section", None, "tp", None),
        P("mirror", None, "tp", None),
    )
    out_specs = (
        P("mirror", "section", None, "tp", None),
        P("mirror", "section", None, "tp", None),
        P("mirror", "section", None, None, "tp"),
        P("mirror", "section", "tp", None),
    )
    return jax.shard_map(shards, mesh=mesh, in_specs=in_specs, out_specs=out_specs, check_vma=False)
```

```python
import math

import numpy as np

import jax
import jax.numpy as jnp
from jax import lax
from jax.sharding import PartitionSpec as P

HD = 128


def passed_along(block, axis, distance):
    devices = range(lax.axis_size(axis))
    route = [(i - distance, i) for i in devices if i - distance in devices]
    return lax.ppermute(block, axis, route)


def flipped(value, axis, mask):
    return lax.ppermute(value, axis, [(i, i ^ mask) for i in range(lax.axis_size(axis))])


def normalize(values, gain_row):
    mean_square = jnp.mean(values * values, axis=-1, keepdims=True)
    return values * lax.rsqrt(mean_square + 1e-05) * gain_row


def segment_mask(segment_ids):
    position = jnp.arange(segment_ids.shape[0], dtype=jnp.int32)
    causal = position[None, :] <= position[:, None]
    return causal & (segment_ids[:, None] == segment_ids[None, :])


def attend(queries, keys_all, values_all, seg_mask):
    scores = jnp.einsum(
        "ihd,jhd->hij", queries, keys_all, preferred_element_type=jnp.float32
    ) / math.sqrt(queries.shape[-1])
    scores = jnp.where(seg_mask[None], scores, -1e30)
    highest = lax.stop_gradient(jnp.max(scores, axis=-1, keepdims=True))
    expo = jnp.exp(scores - highest)
    probs = (expo / jnp.sum(expo, axis=-1, keepdims=True)).astype(values_all.dtype)
    return jnp.einsum("hij,jhd->ihd", probs, values_all, preferred_element_type=jnp.float32)


def embedding(feat_rows, type_rows, type_table):
    onehot = (
        type_rows[:, None] == jnp.arange(type_table.shape[0], dtype=jnp.int32)[None, :]
    ).astype(jnp.bfloat16)
    looked = jnp.dot(onehot, type_table, preferred_element_type=jnp.float32)
    return (feat_rows.astype(jnp.float32) + looked).astype(jnp.bfloat16)


def gathered(blocks):
    full = lax.all_gather(jnp.stack(blocks), "tp", axis=1, tiled=True)
    return [full[i] for i in range(len(blocks))]


def scattered(blocks):
    part = lax.psum_scatter(jnp.stack(blocks), "tp", scatter_dimension=1, tiled=True)
    return [part[i] for i in range(len(blocks))]


def shards(
    feats, types, segs, type_table, gains, w_qkv, w_out, carry_acts, grad_in, saved, cotangent
):
    sections = lax.axis_size("section")
    section_index = lax.axis_index("section")
    on_first_pipe = lax.axis_index("mirror") == 0
    position = jnp.where(on_first_pipe, section_index, sections - 1 - section_index)
    gain_row = gains[0, 0]
    qkv_weight = w_qkv[0, 0]
    out_weight = w_out[0, 0]
    window_steps = feats.shape[1]
    seq_len = segs.shape[3]
    model_width = qkv_weight.shape[1]
    inner_here = qkv_weight.shape[-1]
    heads_here = inner_here // HD

    def mask_for(which, index):
        return segment_mask(lax.dynamic_index_in_dim(segs[0, which], index, 0, keepdims=False))

    def normed_rows(rows):
        return normalize(rows.astype(jnp.float32), gain_row).astype(jnp.bfloat16)

    def heads_of(normed_full):
        projected = jnp.einsum(
            "sd,cdn->csn", normed_full, qkv_weight, preferred_element_type=jnp.float32
        ).astype(jnp.bfloat16)
        return projected.reshape(3, seq_len, heads_here, HD)

    def forward_part(normed_full, seg_mask):
        heads_view = heads_of(normed_full)
        mixed = (
            attend(heads_view[0], heads_view[1], heads_view[2], seg_mask)
            .reshape(seq_len, inner_here)
            .astype(jnp.bfloat16)
        )
        return jnp.dot(mixed, out_weight, preferred_element_type=jnp.float32).astype(jnp.bfloat16)

    def backward_part(normed_full, upstream_full, seg_mask):
        heads_view = heads_of(normed_full)
        primal, pull_attend = jax.vjp(
            lambda query_part, key_part, value_part: attend(
                query_part, key_part, value_part, seg_mask
            ),
            heads_view[0],
            heads_view[1],
            heads_view[2],
        )
        mixed = primal.reshape(seq_len, inner_here).astype(jnp.bfloat16)
        d_mixed = jnp.einsum(
            "sd,nd->sn", upstream_full, out_weight, preferred_element_type=jnp.float32
        ).astype(jnp.bfloat16)
        pulled = pull_attend(d_mixed.astype(jnp.float32).reshape(seq_len, heads_here, HD))
        d_projected = jnp.stack(pulled).reshape(3, seq_len, inner_here)
        d_normed_part = jnp.einsum(
            "csn,cdn->sd", d_projected, qkv_weight, preferred_element_type=jnp.float32
        ).astype(jnp.bfloat16)
        qkv_term = jnp.einsum(
            "sd,csn->cdn", normed_full, d_projected, preferred_element_type=jnp.float32
        )
        out_term = jnp.einsum("sn,sd->nd", mixed, upstream_full, preferred_element_type=jnp.float32)
        return d_normed_part, qkv_term, out_term

    def input_grad(layer_in, upstream, d_normed):
        unused_norm, pull_norm = jax.vjp(
            lambda inputs: normalize(inputs, gain_row), layer_in.astype(jnp.float32)
        )
        d_input = pull_norm(d_normed.astype(jnp.float32))[0]
        return (upstream.astype(jnp.float32) + d_input).astype(jnp.bfloat16)

    pair_axes = ("section", "mirror")
    mirror_size = lax.axis_size("mirror")
    up_pairs = []
    down_pairs = []
    for section in range(sections):
        for mirror in range(mirror_size):
            ahead = 1 if mirror == 0 else -1
            if 0 <= section + ahead < sections:
                up_pairs.append((section * mirror_size + mirror, (section + ahead) * mirror_size + mirror))
            if 0 <= section - ahead < sections:
                down_pairs.append((section * mirror_size + mirror, (section - ahead) * mirror_size + mirror))

    last_step = window_steps - 1
    saved_normed = [normed_rows(saved[0, 0, t]) for t in range(window_steps)]
    qkv_total = jnp.zeros(qkv_weight.shape, jnp.float32)
    out_total = jnp.zeros(out_weight.shape, jnp.float32)

    backward_outs = []
    backward_in = grad_in[0, 0]
    backward_normed_full = [None] * window_steps
    forward_normed_first = None
    for step_index in range(window_steps):
        upstream = jnp.where(position == sections - 1, cotangent[0, step_index], backward_in)
        if step_index == 0:
            upstream_full, backward_normed_full[0] = gathered([upstream, saved_normed[0]])
        else:
            upstream, ready = lax.optimization_barrier((upstream, ready))
            upstream_full = gathered([upstream])[0]
        d_normed_part, qkv_term, out_term = backward_part(
            backward_normed_full[step_index], upstream_full, mask_for(1, step_index + position)
        )
        qkv_total = qkv_total + qkv_term
        out_total = out_total + out_term
        if step_index == last_step:
            last_d_normed_part = d_normed_part
            last_upstream = upstream
            last_upstream_full = upstream_full
            break
        d_normed = scattered([d_normed_part])[0]
        if step_index == 0:
            first_forward_in = jnp.where(
                position == 0, embedding(feats[0, 0], types[0, 0], type_table), carry_acts[0, 0]
            )
            rest, d_normed = lax.optimization_barrier(
                (saved_normed[1:] + [normed_rows(first_forward_in)], d_normed)
            )
            ready = gathered(rest)
            backward_normed_full[1:] = ready[:-1]
            forward_normed_first = ready[-1]
        backward_out = input_grad(saved[0, 0, step_index], upstream, d_normed)
        backward_outs.append(backward_out)
        backward_in = lax.ppermute(backward_out, pair_axes, down_pairs)

    forward_outs = []
    forward_in = carry_acts[0, 0]
    for step_index in range(window_steps):
        embedded = embedding(feats[0, step_index], types[0, step_index], type_table)
        current = jnp.where(position == 0, embedded, forward_in)
        if step_index == 0:
            forward_normed_full, last_upstream_full = lax.optimization_barrier(
                (forward_normed_first, last_upstream_full)
            )
        else:
            forward_normed_full = gathered([normed_rows(current)])[0]
        attn_part = forward_part(
            forward_normed_full, mask_for(0, step_index - position + sections - 1)
        )
        if step_index == last_step:
            attn_rows, d_normed = scattered([attn_part, last_d_normed_part])
            backward_outs.append(input_grad(saved[0, 0, last_step], last_upstream, d_normed))
        else:
            attn_rows = scattered([attn_part])[0]
        forward_out = (current.astype(jnp.float32) + attn_rows.astype(jnp.float32)).astype(
            jnp.bfloat16
        )
        forward_outs.append(forward_out)
        if step_index < last_step:
            forward_in = lax.ppermute(forward_out, pair_axes, up_pairs)

    own_qkv = qkv_total.astype(jnp.bfloat16)
    own_out = out_total.astype(jnp.bfloat16)
    bit_count = lax.axis_size(pair_axes).bit_length() - 1
    section_bits = list(range(1, bit_count))
    if section_bits:
        routes = []
        for start in range(len(section_bits)):
            order = section_bits[start:] + section_bits[:start]
            routes.append([1 | (1 << order[0])] + [1 << bit for bit in order[1:]])
    else:
        routes = [[1]]
    cuts = np.linspace(0, model_width, len(routes) + 1).astype(int)
    qkv_sums = []
    out_sums = []
    for route_index, hops in enumerate(routes):
        low, high = int(cuts[route_index]), int(cuts[route_index + 1])
        piece = (own_qkv[:, low:high, :], own_out[:, low:high])
        for mask in hops:
            piece = flipped(piece, pair_axes, mask)
        qkv_sums.append(
            (own_qkv[:, low:high, :].astype(jnp.float32) + piece[0].astype(jnp.float32)).astype(
                jnp.bfloat16
            )
        )
        out_sums.append(
            (own_out[:, low:high].astype(jnp.float32) + piece[1].astype(jnp.float32)).astype(
                jnp.bfloat16
            )
        )
    grad_qkv = jnp.concatenate(qkv_sums, axis=1)
    grad_out = jnp.concatenate(out_sums, axis=1)
    acts_block = jnp.stack(forward_outs)[None, None]
    grads_block = jnp.stack(backward_outs)[None, None]
    return (acts_block, grads_block, grad_qkv[None, None], grad_out[None, None])


def solution(mesh):
    in_specs = (
        P("mirror", None, "tp", None),
        P("mirror", None, "tp"),
        P("mirror", None, None, None),
        P(),
        P("mirror", "section", None),
        P("mirror", "section", None, None, "tp"),
        P("mirror", "section", "tp", None),
        P("mirror", "section", "tp", None),
        P("mirror", "section", "tp", None),
        P("mirror", "section", None, "tp", None),
        P("mirror", None, "tp", None),
    )
    out_specs = (
        P("mirror", "section", None, "tp", None),
        P("mirror", "section", None, "tp", None),
        P("mirror", "section", None, None, "tp"),
        P("mirror", "section", "tp", None),
    )
    return jax.shard_map(shards, mesh=mesh, in_specs=in_specs, out_specs=out_specs, check_vma=False)
```

```python
import math

import numpy as np

import jax
import jax.numpy as jnp
from jax import lax
from jax.sharding import PartitionSpec as P

HD = 128


def passed_along(block, axis, distance):
    devices = range(lax.axis_size(axis))
    route = [(i - distance, i) for i in devices if i - distance in devices]
    return lax.ppermute(block, axis, route)


def flipped(value, axis, mask):
    return lax.ppermute(value, axis, [(i, i ^ mask) for i in range(lax.axis_size(axis))])


def normalize(values, gain_row):
    mean_square = jnp.mean(values * values, axis=-1, keepdims=True)
    return values * lax.rsqrt(mean_square + 1e-05) * gain_row


def segment_mask(segment_ids):
    position = jnp.arange(segment_ids.shape[0], dtype=jnp.int32)
    causal = position[None, :] <= position[:, None]
    return causal & (segment_ids[:, None] == segment_ids[None, :])


def attend(queries, keys_all, values_all, seg_mask):
    scores = jnp.einsum(
        "ihd,jhd->hij", queries, keys_all, preferred_element_type=jnp.float32
    ) / math.sqrt(queries.shape[-1])
    scores = jnp.where(seg_mask[None], scores, -1e30)
    highest = lax.stop_gradient(jnp.max(scores, axis=-1, keepdims=True))
    expo = jnp.exp(scores - highest)
    probs = (expo / jnp.sum(expo, axis=-1, keepdims=True)).astype(values_all.dtype)
    return jnp.einsum("hij,jhd->ihd", probs, values_all, preferred_element_type=jnp.float32)


def embedding(feat_rows, type_rows, type_table):
    onehot = (
        type_rows[:, None] == jnp.arange(type_table.shape[0], dtype=jnp.int32)[None, :]
    ).astype(jnp.bfloat16)
    looked = jnp.dot(onehot, type_table, preferred_element_type=jnp.float32)
    return (feat_rows.astype(jnp.float32) + looked).astype(jnp.bfloat16)


def gathered(blocks):
    full = lax.all_gather(jnp.stack(blocks), "tp", axis=1, tiled=True)
    return [full[i] for i in range(len(blocks))]


def scattered(blocks):
    part = lax.psum_scatter(jnp.stack(blocks), "tp", scatter_dimension=1, tiled=True)
    return [part[i] for i in range(len(blocks))]


def shards(
    feats, types, segs, type_table, gains, w_qkv, w_out, carry_acts, grad_in, saved, cotangent
):
    sections = lax.axis_size("section")
    section_index = lax.axis_index("section")
    on_first_pipe = lax.axis_index("mirror") == 0
    position = jnp.where(on_first_pipe, section_index, sections - 1 - section_index)
    gain_row = gains[0, 0]
    qkv_weight = w_qkv[0, 0]
    out_weight = w_out[0, 0]
    window_steps = feats.shape[1]
    seq_len = segs.shape[3]
    model_width = qkv_weight.shape[1]
    inner_here = qkv_weight.shape[-1]
    heads_here = inner_here // HD

    def mask_for(which, index):
        return segment_mask(lax.dynamic_index_in_dim(segs[0, which], index, 0, keepdims=False))

    def normed_rows(rows):
        return normalize(rows.astype(jnp.float32), gain_row).astype(jnp.bfloat16)

    def heads_of(normed_full):
        projected = jnp.einsum(
            "sd,cdn->csn", normed_full, qkv_weight, preferred_element_type=jnp.float32
        ).astype(jnp.bfloat16)
        return projected.reshape(3, seq_len, heads_here, HD)

    def forward_part(normed_full, seg_mask):
        heads_view = heads_of(normed_full)
        mixed = (
            attend(heads_view[0], heads_view[1], heads_view[2], seg_mask)
            .reshape(seq_len, inner_here)
            .astype(jnp.bfloat16)
        )
        return jnp.dot(mixed, out_weight, preferred_element_type=jnp.float32).astype(jnp.bfloat16)

    def backward_part(normed_full, upstream_full, seg_mask):
        heads_view = heads_of(normed_full)
        primal, pull_attend = jax.vjp(
            lambda query_part, key_part, value_part: attend(
                query_part, key_part, value_part, seg_mask
            ),
            heads_view[0],
            heads_view[1],
            heads_view[2],
        )
        mixed = primal.reshape(seq_len, inner_here).astype(jnp.bfloat16)
        d_mixed = jnp.einsum(
            "sd,nd->sn", upstream_full, out_weight, preferred_element_type=jnp.float32
        ).astype(jnp.bfloat16)
        pulled = pull_attend(d_mixed.astype(jnp.float32).reshape(seq_len, heads_here, HD))
        d_projected = jnp.stack(pulled).reshape(3, seq_len, inner_here)
        d_normed_part = jnp.einsum(
            "csn,cdn->sd", d_projected, qkv_weight, preferred_element_type=jnp.float32
        ).astype(jnp.bfloat16)
        qkv_term = jnp.einsum(
            "sd,csn->cdn", normed_full, d_projected, preferred_element_type=jnp.float32
        )
        out_term = jnp.einsum("sn,sd->nd", mixed, upstream_full, preferred_element_type=jnp.float32)
        return d_normed_part, qkv_term, out_term

    def input_grad(layer_in, upstream, d_normed):
        unused_norm, pull_norm = jax.vjp(
            lambda inputs: normalize(inputs, gain_row), layer_in.astype(jnp.float32)
        )
        d_input = pull_norm(d_normed.astype(jnp.float32))[0]
        return (upstream.astype(jnp.float32) + d_input).astype(jnp.bfloat16)

    pair_axes = ("section", "mirror")
    mirror_size = lax.axis_size("mirror")
    up_pairs = []
    down_pairs = []
    for section in range(sections):
        for mirror in range(mirror_size):
            ahead = 1 if mirror == 0 else -1
            if 0 <= section + ahead < sections:
                up_pairs.append((section * mirror_size + mirror, (section + ahead) * mirror_size + mirror))
            if 0 <= section - ahead < sections:
                down_pairs.append((section * mirror_size + mirror, (section - ahead) * mirror_size + mirror))

    bit_count = lax.axis_size(pair_axes).bit_length() - 1
    section_bits = list(range(1, bit_count))
    if section_bits:
        routes = []
        for start in range(len(section_bits)):
            order = section_bits[start:] + section_bits[:start]
            routes.append([1 | (1 << order[0])] + [1 << bit for bit in order[1:]])
    else:
        routes = [[1]]
    cuts = np.linspace(0, model_width, len(routes) + 1).astype(int)
    spans = [(int(cuts[i]), int(cuts[i + 1])) for i in range(len(routes))]

    last_step = window_steps - 1
    saved_normed = [normed_rows(saved[0, 0, t]) for t in range(window_steps)]
    qkv_total = jnp.zeros(qkv_weight.shape, jnp.float32)
    out_total = jnp.zeros(out_weight.shape, jnp.float32)

    backward_outs = []
    backward_in = grad_in[0, 0]
    for step_index in range(window_steps):
        upstream = jnp.where(position == sections - 1, cotangent[0, step_index], backward_in)
        if step_index == 0:
            upstream_full, *backward_normed_full = gathered([upstream] + saved_normed)
        else:
            upstream, forward_normed_full = lax.optimization_barrier(
                (upstream, forward_normed_full)
            )
            upstream_full = gathered([upstream])[0]
        d_normed_part, qkv_term, out_term = backward_part(
            backward_normed_full[step_index], upstream_full, mask_for(1, step_index + position)
        )
        qkv_total = qkv_total + qkv_term
        out_total = out_total + out_term
        if step_index == last_step:
            last_d_normed_part = d_normed_part
            last_upstream = upstream
            last_upstream_full = upstream_full
            break
        d_normed = scattered([d_normed_part])[0]
        if step_index == 0:
            first_forward_in = jnp.where(
                position == 0, embedding(feats[0, 0], types[0, 0], type_table), carry_acts[0, 0]
            )
            first_normed, d_normed = lax.optimization_barrier(
                (normed_rows(first_forward_in), d_normed)
            )
            forward_normed_full = gathered([first_normed])[0]
        backward_out = input_grad(saved[0, 0, step_index], upstream, d_normed)
        backward_outs.append(backward_out)
        backward_in = lax.ppermute(backward_out, pair_axes, down_pairs)

    own_qkv = qkv_total.astype(jnp.bfloat16)
    own_out = out_total.astype(jnp.bfloat16)
    in_flight = []
    for (low, high), hops in zip(spans, routes):
        in_flight.append(
            flipped((own_qkv[:, low:high, :], own_out[:, low:high]), pair_axes, hops[0])
        )

    forward_outs = []
    forward_in = carry_acts[0, 0]
    for step_index in range(window_steps):
        embedded = embedding(feats[0, step_index], types[0, step_index], type_table)
        current = jnp.where(position == 0, embedded, forward_in)
        if step_index == 0:
            forward_normed_full, last_upstream_full = lax.optimization_barrier(
                (forward_normed_full, last_upstream_full)
            )
        else:
            forward_normed, in_flight = lax.optimization_barrier((normed_rows(current), in_flight))
            forward_normed_full = gathered([forward_normed])[0]
        attn_part = forward_part(
            forward_normed_full, mask_for(0, step_index - position + sections - 1)
        )
        if step_index == last_step:
            attn_rows, d_normed = scattered([attn_part, last_d_normed_part])
            backward_outs.append(input_grad(saved[0, 0, last_step], last_upstream, d_normed))
        else:
            attn_rows = scattered([attn_part])[0]
        forward_out = (current.astype(jnp.float32) + attn_rows.astype(jnp.float32)).astype(
            jnp.bfloat16
        )
        forward_outs.append(forward_out)
        if step_index < last_step:
            forward_in = lax.ppermute(forward_out, pair_axes, up_pairs)

    qkv_sums = []
    out_sums = []
    for (low, high), hops, piece in zip(spans, routes, in_flight):
        for mask in hops[1:]:
            piece = flipped(piece, pair_axes, mask)
        qkv_sums.append(
            (own_qkv[:, low:high, :].astype(jnp.float32) + piece[0].astype(jnp.float32)).astype(
                jnp.bfloat16
            )
        )
        out_sums.append(
            (own_out[:, low:high].astype(jnp.float32) + piece[1].astype(jnp.float32)).astype(
                jnp.bfloat16
            )
        )
    grad_qkv = jnp.concatenate(qkv_sums, axis=1)
    grad_out = jnp.concatenate(out_sums, axis=1)
    acts_block = jnp.stack(forward_outs)[None, None]
    grads_block = jnp.stack(backward_outs)[None, None]
    return (acts_block, grads_block, grad_qkv[None, None], grad_out[None, None])


def solution(mesh):
    in_specs = (
        P("mirror", None, "tp", None),
        P("mirror", None, "tp"),
        P("mirror", None, None, None),
        P(),
        P("mirror", "section", None),
        P("mirror", "section", None, None, "tp"),
        P("mirror", "section", "tp", None),
        P("mirror", "section", "tp", None),
        P("mirror", "section", "tp", None),
        P("mirror", "section", None, "tp", None),
        P("mirror", None, "tp", None),
    )
    out_specs = (
        P("mirror", "section", None, "tp", None),
        P("mirror", "section", None, "tp", None),
        P("mirror", "section", None, None, "tp"),
        P("mirror", "section", "tp", None),
    )
    return jax.shard_map(shards, mesh=mesh, in_specs=in_specs, out_specs=out_specs, check_vma=False)
```

```python
import math

import numpy as np

import jax
import jax.numpy as jnp
from jax import lax
from jax.sharding import PartitionSpec as P

HD = 128


def passed_along(block, axis, distance):
    devices = range(lax.axis_size(axis))
    route = [(i - distance, i) for i in devices if i - distance in devices]
    return lax.ppermute(block, axis, route)


def flipped(value, axis, mask):
    return lax.ppermute(value, axis, [(i, i ^ mask) for i in range(lax.axis_size(axis))])


def normalize(values, gain_row):
    mean_square = jnp.mean(values * values, axis=-1, keepdims=True)
    return values * lax.rsqrt(mean_square + 1e-05) * gain_row


def segment_mask(segment_ids):
    position = jnp.arange(segment_ids.shape[0], dtype=jnp.int32)
    causal = position[None, :] <= position[:, None]
    return causal & (segment_ids[:, None] == segment_ids[None, :])


def attend(queries, keys_all, values_all, seg_mask):
    scores = jnp.einsum(
        "ihd,jhd->hij", queries, keys_all, preferred_element_type=jnp.float32
    ) / math.sqrt(queries.shape[-1])
    scores = jnp.where(seg_mask[None], scores, -1e30)
    highest = lax.stop_gradient(jnp.max(scores, axis=-1, keepdims=True))
    expo = jnp.exp(scores - highest)
    probs = (expo / jnp.sum(expo, axis=-1, keepdims=True)).astype(values_all.dtype)
    return jnp.einsum("hij,jhd->ihd", probs, values_all, preferred_element_type=jnp.float32)


def embedding(feat_rows, type_rows, type_table):
    onehot = (
        type_rows[:, None] == jnp.arange(type_table.shape[0], dtype=jnp.int32)[None, :]
    ).astype(jnp.bfloat16)
    looked = jnp.dot(onehot, type_table, preferred_element_type=jnp.float32)
    return (feat_rows.astype(jnp.float32) + looked).astype(jnp.bfloat16)


def gathered(blocks):
    full = lax.all_gather(jnp.stack(blocks), "tp", axis=1, tiled=True)
    return [full[i] for i in range(len(blocks))]


def scattered(blocks):
    part = lax.psum_scatter(jnp.stack(blocks), "tp", scatter_dimension=1, tiled=True)
    return [part[i] for i in range(len(blocks))]


def shards(
    feats, types, segs, type_table, gains, w_qkv, w_out, carry_acts, grad_in, saved, cotangent
):
    sections = lax.axis_size("section")
    section_index = lax.axis_index("section")
    on_first_pipe = lax.axis_index("mirror") == 0
    position = jnp.where(on_first_pipe, section_index, sections - 1 - section_index)
    gain_row = gains[0, 0]
    qkv_weight = w_qkv[0, 0]
    out_weight = w_out[0, 0]
    window_steps = feats.shape[1]
    seq_len = segs.shape[3]
    model_width = qkv_weight.shape[1]
    inner_here = qkv_weight.shape[-1]
    heads_here = inner_here // HD

    def mask_for(which, index):
        return segment_mask(lax.dynamic_index_in_dim(segs[0, which], index, 0, keepdims=False))

    def normed_rows(rows):
        return normalize(rows.astype(jnp.float32), gain_row).astype(jnp.bfloat16)

    def heads_of(normed_full):
        projected = jnp.einsum(
            "sd,cdn->csn", normed_full, qkv_weight, preferred_element_type=jnp.float32
        ).astype(jnp.bfloat16)
        return projected.reshape(3, seq_len, heads_here, HD)

    def forward_part(normed_full, seg_mask):
        heads_view = heads_of(normed_full)
        mixed = (
            attend(heads_view[0], heads_view[1], heads_view[2], seg_mask)
            .reshape(seq_len, inner_here)
            .astype(jnp.bfloat16)
        )
        return jnp.dot(mixed, out_weight, preferred_element_type=jnp.float32).astype(jnp.bfloat16)

    def backward_part(normed_full, upstream_full, seg_mask):
        heads_view = heads_of(normed_full)
        primal, pull_attend = jax.vjp(
            lambda query_part, key_part, value_part: attend(
                query_part, key_part, value_part, seg_mask
            ),
            heads_view[0],
            heads_view[1],
            heads_view[2],
        )
        mixed = primal.reshape(seq_len, inner_here).astype(jnp.bfloat16)
        d_mixed = jnp.einsum(
            "sd,nd->sn", upstream_full, out_weight, preferred_element_type=jnp.float32
        ).astype(jnp.bfloat16)
        pulled = pull_attend(d_mixed.astype(jnp.float32).reshape(seq_len, heads_here, HD))
        d_projected = jnp.stack(pulled).reshape(3, seq_len, inner_here)
        d_normed_part = jnp.einsum(
            "csn,cdn->sd", d_projected, qkv_weight, preferred_element_type=jnp.float32
        ).astype(jnp.bfloat16)
        return d_normed_part, d_projected, mixed

    def weight_terms(normed_fulls, d_projecteds, mixeds, upstream_fulls):
        qkv_sum = None
        out_sum = None
        for normed_full, d_projected, mixed, upstream_full in zip(
            normed_fulls, d_projecteds, mixeds, upstream_fulls
        ):
            qkv_term = jnp.einsum(
                "sd,csn->cdn", normed_full, d_projected, preferred_element_type=jnp.float32
            )
            out_term = jnp.einsum(
                "sn,sd->nd", mixed, upstream_full, preferred_element_type=jnp.float32
            )
            qkv_sum = qkv_term if qkv_sum is None else qkv_sum + qkv_term
            out_sum = out_term if out_sum is None else out_sum + out_term
        return qkv_sum.astype(jnp.bfloat16), out_sum.astype(jnp.bfloat16)

    def input_grad(layer_in, upstream, d_normed):
        unused_norm, pull_norm = jax.vjp(
            lambda inputs: normalize(inputs, gain_row), layer_in.astype(jnp.float32)
        )
        d_input = pull_norm(d_normed.astype(jnp.float32))[0]
        return (upstream.astype(jnp.float32) + d_input).astype(jnp.bfloat16)

    pair_axes = ("section", "mirror")
    mirror_size = lax.axis_size("mirror")
    up_pairs = []
    down_pairs = []
    for section in range(sections):
        for mirror in range(mirror_size):
            ahead = 1 if mirror == 0 else -1
            if 0 <= section + ahead < sections:
                up_pairs.append((section * mirror_size + mirror, (section + ahead) * mirror_size + mirror))
            if 0 <= section - ahead < sections:
                down_pairs.append((section * mirror_size + mirror, (section - ahead) * mirror_size + mirror))

    bit_count = lax.axis_size(pair_axes).bit_length() - 1
    section_bits = list(range(1, bit_count))
    if section_bits:
        routes = []
        for start in range(len(section_bits)):
            order = section_bits[start:] + section_bits[:start]
            routes.append([1 | (1 << order[0])] + [1 << bit for bit in order[1:]])
    else:
        routes = [[1]]

    def to_partner(value, axis):
        cuts = np.linspace(0, value.shape[axis], len(routes) + 1).astype(int)
        pieces = []
        for index, hops in enumerate(routes):
            piece = lax.slice_in_dim(value, int(cuts[index]), int(cuts[index + 1]), axis=axis)
            for mask in hops:
                piece = flipped(piece, pair_axes, mask)
            pieces.append(piece)
        return jnp.concatenate(pieces, axis=axis) if len(pieces) > 1 else pieces[0]

    last_step = window_steps - 1
    saved_normed = [normed_rows(saved[0, 0, t]) for t in range(window_steps)]
    backward_normed_full = [None] * window_steps
    upstream_fulls = []
    d_projecteds = []
    mixeds = []
    partner_normed = [None] * window_steps
    partner_upstream = []
    partner_d_projected = []
    partner_mixed = []
    forward_outs = []
    backward_outs = []
    forward_in = carry_acts[0, 0]
    backward_in = grad_in[0, 0]
    for step_index in range(window_steps):
        embedded = embedding(feats[0, step_index], types[0, step_index], type_table)
        current = jnp.where(position == 0, embedded, forward_in)
        upstream = jnp.where(position == sections - 1, cotangent[0, step_index], backward_in)
        if step_index == 0:
            upstream_full, backward_normed_full[0] = gathered([upstream, saved_normed[0]])
            sent = to_partner(jnp.stack([upstream_full, backward_normed_full[0]]), 1)
            partner_upstream.append(sent[0])
            partner_normed[0] = sent[1]
            forward_rows, upstream_full = lax.optimization_barrier(
                ([normed_rows(current)] + saved_normed[1:], upstream_full)
            )
            forward_normed_full, *later = gathered(forward_rows)
            backward_normed_full[1:] = later
            for later_index, later_full in enumerate(later):
                partner_normed[later_index + 1] = to_partner(later_full, 0)
        else:
            upstream, last_result, held = lax.optimization_barrier(
                (upstream, last_result, (partner_upstream, partner_normed[:step_index], partner_d_projected, partner_mixed))
            )
            partner_upstream, normed_done, partner_d_projected, partner_mixed = held
            partner_normed[:step_index] = normed_done
            upstream_full = gathered([upstream])[0]
            partner_upstream.append(to_partner(upstream_full, 0))
            forward_normed, upstream_full = lax.optimization_barrier(
                (normed_rows(current), upstream_full)
            )
            forward_normed_full = gathered([forward_normed])[0]
        d_normed_part, d_projected, mixed = backward_part(
            backward_normed_full[step_index], upstream_full, mask_for(1, step_index + position)
        )
        upstream_fulls.append(upstream_full)
        d_projecteds.append(d_projected)
        mixeds.append(mixed)
        partner_d_projected.append(to_partner(d_projected, 1))
        partner_mixed.append(to_partner(mixed, 0))
        d_normed_part, forward_normed_full = lax.optimization_barrier(
            (d_normed_part, forward_normed_full)
        )
        d_normed = scattered([d_normed_part])[0]
        attn_part = forward_part(
            forward_normed_full, mask_for(0, step_index - position + sections - 1)
        )
        attn_part, d_normed = lax.optimization_barrier((attn_part, d_normed))
        attn_rows = scattered([attn_part])[0]
        last_result = attn_rows
        backward_out = input_grad(saved[0, 0, step_index], upstream, d_normed)
        forward_out = (current.astype(jnp.float32) + attn_rows.astype(jnp.float32)).astype(
            jnp.bfloat16
        )
        forward_outs.append(forward_out)
        backward_outs.append(backward_out)
        if step_index < last_step:
            backward_in = lax.ppermute(backward_out, pair_axes, down_pairs)
            forward_in = lax.ppermute(forward_out, pair_axes, up_pairs)

    own_qkv, own_out = weight_terms(backward_normed_full, d_projecteds, mixeds, upstream_fulls)
    other_qkv, other_out = weight_terms(
        partner_normed, partner_d_projected, partner_mixed, partner_upstream
    )
    grad_qkv = (own_qkv.astype(jnp.float32) + other_qkv.astype(jnp.float32)).astype(jnp.bfloat16)
    grad_out = (own_out.astype(jnp.float32) + other_out.astype(jnp.float32)).astype(jnp.bfloat16)
    acts_block = jnp.stack(forward_outs)[None, None]
    grads_block = jnp.stack(backward_outs)[None, None]
    return (acts_block, grads_block, grad_qkv[None, None], grad_out[None, None])


def solution(mesh):
    in_specs = (
        P("mirror", None, "tp", None),
        P("mirror", None, "tp"),
        P("mirror", None, None, None),
        P(),
        P("mirror", "section", None),
        P("mirror", "section", None, None, "tp"),
        P("mirror", "section", "tp", None),
        P("mirror", "section", "tp", None),
        P("mirror", "section", "tp", None),
        P("mirror", "section", None, "tp", None),
        P("mirror", None, "tp", None),
    )
    out_specs = (
        P("mirror", "section", None, "tp", None),
        P("mirror", "section", None, "tp", None),
        P("mirror", "section", None, None, "tp"),
        P("mirror", "section", "tp", None),
    )
    return jax.shard_map(shards, mesh=mesh, in_specs=in_specs, out_specs=out_specs, check_vma=False)
```

```python
import math

import numpy as np

import jax
import jax.numpy as jnp
from jax import lax
from jax.sharding import PartitionSpec as P

HD = 128


def passed_along(block, axis, distance):
    devices = range(lax.axis_size(axis))
    route = [(i - distance, i) for i in devices if i - distance in devices]
    return lax.ppermute(block, axis, route)


def flipped(value, axis, mask):
    return lax.ppermute(value, axis, [(i, i ^ mask) for i in range(lax.axis_size(axis))])


def normalize(values, gain_row):
    mean_square = jnp.mean(values * values, axis=-1, keepdims=True)
    return values * lax.rsqrt(mean_square + 1e-05) * gain_row


def segment_mask(segment_ids):
    position = jnp.arange(segment_ids.shape[0], dtype=jnp.int32)
    causal = position[None, :] <= position[:, None]
    return causal & (segment_ids[:, None] == segment_ids[None, :])


def attend(queries, keys_all, values_all, seg_mask):
    scores = jnp.einsum(
        "ihd,jhd->hij", queries, keys_all, preferred_element_type=jnp.float32
    ) / math.sqrt(queries.shape[-1])
    scores = jnp.where(seg_mask[None], scores, -1e30)
    highest = lax.stop_gradient(jnp.max(scores, axis=-1, keepdims=True))
    expo = jnp.exp(scores - highest)
    probs = (expo / jnp.sum(expo, axis=-1, keepdims=True)).astype(values_all.dtype)
    return jnp.einsum("hij,jhd->ihd", probs, values_all, preferred_element_type=jnp.float32)


def embedding(feat_rows, type_rows, type_table):
    onehot = (
        type_rows[:, None] == jnp.arange(type_table.shape[0], dtype=jnp.int32)[None, :]
    ).astype(jnp.bfloat16)
    looked = jnp.dot(onehot, type_table, preferred_element_type=jnp.float32)
    return (feat_rows.astype(jnp.float32) + looked).astype(jnp.bfloat16)


def gathered(blocks):
    full = lax.all_gather(jnp.stack(blocks), "tp", axis=1, tiled=True)
    return [full[i] for i in range(len(blocks))]


def scattered(blocks):
    part = lax.psum_scatter(jnp.stack(blocks), "tp", scatter_dimension=1, tiled=True)
    return [part[i] for i in range(len(blocks))]


def shards(
    feats, types, segs, type_table, gains, w_qkv, w_out, carry_acts, grad_in, saved, cotangent
):
    sections = lax.axis_size("section")
    section_index = lax.axis_index("section")
    on_first_pipe = lax.axis_index("mirror") == 0
    position = jnp.where(on_first_pipe, section_index, sections - 1 - section_index)
    gain_row = gains[0, 0]
    qkv_weight = w_qkv[0, 0]
    out_weight = w_out[0, 0]
    window_steps = feats.shape[1]
    seq_len = segs.shape[3]
    model_width = qkv_weight.shape[1]
    inner_here = qkv_weight.shape[-1]
    heads_here = inner_here // HD

    def mask_for(which, index):
        return segment_mask(lax.dynamic_index_in_dim(segs[0, which], index, 0, keepdims=False))

    def normed_rows(rows):
        return normalize(rows.astype(jnp.float32), gain_row).astype(jnp.bfloat16)

    def heads_of(normed_full):
        projected = jnp.einsum(
            "sd,cdn->csn", normed_full, qkv_weight, preferred_element_type=jnp.float32
        ).astype(jnp.bfloat16)
        return projected.reshape(3, seq_len, heads_here, HD)

    def forward_part(normed_full, seg_mask):
        heads_view = heads_of(normed_full)
        mixed = (
            attend(heads_view[0], heads_view[1], heads_view[2], seg_mask)
            .reshape(seq_len, inner_here)
            .astype(jnp.bfloat16)
        )
        return jnp.dot(mixed, out_weight, preferred_element_type=jnp.float32).astype(jnp.bfloat16)

    def backward_part(normed_full, upstream_full, seg_mask):
        heads_view = heads_of(normed_full)
        primal, pull_attend = jax.vjp(
            lambda query_part, key_part, value_part: attend(
                query_part, key_part, value_part, seg_mask
            ),
            heads_view[0],
            heads_view[1],
            heads_view[2],
        )
        mixed = primal.reshape(seq_len, inner_here).astype(jnp.bfloat16)
        d_mixed = jnp.einsum(
            "sd,nd->sn", upstream_full, out_weight, preferred_element_type=jnp.float32
        ).astype(jnp.bfloat16)
        pulled = pull_attend(d_mixed.astype(jnp.float32).reshape(seq_len, heads_here, HD))
        d_projected = jnp.stack(pulled).reshape(3, seq_len, inner_here)
        d_normed_part = jnp.einsum(
            "csn,cdn->sd", d_projected, qkv_weight, preferred_element_type=jnp.float32
        ).astype(jnp.bfloat16)
        return d_normed_part, d_projected, mixed

    def weight_terms(normed_fulls, d_projecteds, mixeds, upstream_fulls):
        qkv_sum = None
        out_sum = None
        for normed_full, d_projected, mixed, upstream_full in zip(
            normed_fulls, d_projecteds, mixeds, upstream_fulls
        ):
            qkv_term = jnp.einsum(
                "sd,csn->cdn", normed_full, d_projected, preferred_element_type=jnp.float32
            )
            out_term = jnp.einsum(
                "sn,sd->nd", mixed, upstream_full, preferred_element_type=jnp.float32
            )
            qkv_sum = qkv_term if qkv_sum is None else qkv_sum + qkv_term
            out_sum = out_term if out_sum is None else out_sum + out_term
        return qkv_sum.astype(jnp.bfloat16), out_sum.astype(jnp.bfloat16)

    def input_grad(layer_in, upstream, d_normed):
        unused_norm, pull_norm = jax.vjp(
            lambda inputs: normalize(inputs, gain_row), layer_in.astype(jnp.float32)
        )
        d_input = pull_norm(d_normed.astype(jnp.float32))[0]
        return (upstream.astype(jnp.float32) + d_input).astype(jnp.bfloat16)

    pair_axes = ("section", "mirror")
    mirror_size = lax.axis_size("mirror")
    up_pairs = []
    down_pairs = []
    for section in range(sections):
        for mirror in range(mirror_size):
            ahead = 1 if mirror == 0 else -1
            if 0 <= section + ahead < sections:
                up_pairs.append((section * mirror_size + mirror, (section + ahead) * mirror_size + mirror))
            if 0 <= section - ahead < sections:
                down_pairs.append((section * mirror_size + mirror, (section - ahead) * mirror_size + mirror))

    bit_count = lax.axis_size(pair_axes).bit_length() - 1
    section_bits = list(range(1, bit_count))
    if section_bits:
        routes = []
        for start in range(len(section_bits)):
            order = section_bits[start:] + section_bits[:start]
            routes.append([1 | (1 << order[0])] + [1 << bit for bit in order[1:]])
    else:
        routes = [[1]]

    def to_partner(value, axis):
        cuts = np.linspace(0, value.shape[axis], len(routes) + 1).astype(int)
        pieces = []
        for index, hops in enumerate(routes):
            piece = lax.slice_in_dim(value, int(cuts[index]), int(cuts[index + 1]), axis=axis)
            for mask in hops:
                piece = flipped(piece, pair_axes, mask)
            pieces.append(piece)
        return jnp.concatenate(pieces, axis=axis) if len(pieces) > 1 else pieces[0]

    last_step = window_steps - 1
    saved_normed = [normed_rows(saved[0, 0, t]) for t in range(window_steps)]
    backward_normed_full = [None] * window_steps
    upstream_fulls = []
    d_projecteds = []
    mixeds = []
    partner_normed = [None] * window_steps
    partner_upstream = []
    partner_d_projected = []
    partner_mixed = []
    forward_outs = []
    backward_outs = []
    forward_in = carry_acts[0, 0]
    backward_in = grad_in[0, 0]
    for step_index in range(window_steps):
        embedded = embedding(feats[0, step_index], types[0, step_index], type_table)
        current = jnp.where(position == 0, embedded, forward_in)
        upstream = jnp.where(position == sections - 1, cotangent[0, step_index], backward_in)
        if step_index == 0:
            upstream_full, backward_normed_full[0] = gathered([upstream, saved_normed[0]])
            forward_rows, upstream_full = lax.optimization_barrier(
                ([normed_rows(current)] + saved_normed[1:], upstream_full)
            )
            forward_normed_full, *later = gathered(forward_rows)
            backward_normed_full[1:] = later
        else:
            upstream_full, forward_normed_full = gathered([upstream, normed_rows(current)])
        d_normed_part, d_projected, mixed = backward_part(
            backward_normed_full[step_index], upstream_full, mask_for(1, step_index + position)
        )
        upstream_fulls.append(upstream_full)
        d_projecteds.append(d_projected)
        mixeds.append(mixed)
        attn_part = forward_part(
            forward_normed_full, mask_for(0, step_index - position + sections - 1)
        )
        d_normed, attn_rows = scattered([d_normed_part, attn_part])
        backward_out = input_grad(saved[0, 0, step_index], upstream, d_normed)
        forward_out = (current.astype(jnp.float32) + attn_rows.astype(jnp.float32)).astype(
            jnp.bfloat16
        )
        forward_outs.append(forward_out)
        backward_outs.append(backward_out)
        if step_index < last_step:
            backward_in = lax.ppermute(backward_out, pair_axes, down_pairs)
            forward_in = lax.ppermute(forward_out, pair_axes, up_pairs)
            held = (upstream_fulls, backward_normed_full, d_projecteds, mixeds)
            held, backward_in, forward_in = lax.optimization_barrier(
                (held, backward_in, forward_in)
            )
            upstream_fulls, backward_normed_full, d_projecteds, mixeds = held
            if step_index == 0:
                for later_index in range(window_steps):
                    partner_normed[later_index] = to_partner(backward_normed_full[later_index], 0)
        partner_upstream.append(to_partner(upstream_fulls[step_index], 0))
        partner_d_projected.append(to_partner(d_projecteds[step_index], 1))
        partner_mixed.append(to_partner(mixeds[step_index], 0))

    own_qkv, own_out = weight_terms(backward_normed_full, d_projecteds, mixeds, upstream_fulls)
    other_qkv, other_out = weight_terms(
        partner_normed, partner_d_projected, partner_mixed, partner_upstream
    )
    grad_qkv = (own_qkv.astype(jnp.float32) + other_qkv.astype(jnp.float32)).astype(jnp.bfloat16)
    grad_out = (own_out.astype(jnp.float32) + other_out.astype(jnp.float32)).astype(jnp.bfloat16)
    acts_block = jnp.stack(forward_outs)[None, None]
    grads_block = jnp.stack(backward_outs)[None, None]
    return (acts_block, grads_block, grad_qkv[None, None], grad_out[None, None])


def solution(mesh):
    in_specs = (
        P("mirror", None, "tp", None),
        P("mirror", None, "tp"),
        P("mirror", None, None, None),
        P(),
        P("mirror", "section", None),
        P("mirror", "section", None, None, "tp"),
        P("mirror", "section", "tp", None),
        P("mirror", "section", "tp", None),
        P("mirror", "section", "tp", None),
        P("mirror", "section", None, "tp", None),
        P("mirror", None, "tp", None),
    )
    out_specs = (
        P("mirror", "section", None, "tp", None),
        P("mirror", "section", None, "tp", None),
        P("mirror", "section", None, None, "tp"),
        P("mirror", "section", "tp", None),
    )
    return jax.shard_map(shards, mesh=mesh, in_specs=in_specs, out_specs=out_specs, check_vma=False)
```

```python
import math

import numpy as np

import jax
import jax.numpy as jnp
from jax import lax
from jax.sharding import PartitionSpec as P

HD = 128


def passed_along(block, axis, distance):
    devices = range(lax.axis_size(axis))
    route = [(i - distance, i) for i in devices if i - distance in devices]
    return lax.ppermute(block, axis, route)


def flipped(value, axis, mask):
    return lax.ppermute(value, axis, [(i, i ^ mask) for i in range(lax.axis_size(axis))])


def normalize(values, gain_row):
    mean_square = jnp.mean(values * values, axis=-1, keepdims=True)
    return values * lax.rsqrt(mean_square + 1e-05) * gain_row


def segment_mask(segment_ids):
    position = jnp.arange(segment_ids.shape[0], dtype=jnp.int32)
    causal = position[None, :] <= position[:, None]
    return causal & (segment_ids[:, None] == segment_ids[None, :])


def attend(queries, keys_all, values_all, seg_mask):
    scores = jnp.einsum(
        "ihd,jhd->hij", queries, keys_all, preferred_element_type=jnp.float32
    ) / math.sqrt(queries.shape[-1])
    scores = jnp.where(seg_mask[None], scores, -1e30)
    highest = lax.stop_gradient(jnp.max(scores, axis=-1, keepdims=True))
    expo = jnp.exp(scores - highest)
    probs = (expo / jnp.sum(expo, axis=-1, keepdims=True)).astype(values_all.dtype)
    return jnp.einsum("hij,jhd->ihd", probs, values_all, preferred_element_type=jnp.float32)


def embedding(feat_rows, type_rows, type_table):
    onehot = (
        type_rows[:, None] == jnp.arange(type_table.shape[0], dtype=jnp.int32)[None, :]
    ).astype(jnp.bfloat16)
    looked = jnp.dot(onehot, type_table, preferred_element_type=jnp.float32)
    return (feat_rows.astype(jnp.float32) + looked).astype(jnp.bfloat16)


def gathered(blocks):
    full = lax.all_gather(jnp.stack(blocks), "tp", axis=1, tiled=True)
    return [full[i] for i in range(len(blocks))]


def scattered(blocks):
    part = lax.psum_scatter(jnp.stack(blocks), "tp", scatter_dimension=1, tiled=True)
    return [part[i] for i in range(len(blocks))]


def shards(
    feats, types, segs, type_table, gains, w_qkv, w_out, carry_acts, grad_in, saved, cotangent
):
    sections = lax.axis_size("section")
    section_index = lax.axis_index("section")
    on_first_pipe = lax.axis_index("mirror") == 0
    position = jnp.where(on_first_pipe, section_index, sections - 1 - section_index)
    gain_row = gains[0, 0]
    qkv_weight = w_qkv[0, 0]
    out_weight = w_out[0, 0]
    window_steps = feats.shape[1]
    seq_len = segs.shape[3]
    model_width = qkv_weight.shape[1]
    inner_here = qkv_weight.shape[-1]
    heads_here = inner_here // HD

    def mask_for(which, index):
        return segment_mask(lax.dynamic_index_in_dim(segs[0, which], index, 0, keepdims=False))

    def normed_rows(rows):
        return normalize(rows.astype(jnp.float32), gain_row).astype(jnp.bfloat16)

    def heads_of(normed_full):
        projected = jnp.einsum(
            "sd,cdn->csn", normed_full, qkv_weight, preferred_element_type=jnp.float32
        ).astype(jnp.bfloat16)
        return projected.reshape(3, seq_len, heads_here, HD)

    def forward_part(normed_full, seg_mask):
        heads_view = heads_of(normed_full)
        mixed = (
            attend(heads_view[0], heads_view[1], heads_view[2], seg_mask)
            .reshape(seq_len, inner_here)
            .astype(jnp.bfloat16)
        )
        return jnp.dot(mixed, out_weight, preferred_element_type=jnp.float32).astype(jnp.bfloat16)

    def backward_part(normed_full, upstream_full, seg_mask):
        heads_view = heads_of(normed_full)
        primal, pull_attend = jax.vjp(
            lambda query_part, key_part, value_part: attend(
                query_part, key_part, value_part, seg_mask
            ),
            heads_view[0],
            heads_view[1],
            heads_view[2],
        )
        mixed = primal.reshape(seq_len, inner_here).astype(jnp.bfloat16)
        d_mixed = jnp.einsum(
            "sd,nd->sn", upstream_full, out_weight, preferred_element_type=jnp.float32
        ).astype(jnp.bfloat16)
        pulled = pull_attend(d_mixed.astype(jnp.float32).reshape(seq_len, heads_here, HD))
        d_projected = jnp.stack(pulled).reshape(3, seq_len, inner_here)
        d_normed_part = jnp.einsum(
            "csn,cdn->sd", d_projected, qkv_weight, preferred_element_type=jnp.float32
        ).astype(jnp.bfloat16)
        return d_normed_part, d_projected, mixed

    def weight_terms(normed_fulls, d_projecteds, mixeds, upstream_fulls):
        qkv_sum = None
        out_sum = None
        for normed_full, d_projected, mixed, upstream_full in zip(
            normed_fulls, d_projecteds, mixeds, upstream_fulls
        ):
            qkv_term = jnp.einsum(
                "sd,csn->cdn", normed_full, d_projected, preferred_element_type=jnp.float32
            )
            out_term = jnp.einsum(
                "sn,sd->nd", mixed, upstream_full, preferred_element_type=jnp.float32
            )
            qkv_sum = qkv_term if qkv_sum is None else qkv_sum + qkv_term
            out_sum = out_term if out_sum is None else out_sum + out_term
        return qkv_sum.astype(jnp.bfloat16), out_sum.astype(jnp.bfloat16)

    def input_grad(layer_in, upstream, d_normed):
        unused_norm, pull_norm = jax.vjp(
            lambda inputs: normalize(inputs, gain_row), layer_in.astype(jnp.float32)
        )
        d_input = pull_norm(d_normed.astype(jnp.float32))[0]
        return (upstream.astype(jnp.float32) + d_input).astype(jnp.bfloat16)

    pair_axes = ("section", "mirror")
    mirror_size = lax.axis_size("mirror")
    up_pairs = []
    down_pairs = []
    for section in range(sections):
        for mirror in range(mirror_size):
            ahead = 1 if mirror == 0 else -1
            if 0 <= section + ahead < sections:
                up_pairs.append((section * mirror_size + mirror, (section + ahead) * mirror_size + mirror))
            if 0 <= section - ahead < sections:
                down_pairs.append((section * mirror_size + mirror, (section - ahead) * mirror_size + mirror))

    bit_count = lax.axis_size(pair_axes).bit_length() - 1
    section_bits = list(range(1, bit_count))
    if section_bits:
        routes = []
        for start in range(len(section_bits)):
            order = section_bits[start:] + section_bits[:start]
            routes.append([1 | (1 << order[0])] + [1 << bit for bit in order[1:]])
    else:
        routes = [[1]]

    def to_partner(value, axis):
        cuts = np.linspace(0, value.shape[axis], len(routes) + 1).astype(int)
        pieces = []
        for index, hops in enumerate(routes):
            piece = lax.slice_in_dim(value, int(cuts[index]), int(cuts[index + 1]), axis=axis)
            for mask in hops:
                piece = flipped(piece, pair_axes, mask)
            pieces.append(piece)
        return jnp.concatenate(pieces, axis=axis) if len(pieces) > 1 else pieces[0]

    last_step = window_steps - 1
    saved_normed = [normed_rows(saved[0, 0, t]) for t in range(window_steps)]
    backward_normed_full = [None] * window_steps
    upstream_fulls = []
    d_projecteds = []
    mixeds = []
    partner_normed = [None] * window_steps
    partner_upstream = []
    partner_d_projected = []
    partner_mixed = []
    forward_outs = []
    backward_outs = []
    forward_in = carry_acts[0, 0]
    backward_in = grad_in[0, 0]
    for step_index in range(window_steps):
        embedded = embedding(feats[0, step_index], types[0, step_index], type_table)
        current = jnp.where(position == 0, embedded, forward_in)
        upstream = jnp.where(position == sections - 1, cotangent[0, step_index], backward_in)
        if step_index == 0:
            upstream_full, backward_normed_full[0] = gathered([upstream, saved_normed[0]])
            forward_rows, upstream_full = lax.optimization_barrier(
                ([normed_rows(current)] + saved_normed[1:], upstream_full)
            )
            forward_normed_full, *later = gathered(forward_rows)
            backward_normed_full[1:] = later
            rows_sent = [upstream_full, backward_normed_full[0]]
        else:
            upstream, last_result = lax.optimization_barrier((upstream, last_result))
            upstream_full = gathered([upstream])[0]
            rows_sent = [upstream_full] + ([backward_normed_full[step_index]] if step_index == 1 else [])
            if step_index == 1:
                rows_sent += backward_normed_full[2:]
            forward_normed, upstream_full = lax.optimization_barrier(
                (normed_rows(current), upstream_full)
            )
            forward_normed_full = gathered([forward_normed])[0]
        d_normed_part, d_projected, mixed = backward_part(
            backward_normed_full[step_index], upstream_full, mask_for(1, step_index + position)
        )
        upstream_fulls.append(upstream_full)
        d_projecteds.append(d_projected)
        mixeds.append(mixed)
        rows_back = to_partner(jnp.stack(rows_sent), 1)
        small_back = to_partner(jnp.concatenate([d_projected, mixed[None]]), 1)
        partner_upstream.append(rows_back[0])
        if step_index == 0:
            partner_normed[0] = rows_back[1]
        elif step_index == 1:
            partner_normed[1:] = [rows_back[i] for i in range(1, rows_back.shape[0])]
        partner_d_projected.append(small_back[:3])
        partner_mixed.append(small_back[3])
        d_normed_part, forward_normed_full = lax.optimization_barrier(
            (d_normed_part, forward_normed_full)
        )
        d_normed = scattered([d_normed_part])[0]
        attn_part = forward_part(
            forward_normed_full, mask_for(0, step_index - position + sections - 1)
        )
        attn_part, d_normed = lax.optimization_barrier((attn_part, d_normed))
        attn_rows = scattered([attn_part])[0]
        last_result = attn_rows
        backward_out = input_grad(saved[0, 0, step_index], upstream, d_normed)
        forward_out = (current.astype(jnp.float32) + attn_rows.astype(jnp.float32)).astype(
            jnp.bfloat16
        )
        forward_outs.append(forward_out)
        backward_outs.append(backward_out)
        if step_index < last_step:
            held = (partner_upstream, partner_normed[:1], partner_d_projected, partner_mixed)
            backward_out, held = lax.optimization_barrier((backward_out, held))
            partner_upstream, partner_normed[:1], partner_d_projected, partner_mixed = held
            backward_in = lax.ppermute(backward_out, pair_axes, down_pairs)
            forward_in = lax.ppermute(forward_out, pair_axes, up_pairs)

    own_qkv, own_out = weight_terms(backward_normed_full, d_projecteds, mixeds, upstream_fulls)
    other_qkv, other_out = weight_terms(
        partner_normed, partner_d_projected, partner_mixed, partner_upstream
    )
    grad_qkv = (own_qkv.astype(jnp.float32) + other_qkv.astype(jnp.float32)).astype(jnp.bfloat16)
    grad_out = (own_out.astype(jnp.float32) + other_out.astype(jnp.float32)).astype(jnp.bfloat16)
    acts_block = jnp.stack(forward_outs)[None, None]
    grads_block = jnp.stack(backward_outs)[None, None]
    return (acts_block, grads_block, grad_qkv[None, None], grad_out[None, None])


def solution(mesh):
    in_specs = (
        P("mirror", None, "tp", None),
        P("mirror", None, "tp"),
        P("mirror", None, None, None),
        P(),
        P("mirror", "section", None),
        P("mirror", "section", None, None, "tp"),
        P("mirror", "section", "tp", None),
        P("mirror", "section", "tp", None),
        P("mirror", "section", "tp", None),
        P("mirror", "section", None, "tp", None),
        P("mirror", None, "tp", None),
    )
    out_specs = (
        P("mirror", "section", None, "tp", None),
        P("mirror", "section", None, "tp", None),
        P("mirror", "section", None, None, "tp"),
        P("mirror", "section", "tp", None),
    )
    return jax.shard_map(shards, mesh=mesh, in_specs=in_specs, out_specs=out_specs, check_vma=False)
```

```python
import math

import numpy as np

import jax
import jax.numpy as jnp
from jax import lax
from jax.sharding import PartitionSpec as P

HD = 128


def passed_along(block, axis, distance):
    devices = range(lax.axis_size(axis))
    route = [(i - distance, i) for i in devices if i - distance in devices]
    return lax.ppermute(block, axis, route)


def flipped(value, axis, mask):
    return lax.ppermute(value, axis, [(i, i ^ mask) for i in range(lax.axis_size(axis))])


def normalize(values, gain_row):
    mean_square = jnp.mean(values * values, axis=-1, keepdims=True)
    return values * lax.rsqrt(mean_square + 1e-05) * gain_row


def segment_mask(segment_ids):
    position = jnp.arange(segment_ids.shape[0], dtype=jnp.int32)
    causal = position[None, :] <= position[:, None]
    return causal & (segment_ids[:, None] == segment_ids[None, :])


def attend(queries, keys_all, values_all, seg_mask):
    scores = jnp.einsum(
        "ihd,jhd->hij", queries, keys_all, preferred_element_type=jnp.float32
    ) / math.sqrt(queries.shape[-1])
    scores = jnp.where(seg_mask[None], scores, -1e30)
    highest = lax.stop_gradient(jnp.max(scores, axis=-1, keepdims=True))
    expo = jnp.exp(scores - highest)
    probs = (expo / jnp.sum(expo, axis=-1, keepdims=True)).astype(values_all.dtype)
    return jnp.einsum("hij,jhd->ihd", probs, values_all, preferred_element_type=jnp.float32)


def embedding(feat_rows, type_rows, type_table):
    onehot = (
        type_rows[:, None] == jnp.arange(type_table.shape[0], dtype=jnp.int32)[None, :]
    ).astype(jnp.bfloat16)
    looked = jnp.dot(onehot, type_table, preferred_element_type=jnp.float32)
    return (feat_rows.astype(jnp.float32) + looked).astype(jnp.bfloat16)


def gathered(blocks):
    full = lax.all_gather(jnp.stack(blocks), "tp", axis=1, tiled=True)
    return [full[i] for i in range(len(blocks))]


def scattered(blocks):
    part = lax.psum_scatter(jnp.stack(blocks), "tp", scatter_dimension=1, tiled=True)
    return [part[i] for i in range(len(blocks))]


def shards(
    feats, types, segs, type_table, gains, w_qkv, w_out, carry_acts, grad_in, saved, cotangent
):
    sections = lax.axis_size("section")
    section_index = lax.axis_index("section")
    on_first_pipe = lax.axis_index("mirror") == 0
    position = jnp.where(on_first_pipe, section_index, sections - 1 - section_index)
    gain_row = gains[0, 0]
    qkv_weight = w_qkv[0, 0]
    out_weight = w_out[0, 0]
    window_steps = feats.shape[1]
    seq_len = segs.shape[3]
    model_width = qkv_weight.shape[1]
    inner_here = qkv_weight.shape[-1]
    heads_here = inner_here // HD

    def mask_for(which, index):
        return segment_mask(lax.dynamic_index_in_dim(segs[0, which], index, 0, keepdims=False))

    def normed_rows(rows):
        return normalize(rows.astype(jnp.float32), gain_row).astype(jnp.bfloat16)

    def heads_of(normed_full):
        projected = jnp.einsum(
            "sd,cdn->csn", normed_full, qkv_weight, preferred_element_type=jnp.float32
        ).astype(jnp.bfloat16)
        return projected.reshape(3, seq_len, heads_here, HD)

    def forward_part(normed_full, seg_mask):
        heads_view = heads_of(normed_full)
        mixed = (
            attend(heads_view[0], heads_view[1], heads_view[2], seg_mask)
            .reshape(seq_len, inner_here)
            .astype(jnp.bfloat16)
        )
        return jnp.dot(mixed, out_weight, preferred_element_type=jnp.float32).astype(jnp.bfloat16)

    def backward_part(normed_full, upstream_full, seg_mask):
        heads_view = heads_of(normed_full)
        primal, pull_attend = jax.vjp(
            lambda query_part, key_part, value_part: attend(
                query_part, key_part, value_part, seg_mask
            ),
            heads_view[0],
            heads_view[1],
            heads_view[2],
        )
        mixed = primal.reshape(seq_len, inner_here).astype(jnp.bfloat16)
        d_mixed = jnp.einsum(
            "sd,nd->sn", upstream_full, out_weight, preferred_element_type=jnp.float32
        ).astype(jnp.bfloat16)
        pulled = pull_attend(d_mixed.astype(jnp.float32).reshape(seq_len, heads_here, HD))
        d_projected = jnp.stack(pulled).reshape(3, seq_len, inner_here)
        d_normed_part = jnp.einsum(
            "csn,cdn->sd", d_projected, qkv_weight, preferred_element_type=jnp.float32
        ).astype(jnp.bfloat16)
        return d_normed_part, d_projected, mixed

    def weight_terms(normed_fulls, d_projecteds, mixeds, upstream_fulls):
        qkv_sum = None
        out_sum = None
        for normed_full, d_projected, mixed, upstream_full in zip(
            normed_fulls, d_projecteds, mixeds, upstream_fulls
        ):
            qkv_term = jnp.einsum(
                "sd,csn->cdn", normed_full, d_projected, preferred_element_type=jnp.float32
            )
            out_term = jnp.einsum(
                "sn,sd->nd", mixed, upstream_full, preferred_element_type=jnp.float32
            )
            qkv_sum = qkv_term if qkv_sum is None else qkv_sum + qkv_term
            out_sum = out_term if out_sum is None else out_sum + out_term
        return qkv_sum.astype(jnp.bfloat16), out_sum.astype(jnp.bfloat16)

    def input_grad(layer_in, upstream, d_normed):
        unused_norm, pull_norm = jax.vjp(
            lambda inputs: normalize(inputs, gain_row), layer_in.astype(jnp.float32)
        )
        d_input = pull_norm(d_normed.astype(jnp.float32))[0]
        return (upstream.astype(jnp.float32) + d_input).astype(jnp.bfloat16)

    pair_axes = ("section", "mirror")
    mirror_size = lax.axis_size("mirror")
    up_pairs = []
    down_pairs = []
    for section in range(sections):
        for mirror in range(mirror_size):
            ahead = 1 if mirror == 0 else -1
            if 0 <= section + ahead < sections:
                up_pairs.append((section * mirror_size + mirror, (section + ahead) * mirror_size + mirror))
            if 0 <= section - ahead < sections:
                down_pairs.append((section * mirror_size + mirror, (section - ahead) * mirror_size + mirror))

    bit_count = lax.axis_size(pair_axes).bit_length() - 1
    section_bits = list(range(1, bit_count))
    if section_bits:
        routes = []
        for start in range(len(section_bits)):
            order = section_bits[start:] + section_bits[:start]
            routes.append([1 | (1 << order[0])] + [1 << bit for bit in order[1:]])
    else:
        routes = [[1]]

    def to_partner(value):
        return flipped(value, pair_axes, (1 << bit_count) - 1)

    last_step = window_steps - 1
    saved_normed = [normed_rows(saved[0, 0, t]) for t in range(window_steps)]
    backward_normed_full = [None] * window_steps
    upstream_fulls = []
    d_projecteds = []
    mixeds = []
    partner_normed = [None] * window_steps
    partner_upstream = []
    partner_d_projected = []
    partner_mixed = []
    forward_outs = []
    backward_outs = []
    forward_in = carry_acts[0, 0]
    backward_in = grad_in[0, 0]
    inbox = {}
    deferred = {}
    tie_scatter = {}
    for step_index in range(window_steps):
        embedded = embedding(feats[0, step_index], types[0, step_index], type_table)
        current = jnp.where(position == 0, embedded, forward_in)
        upstream = jnp.where(position == sections - 1, cotangent[0, step_index], backward_in)
        if step_index == 0:
            upstream_full, backward_normed_full[0] = gathered([upstream, saved_normed[0]])
            tie_scatter["first"] = to_partner(jnp.stack([upstream_full, backward_normed_full[0]]))
            forward_rows, upstream_full = lax.optimization_barrier(
                ([normed_rows(current)] + saved_normed[1:], upstream_full)
            )
            forward_normed_full, *later = gathered(forward_rows)
            backward_normed_full[1:] = later
            if later:
                deferred["later"] = jnp.stack(later)
        else:
            upstream_full, forward_normed_full = gathered([upstream, normed_rows(current)])
            inbox[f"rows{step_index}"] = to_partner(upstream_full)
        d_normed_part, d_projected, mixed = backward_part(
            backward_normed_full[step_index], upstream_full, mask_for(1, step_index + position)
        )
        upstream_fulls.append(upstream_full)
        d_projecteds.append(d_projected)
        mixeds.append(mixed)
        small = jnp.concatenate([d_projected, mixed[None]])
        if step_index < last_step:
            deferred[f"small{step_index}"] = small
        else:
            inbox[f"small{step_index}"] = to_partner(small)
        attn_part = forward_part(
            forward_normed_full, mask_for(0, step_index - position + sections - 1)
        )
        (d_normed_part, attn_part), tie_scatter = lax.optimization_barrier(
            ((d_normed_part, attn_part), tie_scatter)
        )
        inbox.update(tie_scatter)
        tie_scatter = {}
        d_normed, attn_rows = scattered([d_normed_part, attn_part])
        backward_out = input_grad(saved[0, 0, step_index], upstream, d_normed)
        forward_out = (current.astype(jnp.float32) + attn_rows.astype(jnp.float32)).astype(
            jnp.bfloat16
        )
        forward_outs.append(forward_out)
        backward_outs.append(backward_out)
        if step_index < last_step:
            backward_in = lax.ppermute(backward_out, pair_axes, down_pairs)
            forward_in = lax.ppermute(forward_out, pair_axes, up_pairs)
            deferred, backward_in, forward_in = lax.optimization_barrier(
                (deferred, backward_in, forward_in)
            )
            tie_scatter = {key: to_partner(value) for key, value in deferred.items()}
            deferred = {}

    partner_upstream = [inbox["first"][0]] + [inbox[f"rows{t}"] for t in range(1, window_steps)]
    partner_normed = [inbox["first"][1]] + (
        [inbox["later"][t] for t in range(window_steps - 1)] if window_steps > 1 else []
    )
    partner_d_projected = [inbox[f"small{t}"][:3] for t in range(window_steps)]
    partner_mixed = [inbox[f"small{t}"][3] for t in range(window_steps)]
    own_qkv, own_out = weight_terms(backward_normed_full, d_projecteds, mixeds, upstream_fulls)
    other_qkv, other_out = weight_terms(
        partner_normed, partner_d_projected, partner_mixed, partner_upstream
    )
    grad_qkv = (own_qkv.astype(jnp.float32) + other_qkv.astype(jnp.float32)).astype(jnp.bfloat16)
    grad_out = (own_out.astype(jnp.float32) + other_out.astype(jnp.float32)).astype(jnp.bfloat16)
    acts_block = jnp.stack(forward_outs)[None, None]
    grads_block = jnp.stack(backward_outs)[None, None]
    return (acts_block, grads_block, grad_qkv[None, None], grad_out[None, None])


def solution(mesh):
    in_specs = (
        P("mirror", None, "tp", None),
        P("mirror", None, "tp"),
        P("mirror", None, None, None),
        P(),
        P("mirror", "section", None),
        P("mirror", "section", None, None, "tp"),
        P("mirror", "section", "tp", None),
        P("mirror", "section", "tp", None),
        P("mirror", "section", "tp", None),
        P("mirror", "section", None, "tp", None),
        P("mirror", None, "tp", None),
    )
    out_specs = (
        P("mirror", "section", None, "tp", None),
        P("mirror", "section", None, "tp", None),
        P("mirror", "section", None, None, "tp"),
        P("mirror", "section", "tp", None),
    )
    return jax.shard_map(shards, mesh=mesh, in_specs=in_specs, out_specs=out_specs, check_vma=False)
```

```python
import math

import numpy as np

import jax
import jax.numpy as jnp
from jax import lax
from jax.sharding import PartitionSpec as P

HD = 128


def passed_along(block, axis, distance):
    devices = range(lax.axis_size(axis))
    route = [(i - distance, i) for i in devices if i - distance in devices]
    return lax.ppermute(block, axis, route)


def flipped(value, axis, mask):
    return lax.ppermute(value, axis, [(i, i ^ mask) for i in range(lax.axis_size(axis))])


def normalize(values, gain_row):
    mean_square = jnp.mean(values * values, axis=-1, keepdims=True)
    return values * lax.rsqrt(mean_square + 1e-05) * gain_row


def segment_mask(segment_ids):
    position = jnp.arange(segment_ids.shape[0], dtype=jnp.int32)
    causal = position[None, :] <= position[:, None]
    return causal & (segment_ids[:, None] == segment_ids[None, :])


def attend(queries, keys_all, values_all, seg_mask):
    scores = jnp.einsum(
        "ihd,jhd->hij", queries, keys_all, preferred_element_type=jnp.float32
    ) / math.sqrt(queries.shape[-1])
    scores = jnp.where(seg_mask[None], scores, -1e30)
    highest = lax.stop_gradient(jnp.max(scores, axis=-1, keepdims=True))
    expo = jnp.exp(scores - highest)
    probs = (expo / jnp.sum(expo, axis=-1, keepdims=True)).astype(values_all.dtype)
    return jnp.einsum("hij,jhd->ihd", probs, values_all, preferred_element_type=jnp.float32)


def embedding(feat_rows, type_rows, type_table):
    onehot = (
        type_rows[:, None] == jnp.arange(type_table.shape[0], dtype=jnp.int32)[None, :]
    ).astype(jnp.bfloat16)
    looked = jnp.dot(onehot, type_table, preferred_element_type=jnp.float32)
    return (feat_rows.astype(jnp.float32) + looked).astype(jnp.bfloat16)


def gathered(blocks):
    full = lax.all_gather(jnp.stack(blocks), "tp", axis=1, tiled=True)
    return [full[i] for i in range(len(blocks))]


def scattered(blocks):
    part = lax.psum_scatter(jnp.stack(blocks), "tp", scatter_dimension=1, tiled=True)
    return [part[i] for i in range(len(blocks))]


def shards(
    feats, types, segs, type_table, gains, w_qkv, w_out, carry_acts, grad_in, saved, cotangent
):
    sections = lax.axis_size("section")
    section_index = lax.axis_index("section")
    on_first_pipe = lax.axis_index("mirror") == 0
    position = jnp.where(on_first_pipe, section_index, sections - 1 - section_index)
    gain_row = gains[0, 0]
    qkv_weight = w_qkv[0, 0]
    out_weight = w_out[0, 0]
    window_steps = feats.shape[1]
    seq_len = segs.shape[3]
    model_width = qkv_weight.shape[1]
    inner_here = qkv_weight.shape[-1]
    heads_here = inner_here // HD

    def mask_for(which, index):
        return segment_mask(lax.dynamic_index_in_dim(segs[0, which], index, 0, keepdims=False))

    def normed_rows(rows):
        return normalize(rows.astype(jnp.float32), gain_row).astype(jnp.bfloat16)

    def heads_of(normed_full):
        projected = jnp.einsum(
            "sd,cdn->csn", normed_full, qkv_weight, preferred_element_type=jnp.float32
        ).astype(jnp.bfloat16)
        return projected.reshape(3, seq_len, heads_here, HD)

    def forward_part(normed_full, seg_mask):
        heads_view = heads_of(normed_full)
        mixed = (
            attend(heads_view[0], heads_view[1], heads_view[2], seg_mask)
            .reshape(seq_len, inner_here)
            .astype(jnp.bfloat16)
        )
        return jnp.dot(mixed, out_weight, preferred_element_type=jnp.float32).astype(jnp.bfloat16)

    def backward_part(normed_full, upstream_full, seg_mask):
        heads_view = heads_of(normed_full)
        primal, pull_attend = jax.vjp(
            lambda query_part, key_part, value_part: attend(
                query_part, key_part, value_part, seg_mask
            ),
            heads_view[0],
            heads_view[1],
            heads_view[2],
        )
        mixed = primal.reshape(seq_len, inner_here).astype(jnp.bfloat16)
        d_mixed = jnp.einsum(
            "sd,nd->sn", upstream_full, out_weight, preferred_element_type=jnp.float32
        ).astype(jnp.bfloat16)
        pulled = pull_attend(d_mixed.astype(jnp.float32).reshape(seq_len, heads_here, HD))
        d_projected = jnp.stack(pulled).reshape(3, seq_len, inner_here)
        d_normed_part = jnp.einsum(
            "csn,cdn->sd", d_projected, qkv_weight, preferred_element_type=jnp.float32
        ).astype(jnp.bfloat16)
        return d_normed_part, d_projected, mixed

    def weight_terms(normed_fulls, d_projecteds, mixeds, upstream_fulls):
        qkv_sum = None
        out_sum = None
        for normed_full, d_projected, mixed, upstream_full in zip(
            normed_fulls, d_projecteds, mixeds, upstream_fulls
        ):
            qkv_term = jnp.einsum(
                "sd,csn->cdn", normed_full, d_projected, preferred_element_type=jnp.float32
            )
            out_term = jnp.einsum(
                "sn,sd->nd", mixed, upstream_full, preferred_element_type=jnp.float32
            )
            qkv_sum = qkv_term if qkv_sum is None else qkv_sum + qkv_term
            out_sum = out_term if out_sum is None else out_sum + out_term
        return qkv_sum.astype(jnp.bfloat16), out_sum.astype(jnp.bfloat16)

    def input_grad(layer_in, upstream, d_normed):
        unused_norm, pull_norm = jax.vjp(
            lambda inputs: normalize(inputs, gain_row), layer_in.astype(jnp.float32)
        )
        d_input = pull_norm(d_normed.astype(jnp.float32))[0]
        return (upstream.astype(jnp.float32) + d_input).astype(jnp.bfloat16)

    pair_axes = ("section", "mirror")
    mirror_size = lax.axis_size("mirror")
    up_pairs = []
    down_pairs = []
    for section in range(sections):
        for mirror in range(mirror_size):
            ahead = 1 if mirror == 0 else -1
            if 0 <= section + ahead < sections:
                up_pairs.append((section * mirror_size + mirror, (section + ahead) * mirror_size + mirror))
            if 0 <= section - ahead < sections:
                down_pairs.append((section * mirror_size + mirror, (section - ahead) * mirror_size + mirror))

    bit_count = lax.axis_size(pair_axes).bit_length() - 1
    section_bits = list(range(1, bit_count))
    if section_bits:
        routes = []
        for start in range(len(section_bits)):
            order = section_bits[start:] + section_bits[:start]
            routes.append([1 | (1 << order[0])] + [1 << bit for bit in order[1:]])
    else:
        routes = [[1]]

    def to_partner(value):
        return flipped(value, pair_axes, (1 << bit_count) - 1)

    last_step = window_steps - 1
    saved_normed = [normed_rows(saved[0, 0, t]) for t in range(window_steps)]
    backward_normed_full = [None] * window_steps
    upstream_fulls = []
    d_projecteds = []
    mixeds = []
    partner_normed = [None] * window_steps
    partner_upstream = []
    partner_d_projected = []
    partner_mixed = []
    forward_outs = []
    backward_outs = []
    forward_in = carry_acts[0, 0]
    backward_in = grad_in[0, 0]
    inbox = {}
    deferred = {}
    tie_scatter = {}
    for step_index in range(window_steps):
        embedded = embedding(feats[0, step_index], types[0, step_index], type_table)
        current = jnp.where(position == 0, embedded, forward_in)
        upstream = jnp.where(position == sections - 1, cotangent[0, step_index], backward_in)
        if step_index == 0:
            upstream_full, backward_normed_full[0] = gathered([upstream, saved_normed[0]])
            tie_scatter["first"] = to_partner(jnp.stack([upstream_full, backward_normed_full[0]]))
            forward_normed, upstream_full = lax.optimization_barrier(
                (normed_rows(current), upstream_full)
            )
            forward_normed_full = gathered([forward_normed])[0]
        else:
            upstream_full, forward_normed_full = gathered([upstream, normed_rows(current)])
            inbox[f"rows{step_index}"] = to_partner(upstream_full)
        d_normed_part, d_projected, mixed = backward_part(
            backward_normed_full[step_index], upstream_full, mask_for(1, step_index + position)
        )
        upstream_fulls.append(upstream_full)
        d_projecteds.append(d_projected)
        mixeds.append(mixed)
        small = jnp.concatenate([d_projected, mixed[None]])
        if step_index < last_step:
            deferred[f"small{step_index}"] = small
        else:
            inbox[f"small{step_index}"] = to_partner(small)
        attn_part = forward_part(
            forward_normed_full, mask_for(0, step_index - position + sections - 1)
        )
        (d_normed_part, attn_part), tie_scatter = lax.optimization_barrier(
            ((d_normed_part, attn_part), tie_scatter)
        )
        inbox.update(tie_scatter)
        tie_scatter = {}
        d_normed, attn_rows = scattered([d_normed_part, attn_part])
        if step_index == 0 and window_steps > 1:
            later_rows, d_normed = lax.optimization_barrier((saved_normed[1:], d_normed))
            later = gathered(later_rows)
            backward_normed_full[1:] = later
            deferred["later"] = jnp.stack(later)
        backward_out = input_grad(saved[0, 0, step_index], upstream, d_normed)
        forward_out = (current.astype(jnp.float32) + attn_rows.astype(jnp.float32)).astype(
            jnp.bfloat16
        )
        forward_outs.append(forward_out)
        backward_outs.append(backward_out)
        if step_index < last_step:
            backward_in = lax.ppermute(backward_out, pair_axes, down_pairs)
            forward_in = lax.ppermute(forward_out, pair_axes, up_pairs)
            deferred, backward_in, forward_in = lax.optimization_barrier(
                (deferred, backward_in, forward_in)
            )
            tie_scatter = {key: to_partner(value) for key, value in deferred.items()}
            deferred = {}

    partner_upstream = [inbox["first"][0]] + [inbox[f"rows{t}"] for t in range(1, window_steps)]
    partner_normed = [inbox["first"][1]] + (
        [inbox["later"][t] for t in range(window_steps - 1)] if window_steps > 1 else []
    )
    partner_d_projected = [inbox[f"small{t}"][:3] for t in range(window_steps)]
    partner_mixed = [inbox[f"small{t}"][3] for t in range(window_steps)]
    own_qkv, own_out = weight_terms(backward_normed_full, d_projecteds, mixeds, upstream_fulls)
    other_qkv, other_out = weight_terms(
        partner_normed, partner_d_projected, partner_mixed, partner_upstream
    )
    grad_qkv = (own_qkv.astype(jnp.float32) + other_qkv.astype(jnp.float32)).astype(jnp.bfloat16)
    grad_out = (own_out.astype(jnp.float32) + other_out.astype(jnp.float32)).astype(jnp.bfloat16)
    acts_block = jnp.stack(forward_outs)[None, None]
    grads_block = jnp.stack(backward_outs)[None, None]
    return (acts_block, grads_block, grad_qkv[None, None], grad_out[None, None])


def solution(mesh):
    in_specs = (
        P("mirror", None, "tp", None),
        P("mirror", None, "tp"),
        P("mirror", None, None, None),
        P(),
        P("mirror", "section", None),
        P("mirror", "section", None, None, "tp"),
        P("mirror", "section", "tp", None),
        P("mirror", "section", "tp", None),
        P("mirror", "section", "tp", None),
        P("mirror", "section", None, "tp", None),
        P("mirror", None, "tp", None),
    )
    out_specs = (
        P("mirror", "section", None, "tp", None),
        P("mirror", "section", None, "tp", None),
        P("mirror", "section", None, None, "tp"),
        P("mirror", "section", "tp", None),
    )
    return jax.shard_map(shards, mesh=mesh, in_specs=in_specs, out_specs=out_specs, check_vma=False)
```

```python
import math

import numpy as np

import jax
import jax.numpy as jnp
from jax import lax
from jax.sharding import PartitionSpec as P

HD = 128


def passed_along(block, axis, distance):
    devices = range(lax.axis_size(axis))
    route = [(i - distance, i) for i in devices if i - distance in devices]
    return lax.ppermute(block, axis, route)


def flipped(value, axis, mask):
    return lax.ppermute(value, axis, [(i, i ^ mask) for i in range(lax.axis_size(axis))])


def normalize(values, gain_row):
    mean_square = jnp.mean(values * values, axis=-1, keepdims=True)
    return values * lax.rsqrt(mean_square + 1e-05) * gain_row


def segment_mask(segment_ids):
    position = jnp.arange(segment_ids.shape[0], dtype=jnp.int32)
    causal = position[None, :] <= position[:, None]
    return causal & (segment_ids[:, None] == segment_ids[None, :])


def attend(queries, keys_all, values_all, seg_mask):
    scores = jnp.einsum(
        "ihd,jhd->hij", queries, keys_all, preferred_element_type=jnp.float32
    ) / math.sqrt(queries.shape[-1])
    scores = jnp.where(seg_mask[None], scores, -1e30)
    highest = lax.stop_gradient(jnp.max(scores, axis=-1, keepdims=True))
    expo = jnp.exp(scores - highest)
    probs = (expo / jnp.sum(expo, axis=-1, keepdims=True)).astype(values_all.dtype)
    return jnp.einsum("hij,jhd->ihd", probs, values_all, preferred_element_type=jnp.float32)


def embedding(feat_rows, type_rows, type_table):
    onehot = (
        type_rows[:, None] == jnp.arange(type_table.shape[0], dtype=jnp.int32)[None, :]
    ).astype(jnp.bfloat16)
    looked = jnp.dot(onehot, type_table, preferred_element_type=jnp.float32)
    return (feat_rows.astype(jnp.float32) + looked).astype(jnp.bfloat16)


def gathered(blocks):
    full = lax.all_gather(jnp.stack(blocks), "tp", axis=1, tiled=True)
    return [full[i] for i in range(len(blocks))]


def scattered(blocks):
    part = lax.psum_scatter(jnp.stack(blocks), "tp", scatter_dimension=1, tiled=True)
    return [part[i] for i in range(len(blocks))]


def shards(
    feats, types, segs, type_table, gains, w_qkv, w_out, carry_acts, grad_in, saved, cotangent
):
    sections = lax.axis_size("section")
    section_index = lax.axis_index("section")
    on_first_pipe = lax.axis_index("mirror") == 0
    position = jnp.where(on_first_pipe, section_index, sections - 1 - section_index)
    gain_row = gains[0, 0]
    qkv_weight = w_qkv[0, 0]
    out_weight = w_out[0, 0]
    window_steps = feats.shape[1]
    seq_len = segs.shape[3]
    model_width = qkv_weight.shape[1]
    inner_here = qkv_weight.shape[-1]
    heads_here = inner_here // HD

    def mask_for(which, index):
        return segment_mask(lax.dynamic_index_in_dim(segs[0, which], index, 0, keepdims=False))

    def normed_rows(rows):
        return normalize(rows.astype(jnp.float32), gain_row).astype(jnp.bfloat16)

    def heads_of(normed_full):
        projected = jnp.einsum(
            "sd,cdn->csn", normed_full, qkv_weight, preferred_element_type=jnp.float32
        ).astype(jnp.bfloat16)
        return projected.reshape(3, seq_len, heads_here, HD)

    def forward_part(normed_full, seg_mask):
        heads_view = heads_of(normed_full)
        mixed = (
            attend(heads_view[0], heads_view[1], heads_view[2], seg_mask)
            .reshape(seq_len, inner_here)
            .astype(jnp.bfloat16)
        )
        return jnp.dot(mixed, out_weight, preferred_element_type=jnp.float32).astype(jnp.bfloat16)

    def backward_part(normed_full, upstream_full, seg_mask):
        heads_view = heads_of(normed_full)
        primal, pull_attend = jax.vjp(
            lambda query_part, key_part, value_part: attend(
                query_part, key_part, value_part, seg_mask
            ),
            heads_view[0],
            heads_view[1],
            heads_view[2],
        )
        mixed = primal.reshape(seq_len, inner_here).astype(jnp.bfloat16)
        d_mixed = jnp.einsum(
            "sd,nd->sn", upstream_full, out_weight, preferred_element_type=jnp.float32
        ).astype(jnp.bfloat16)
        pulled = pull_attend(d_mixed.astype(jnp.float32).reshape(seq_len, heads_here, HD))
        d_projected = jnp.stack(pulled).reshape(3, seq_len, inner_here)
        d_normed_part = jnp.einsum(
            "csn,cdn->sd", d_projected, qkv_weight, preferred_element_type=jnp.float32
        ).astype(jnp.bfloat16)
        return d_normed_part, d_projected, mixed

    def weight_terms(normed_fulls, d_projecteds, mixeds, upstream_fulls):
        qkv_sum = None
        out_sum = None
        for normed_full, d_projected, mixed, upstream_full in zip(
            normed_fulls, d_projecteds, mixeds, upstream_fulls
        ):
            qkv_term = jnp.einsum(
                "sd,csn->cdn", normed_full, d_projected, preferred_element_type=jnp.float32
            )
            out_term = jnp.einsum(
                "sn,sd->nd", mixed, upstream_full, preferred_element_type=jnp.float32
            )
            qkv_sum = qkv_term if qkv_sum is None else qkv_sum + qkv_term
            out_sum = out_term if out_sum is None else out_sum + out_term
        return qkv_sum.astype(jnp.bfloat16), out_sum.astype(jnp.bfloat16)

    def input_grad(layer_in, upstream, d_normed):
        unused_norm, pull_norm = jax.vjp(
            lambda inputs: normalize(inputs, gain_row), layer_in.astype(jnp.float32)
        )
        d_input = pull_norm(d_normed.astype(jnp.float32))[0]
        return (upstream.astype(jnp.float32) + d_input).astype(jnp.bfloat16)

    pair_axes = ("section", "mirror")
    mirror_size = lax.axis_size("mirror")
    up_pairs = []
    down_pairs = []
    for section in range(sections):
        for mirror in range(mirror_size):
            ahead = 1 if mirror == 0 else -1
            if 0 <= section + ahead < sections:
                up_pairs.append((section * mirror_size + mirror, (section + ahead) * mirror_size + mirror))
            if 0 <= section - ahead < sections:
                down_pairs.append((section * mirror_size + mirror, (section - ahead) * mirror_size + mirror))

    bit_count = lax.axis_size(pair_axes).bit_length() - 1
    section_bits = list(range(1, bit_count))
    if section_bits:
        routes = []
        for start in range(len(section_bits)):
            order = section_bits[start:] + section_bits[:start]
            routes.append([1 | (1 << order[0])] + [1 << bit for bit in order[1:]])
    else:
        routes = [[1]]

    def to_partner(value):
        return flipped(value, pair_axes, (1 << bit_count) - 1)

    last_step = window_steps - 1
    saved_normed = [normed_rows(saved[0, 0, t]) for t in range(window_steps)]
    backward_normed_full = [None] * window_steps
    upstream_fulls = []
    d_projecteds = []
    mixeds = []
    partner_normed = [None] * window_steps
    partner_upstream = []
    partner_d_projected = []
    partner_mixed = []
    forward_outs = []
    backward_outs = []
    forward_in = carry_acts[0, 0]
    backward_in = grad_in[0, 0]
    inbox = {}
    deferred = {}
    tie_scatter = {}
    for step_index in range(window_steps):
        embedded = embedding(feats[0, step_index], types[0, step_index], type_table)
        current = jnp.where(position == 0, embedded, forward_in)
        upstream = jnp.where(position == sections - 1, cotangent[0, step_index], backward_in)
        if step_index == 0:
            upstream_full, backward_normed_full[0] = gathered([upstream, saved_normed[0]])
            first_sent = to_partner(jnp.stack([upstream_full, backward_normed_full[0]]))
            forward_normed, upstream_full = lax.optimization_barrier(
                (normed_rows(current), upstream_full)
            )
            forward_normed_full = gathered([forward_normed])[0]
        else:
            upstream_full, forward_normed_full = gathered([upstream, normed_rows(current)])
            inbox[f"rows{step_index}"] = to_partner(upstream_full)
        d_normed_part, d_projected, mixed = backward_part(
            backward_normed_full[step_index], upstream_full, mask_for(1, step_index + position)
        )
        upstream_fulls.append(upstream_full)
        d_projecteds.append(d_projected)
        mixeds.append(mixed)
        small = jnp.concatenate([d_projected, mixed[None]])
        if step_index < last_step:
            deferred[f"small{step_index}"] = small
        else:
            inbox[f"small{step_index}"] = to_partner(small)
        attn_part = forward_part(
            forward_normed_full, mask_for(0, step_index - position + sections - 1)
        )
        (d_normed_part, attn_part), tie_scatter = lax.optimization_barrier(
            ((d_normed_part, attn_part), tie_scatter)
        )
        inbox.update(tie_scatter)
        tie_scatter = {}
        d_normed, attn_rows = scattered([d_normed_part, attn_part])
        if step_index == 0 and window_steps > 1:
            later_rows, d_normed = lax.optimization_barrier((saved_normed[1:], d_normed))
            later = gathered(later_rows)
            backward_normed_full[1:] = later
            deferred["later"] = jnp.stack(later)
        backward_out = input_grad(saved[0, 0, step_index], upstream, d_normed)
        forward_out = (current.astype(jnp.float32) + attn_rows.astype(jnp.float32)).astype(
            jnp.bfloat16
        )
        forward_outs.append(forward_out)
        backward_outs.append(backward_out)
        if step_index < last_step:
            backward_in = lax.ppermute(backward_out, pair_axes, down_pairs)
            forward_in = lax.ppermute(forward_out, pair_axes, up_pairs)
            if step_index == 0:
                deferred, first_sent, backward_in, forward_in = lax.optimization_barrier(
                    (deferred, first_sent, backward_in, forward_in)
                )
                inbox["first"] = first_sent
            else:
                deferred, backward_in, forward_in = lax.optimization_barrier(
                    (deferred, backward_in, forward_in)
                )
            tie_scatter = {key: to_partner(value) for key, value in deferred.items()}
            deferred = {}

    partner_upstream = [inbox["first"][0]] + [inbox[f"rows{t}"] for t in range(1, window_steps)]
    partner_normed = [inbox["first"][1]] + (
        [inbox["later"][t] for t in range(window_steps - 1)] if window_steps > 1 else []
    )
    partner_d_projected = [inbox[f"small{t}"][:3] for t in range(window_steps)]
    partner_mixed = [inbox[f"small{t}"][3] for t in range(window_steps)]
    own_qkv, own_out = weight_terms(backward_normed_full, d_projecteds, mixeds, upstream_fulls)
    other_qkv, other_out = weight_terms(
        partner_normed, partner_d_projected, partner_mixed, partner_upstream
    )
    grad_qkv = (own_qkv.astype(jnp.float32) + other_qkv.astype(jnp.float32)).astype(jnp.bfloat16)
    grad_out = (own_out.astype(jnp.float32) + other_out.astype(jnp.float32)).astype(jnp.bfloat16)
    acts_block = jnp.stack(forward_outs)[None, None]
    grads_block = jnp.stack(backward_outs)[None, None]
    return (acts_block, grads_block, grad_qkv[None, None], grad_out[None, None])


def solution(mesh):
    in_specs = (
        P("mirror", None, "tp", None),
        P("mirror", None, "tp"),
        P("mirror", None, None, None),
        P(),
        P("mirror", "section", None),
        P("mirror", "section", None, None, "tp"),
        P("mirror", "section", "tp", None),
        P("mirror", "section", "tp", None),
        P("mirror", "section", "tp", None),
        P("mirror", "section", None, "tp", None),
        P("mirror", None, "tp", None),
    )
    out_specs = (
        P("mirror", "section", None, "tp", None),
        P("mirror", "section", None, "tp", None),
        P("mirror", "section", None, None, "tp"),
        P("mirror", "section", "tp", None),
    )
    return jax.shard_map(shards, mesh=mesh, in_specs=in_specs, out_specs=out_specs, check_vma=False)
```

```python
import math

import numpy as np

import jax
import jax.numpy as jnp
from jax import lax
from jax.sharding import PartitionSpec as P

HD = 128


def passed_along(block, axis, distance):
    devices = range(lax.axis_size(axis))
    route = [(i - distance, i) for i in devices if i - distance in devices]
    return lax.ppermute(block, axis, route)


def flipped(value, axis, mask):
    return lax.ppermute(value, axis, [(i, i ^ mask) for i in range(lax.axis_size(axis))])


def normalize(values, gain_row):
    mean_square = jnp.mean(values * values, axis=-1, keepdims=True)
    return values * lax.rsqrt(mean_square + 1e-05) * gain_row


def segment_mask(segment_ids):
    position = jnp.arange(segment_ids.shape[0], dtype=jnp.int32)
    causal = position[None, :] <= position[:, None]
    return causal & (segment_ids[:, None] == segment_ids[None, :])


def attend(queries, keys_all, values_all, seg_mask):
    scores = jnp.einsum(
        "ihd,jhd->hij", queries, keys_all, preferred_element_type=jnp.float32
    ) / math.sqrt(queries.shape[-1])
    scores = jnp.where(seg_mask[None], scores, -1e30)
    highest = lax.stop_gradient(jnp.max(scores, axis=-1, keepdims=True))
    expo = jnp.exp(scores - highest)
    probs = (expo / jnp.sum(expo, axis=-1, keepdims=True)).astype(values_all.dtype)
    return jnp.einsum("hij,jhd->ihd", probs, values_all, preferred_element_type=jnp.float32)


def embedding(feat_rows, type_rows, type_table):
    onehot = (
        type_rows[:, None] == jnp.arange(type_table.shape[0], dtype=jnp.int32)[None, :]
    ).astype(jnp.bfloat16)
    looked = jnp.dot(onehot, type_table, preferred_element_type=jnp.float32)
    return (feat_rows.astype(jnp.float32) + looked).astype(jnp.bfloat16)


def gathered(blocks):
    full = lax.all_gather(jnp.stack(blocks), "tp", axis=1, tiled=True)
    return [full[i] for i in range(len(blocks))]


def scattered(blocks):
    part = lax.psum_scatter(jnp.stack(blocks), "tp", scatter_dimension=1, tiled=True)
    return [part[i] for i in range(len(blocks))]


def shards(
    feats, types, segs, type_table, gains, w_qkv, w_out, carry_acts, grad_in, saved, cotangent
):
    sections = lax.axis_size("section")
    section_index = lax.axis_index("section")
    on_first_pipe = lax.axis_index("mirror") == 0
    position = jnp.where(on_first_pipe, section_index, sections - 1 - section_index)
    gain_row = gains[0, 0]
    qkv_weight = w_qkv[0, 0]
    out_weight = w_out[0, 0]
    window_steps = feats.shape[1]
    seq_len = segs.shape[3]
    model_width = qkv_weight.shape[1]
    inner_here = qkv_weight.shape[-1]
    heads_here = inner_here // HD

    def mask_for(which, index):
        return segment_mask(lax.dynamic_index_in_dim(segs[0, which], index, 0, keepdims=False))

    def normed_rows(rows):
        return normalize(rows.astype(jnp.float32), gain_row).astype(jnp.bfloat16)

    def heads_of(normed_full):
        projected = jnp.einsum(
            "sd,cdn->csn", normed_full, qkv_weight, preferred_element_type=jnp.float32
        ).astype(jnp.bfloat16)
        return projected.reshape(3, seq_len, heads_here, HD)

    def forward_part(normed_full, seg_mask):
        heads_view = heads_of(normed_full)
        mixed = (
            attend(heads_view[0], heads_view[1], heads_view[2], seg_mask)
            .reshape(seq_len, inner_here)
            .astype(jnp.bfloat16)
        )
        return jnp.dot(mixed, out_weight, preferred_element_type=jnp.float32).astype(jnp.bfloat16)

    def backward_part(normed_full, upstream_full, seg_mask):
        heads_view = heads_of(normed_full)
        primal, pull_attend = jax.vjp(
            lambda query_part, key_part, value_part: attend(
                query_part, key_part, value_part, seg_mask
            ),
            heads_view[0],
            heads_view[1],
            heads_view[2],
        )
        mixed = primal.reshape(seq_len, inner_here).astype(jnp.bfloat16)
        d_mixed = jnp.einsum(
            "sd,nd->sn", upstream_full, out_weight, preferred_element_type=jnp.float32
        ).astype(jnp.bfloat16)
        pulled = pull_attend(d_mixed.astype(jnp.float32).reshape(seq_len, heads_here, HD))
        d_projected = jnp.stack(pulled).reshape(3, seq_len, inner_here)
        d_normed_part = jnp.einsum(
            "csn,cdn->sd", d_projected, qkv_weight, preferred_element_type=jnp.float32
        ).astype(jnp.bfloat16)
        return d_normed_part, d_projected, mixed

    def weight_terms(normed_fulls, d_projecteds, mixeds, upstream_fulls):
        qkv_sum = None
        out_sum = None
        for normed_full, d_projected, mixed, upstream_full in zip(
            normed_fulls, d_projecteds, mixeds, upstream_fulls
        ):
            qkv_term = jnp.einsum(
                "sd,csn->cdn", normed_full, d_projected, preferred_element_type=jnp.float32
            )
            out_term = jnp.einsum(
                "sn,sd->nd", mixed, upstream_full, preferred_element_type=jnp.float32
            )
            qkv_sum = qkv_term if qkv_sum is None else qkv_sum + qkv_term
            out_sum = out_term if out_sum is None else out_sum + out_term
        return qkv_sum.astype(jnp.bfloat16), out_sum.astype(jnp.bfloat16)

    def input_grad(layer_in, upstream, d_normed):
        unused_norm, pull_norm = jax.vjp(
            lambda inputs: normalize(inputs, gain_row), layer_in.astype(jnp.float32)
        )
        d_input = pull_norm(d_normed.astype(jnp.float32))[0]
        return (upstream.astype(jnp.float32) + d_input).astype(jnp.bfloat16)

    pair_axes = ("section", "mirror")
    mirror_size = lax.axis_size("mirror")
    up_pairs = []
    down_pairs = []
    for section in range(sections):
        for mirror in range(mirror_size):
            ahead = 1 if mirror == 0 else -1
            if 0 <= section + ahead < sections:
                up_pairs.append((section * mirror_size + mirror, (section + ahead) * mirror_size + mirror))
            if 0 <= section - ahead < sections:
                down_pairs.append((section * mirror_size + mirror, (section - ahead) * mirror_size + mirror))

    bit_count = lax.axis_size(pair_axes).bit_length() - 1
    section_bits = list(range(1, bit_count))
    if section_bits:
        routes = []
        for start in range(len(section_bits)):
            order = section_bits[start:] + section_bits[:start]
            routes.append([1 | (1 << order[0])] + [1 << bit for bit in order[1:]])
    else:
        routes = [[1]]

    def to_partner(value):
        return flipped(value, pair_axes, (1 << bit_count) - 1)

    last_step = window_steps - 1
    saved_rows = [saved[0, 0, t] for t in range(window_steps)]
    backward_normed_full = [None] * window_steps
    upstream_fulls = []
    d_projecteds = []
    mixeds = []
    partner_normed = [None] * window_steps
    partner_upstream = []
    partner_d_projected = []
    partner_mixed = []
    forward_outs = []
    backward_outs = []
    forward_in = carry_acts[0, 0]
    backward_in = grad_in[0, 0]
    inbox = {}
    deferred = {}
    tie_scatter = {}
    for step_index in range(window_steps):
        embedded = embedding(feats[0, step_index], types[0, step_index], type_table)
        current = jnp.where(position == 0, embedded, forward_in)
        upstream = jnp.where(position == sections - 1, cotangent[0, step_index], backward_in)
        if step_index == 0:
            upstream_full, saved_full = gathered([upstream, saved_rows[0]])
            backward_normed_full[0] = normed_rows(saved_full)
            first_sent = to_partner(jnp.stack([upstream_full, backward_normed_full[0]]))
            forward_normed, upstream_full = lax.optimization_barrier(
                (normed_rows(current), upstream_full)
            )
            forward_normed_full = gathered([forward_normed])[0]
        else:
            upstream_full, forward_normed_full = gathered([upstream, normed_rows(current)])
            inbox[f"rows{step_index}"] = to_partner(upstream_full)
        d_normed_part, d_projected, mixed = backward_part(
            backward_normed_full[step_index], upstream_full, mask_for(1, step_index + position)
        )
        upstream_fulls.append(upstream_full)
        d_projecteds.append(d_projected)
        mixeds.append(mixed)
        small = jnp.concatenate([d_projected, mixed[None]])
        if step_index < last_step:
            deferred[f"small{step_index}"] = small
        else:
            inbox[f"small{step_index}"] = to_partner(small)
        attn_part = forward_part(
            forward_normed_full, mask_for(0, step_index - position + sections - 1)
        )
        (d_normed_part, attn_part), tie_scatter = lax.optimization_barrier(
            ((d_normed_part, attn_part), tie_scatter)
        )
        inbox.update(tie_scatter)
        tie_scatter = {}
        d_normed, attn_rows = scattered([d_normed_part, attn_part])
        if step_index == 0 and window_steps > 1:
            later_rows, d_normed = lax.optimization_barrier((saved_rows[1:], d_normed))
            later = [normed_rows(rows) for rows in gathered(later_rows)]
            backward_normed_full[1:] = later
            deferred["later"] = jnp.stack(later)
        backward_out = input_grad(saved[0, 0, step_index], upstream, d_normed)
        forward_out = (current.astype(jnp.float32) + attn_rows.astype(jnp.float32)).astype(
            jnp.bfloat16
        )
        forward_outs.append(forward_out)
        backward_outs.append(backward_out)
        if step_index < last_step:
            backward_in = lax.ppermute(backward_out, pair_axes, down_pairs)
            forward_in = lax.ppermute(forward_out, pair_axes, up_pairs)
            if step_index == 0:
                deferred, first_sent, backward_in, forward_in = lax.optimization_barrier(
                    (deferred, first_sent, backward_in, forward_in)
                )
                inbox["first"] = first_sent
            else:
                deferred, backward_in, forward_in = lax.optimization_barrier(
                    (deferred, backward_in, forward_in)
                )
            tie_scatter = {key: to_partner(value) for key, value in deferred.items()}
            deferred = {}

    partner_upstream = [inbox["first"][0]] + [inbox[f"rows{t}"] for t in range(1, window_steps)]
    partner_normed = [inbox["first"][1]] + (
        [inbox["later"][t] for t in range(window_steps - 1)] if window_steps > 1 else []
    )
    partner_d_projected = [inbox[f"small{t}"][:3] for t in range(window_steps)]
    partner_mixed = [inbox[f"small{t}"][3] for t in range(window_steps)]
    own_qkv, own_out = weight_terms(backward_normed_full, d_projecteds, mixeds, upstream_fulls)
    other_qkv, other_out = weight_terms(
        partner_normed, partner_d_projected, partner_mixed, partner_upstream
    )
    grad_qkv = (own_qkv.astype(jnp.float32) + other_qkv.astype(jnp.float32)).astype(jnp.bfloat16)
    grad_out = (own_out.astype(jnp.float32) + other_out.astype(jnp.float32)).astype(jnp.bfloat16)
    acts_block = jnp.stack(forward_outs)[None, None]
    grads_block = jnp.stack(backward_outs)[None, None]
    return (acts_block, grads_block, grad_qkv[None, None], grad_out[None, None])


def solution(mesh):
    in_specs = (
        P("mirror", None, "tp", None),
        P("mirror", None, "tp"),
        P("mirror", None, None, None),
        P(),
        P("mirror", "section", None),
        P("mirror", "section", None, None, "tp"),
        P("mirror", "section", "tp", None),
        P("mirror", "section", "tp", None),
        P("mirror", "section", "tp", None),
        P("mirror", "section", None, "tp", None),
        P("mirror", None, "tp", None),
    )
    out_specs = (
        P("mirror", "section", None, "tp", None),
        P("mirror", "section", None, "tp", None),
        P("mirror", "section", None, None, "tp"),
        P("mirror", "section", "tp", None),
    )
    return jax.shard_map(shards, mesh=mesh, in_specs=in_specs, out_specs=out_specs, check_vma=False)
```

```python
import math

import numpy as np

import jax
import jax.numpy as jnp
from jax import lax
from jax.sharding import PartitionSpec as P

HD = 128


def passed_along(block, axis, distance):
    devices = range(lax.axis_size(axis))
    route = [(i - distance, i) for i in devices if i - distance in devices]
    return lax.ppermute(block, axis, route)


def flipped(value, axis, mask):
    return lax.ppermute(value, axis, [(i, i ^ mask) for i in range(lax.axis_size(axis))])


def normalize(values, gain_row):
    mean_square = jnp.mean(values * values, axis=-1, keepdims=True)
    return values * lax.rsqrt(mean_square + 1e-05) * gain_row


def segment_mask(segment_ids):
    position = jnp.arange(segment_ids.shape[0], dtype=jnp.int32)
    causal = position[None, :] <= position[:, None]
    return causal & (segment_ids[:, None] == segment_ids[None, :])


def attend(queries, keys_all, values_all, seg_mask):
    scores = jnp.einsum(
        "ihd,jhd->hij", queries, keys_all, preferred_element_type=jnp.float32
    ) / math.sqrt(queries.shape[-1])
    scores = jnp.where(seg_mask[None], scores, -1e30)
    highest = lax.stop_gradient(jnp.max(scores, axis=-1, keepdims=True))
    expo = jnp.exp(scores - highest)
    probs = (expo / jnp.sum(expo, axis=-1, keepdims=True)).astype(values_all.dtype)
    return jnp.einsum("hij,jhd->ihd", probs, values_all, preferred_element_type=jnp.float32)


def embedding(feat_rows, type_rows, type_table):
    onehot = (
        type_rows[:, None] == jnp.arange(type_table.shape[0], dtype=jnp.int32)[None, :]
    ).astype(jnp.bfloat16)
    looked = jnp.dot(onehot, type_table, preferred_element_type=jnp.float32)
    return (feat_rows.astype(jnp.float32) + looked).astype(jnp.bfloat16)


def gathered(blocks):
    full = lax.all_gather(jnp.stack(blocks), "tp", axis=1, tiled=True)
    return [full[i] for i in range(len(blocks))]


def scattered(blocks):
    part = lax.psum_scatter(jnp.stack(blocks), "tp", scatter_dimension=1, tiled=True)
    return [part[i] for i in range(len(blocks))]


def shards(
    feats, types, segs, type_table, gains, w_qkv, w_out, carry_acts, grad_in, saved, cotangent
):
    sections = lax.axis_size("section")
    section_index = lax.axis_index("section")
    on_first_pipe = lax.axis_index("mirror") == 0
    position = jnp.where(on_first_pipe, section_index, sections - 1 - section_index)
    gain_row = gains[0, 0]
    qkv_weight = w_qkv[0, 0]
    out_weight = w_out[0, 0]
    window_steps = feats.shape[1]
    seq_len = segs.shape[3]
    model_width = qkv_weight.shape[1]
    inner_here = qkv_weight.shape[-1]
    heads_here = inner_here // HD

    def mask_for(which, index):
        return segment_mask(lax.dynamic_index_in_dim(segs[0, which], index, 0, keepdims=False))

    def normed_rows(rows):
        return normalize(rows.astype(jnp.float32), gain_row).astype(jnp.bfloat16)

    def heads_of(normed_full):
        projected = jnp.einsum(
            "sd,cdn->csn", normed_full, qkv_weight, preferred_element_type=jnp.float32
        ).astype(jnp.bfloat16)
        return projected.reshape(3, seq_len, heads_here, HD)

    def forward_part(normed_full, seg_mask):
        heads_view = heads_of(normed_full)
        mixed = (
            attend(heads_view[0], heads_view[1], heads_view[2], seg_mask)
            .reshape(seq_len, inner_here)
            .astype(jnp.bfloat16)
        )
        return mixed

    def backward_part(normed_full, upstream_full, seg_mask):
        heads_view = heads_of(normed_full)
        primal, pull_attend = jax.vjp(
            lambda query_part, key_part, value_part: attend(
                query_part, key_part, value_part, seg_mask
            ),
            heads_view[0],
            heads_view[1],
            heads_view[2],
        )
        mixed = primal.reshape(seq_len, inner_here).astype(jnp.bfloat16)
        d_mixed = jnp.einsum(
            "sd,nd->sn", upstream_full, out_weight, preferred_element_type=jnp.float32
        ).astype(jnp.bfloat16)
        pulled = pull_attend(d_mixed.astype(jnp.float32).reshape(seq_len, heads_here, HD))
        d_projected = jnp.stack(pulled).reshape(3, seq_len, inner_here)
        return d_projected, mixed

    qkv_rows = jnp.transpose(qkv_weight, (0, 2, 1)).reshape(3 * inner_here, model_width)
    block_weight = jnp.concatenate(
        [
            jnp.stack([qkv_rows, jnp.zeros_like(qkv_rows)], axis=1),
            jnp.stack([jnp.zeros_like(out_weight), out_weight], axis=1),
        ],
        axis=0,
    )

    def projected_back(d_projected, forward_mixed):
        lhs = jnp.concatenate(
            [jnp.transpose(d_projected, (1, 0, 2)).reshape(seq_len, 3 * inner_here), forward_mixed],
            axis=1,
        )
        return jnp.einsum(
            "sk,ktd->tsd", lhs, block_weight, preferred_element_type=jnp.float32
        ).astype(jnp.bfloat16)

    def weight_terms(normed_fulls, d_projecteds, mixeds, upstream_fulls):
        qkv_sum = None
        out_sum = None
        for normed_full, d_projected, mixed, upstream_full in zip(
            normed_fulls, d_projecteds, mixeds, upstream_fulls
        ):
            qkv_term = jnp.einsum(
                "sd,csn->cdn", normed_full, d_projected, preferred_element_type=jnp.float32
            )
            out_term = jnp.einsum(
                "sn,sd->nd", mixed, upstream_full, preferred_element_type=jnp.float32
            )
            qkv_sum = qkv_term if qkv_sum is None else qkv_sum + qkv_term
            out_sum = out_term if out_sum is None else out_sum + out_term
        return qkv_sum.astype(jnp.bfloat16), out_sum.astype(jnp.bfloat16)

    def input_grad(layer_in, upstream, d_normed):
        unused_norm, pull_norm = jax.vjp(
            lambda inputs: normalize(inputs, gain_row), layer_in.astype(jnp.float32)
        )
        d_input = pull_norm(d_normed.astype(jnp.float32))[0]
        return (upstream.astype(jnp.float32) + d_input).astype(jnp.bfloat16)

    pair_axes = ("section", "mirror")
    mirror_size = lax.axis_size("mirror")
    up_pairs = []
    down_pairs = []
    for section in range(sections):
        for mirror in range(mirror_size):
            ahead = 1 if mirror == 0 else -1
            if 0 <= section + ahead < sections:
                up_pairs.append((section * mirror_size + mirror, (section + ahead) * mirror_size + mirror))
            if 0 <= section - ahead < sections:
                down_pairs.append((section * mirror_size + mirror, (section - ahead) * mirror_size + mirror))

    bit_count = lax.axis_size(pair_axes).bit_length() - 1
    section_bits = list(range(1, bit_count))
    if section_bits:
        routes = []
        for start in range(len(section_bits)):
            order = section_bits[start:] + section_bits[:start]
            routes.append([1 | (1 << order[0])] + [1 << bit for bit in order[1:]])
    else:
        routes = [[1]]

    def to_partner(value):
        return flipped(value, pair_axes, (1 << bit_count) - 1)

    last_step = window_steps - 1
    saved_normed = [normed_rows(saved[0, 0, t]) for t in range(window_steps)]
    backward_normed_full = [None] * window_steps
    upstream_fulls = []
    d_projecteds = []
    mixeds = []
    partner_normed = [None] * window_steps
    partner_upstream = []
    partner_d_projected = []
    partner_mixed = []
    forward_outs = []
    backward_outs = []
    forward_in = carry_acts[0, 0]
    backward_in = grad_in[0, 0]
    inbox = {}
    deferred = {}
    tie_scatter = {}
    for step_index in range(window_steps):
        embedded = embedding(feats[0, step_index], types[0, step_index], type_table)
        current = jnp.where(position == 0, embedded, forward_in)
        upstream = jnp.where(position == sections - 1, cotangent[0, step_index], backward_in)
        if step_index == 0:
            upstream_full, backward_normed_full[0] = gathered([upstream, saved_normed[0]])
            first_sent = to_partner(jnp.stack([upstream_full, backward_normed_full[0]]))
            forward_normed, upstream_full = lax.optimization_barrier(
                (normed_rows(current), upstream_full)
            )
            forward_normed_full = gathered([forward_normed])[0]
        else:
            upstream_full, forward_normed_full = gathered([upstream, normed_rows(current)])
            inbox[f"rows{step_index}"] = to_partner(upstream_full)
        d_projected, mixed = backward_part(
            backward_normed_full[step_index], upstream_full, mask_for(1, step_index + position)
        )
        upstream_fulls.append(upstream_full)
        d_projecteds.append(d_projected)
        mixeds.append(mixed)
        small = jnp.concatenate([d_projected, mixed[None]])
        if step_index < last_step:
            deferred[f"small{step_index}"] = small
        else:
            inbox[f"small{step_index}"] = to_partner(small)
        forward_mixed = forward_part(
            forward_normed_full, mask_for(0, step_index - position + sections - 1)
        )
        both_parts, tie_scatter = lax.optimization_barrier(
            (projected_back(d_projected, forward_mixed), tie_scatter)
        )
        inbox.update(tie_scatter)
        tie_scatter = {}
        both_rows = lax.psum_scatter(both_parts, "tp", scatter_dimension=1, tiled=True)
        d_normed, attn_rows = both_rows[0], both_rows[1]
        if step_index == 0 and window_steps > 1:
            later_rows, d_normed = lax.optimization_barrier((saved_normed[1:], d_normed))
            later = gathered(later_rows)
            backward_normed_full[1:] = later
            deferred["later"] = jnp.stack(later)
        backward_out = input_grad(saved[0, 0, step_index], upstream, d_normed)
        forward_out = (current.astype(jnp.float32) + attn_rows.astype(jnp.float32)).astype(
            jnp.bfloat16
        )
        forward_outs.append(forward_out)
        backward_outs.append(backward_out)
        if step_index < last_step:
            backward_in = lax.ppermute(backward_out, pair_axes, down_pairs)
            forward_in = lax.ppermute(forward_out, pair_axes, up_pairs)
            if step_index == 0:
                deferred, first_sent, backward_in, forward_in = lax.optimization_barrier(
                    (deferred, first_sent, backward_in, forward_in)
                )
                inbox["first"] = first_sent
            else:
                deferred, backward_in, forward_in = lax.optimization_barrier(
                    (deferred, backward_in, forward_in)
                )
            tie_scatter = {key: to_partner(value) for key, value in deferred.items()}
            deferred = {}

    partner_upstream = [inbox["first"][0]] + [inbox[f"rows{t}"] for t in range(1, window_steps)]
    partner_normed = [inbox["first"][1]] + (
        [inbox["later"][t] for t in range(window_steps - 1)] if window_steps > 1 else []
    )
    partner_d_projected = [inbox[f"small{t}"][:3] for t in range(window_steps)]
    partner_mixed = [inbox[f"small{t}"][3] for t in range(window_steps)]
    own_qkv, own_out = weight_terms(backward_normed_full, d_projecteds, mixeds, upstream_fulls)
    other_qkv, other_out = weight_terms(
        partner_normed, partner_d_projected, partner_mixed, partner_upstream
    )
    grad_qkv = (own_qkv.astype(jnp.float32) + other_qkv.astype(jnp.float32)).astype(jnp.bfloat16)
    grad_out = (own_out.astype(jnp.float32) + other_out.astype(jnp.float32)).astype(jnp.bfloat16)
    acts_block = jnp.stack(forward_outs)[None, None]
    grads_block = jnp.stack(backward_outs)[None, None]
    return (acts_block, grads_block, grad_qkv[None, None], grad_out[None, None])


def solution(mesh):
    in_specs = (
        P("mirror", None, "tp", None),
        P("mirror", None, "tp"),
        P("mirror", None, None, None),
        P(),
        P("mirror", "section", None),
        P("mirror", "section", None, None, "tp"),
        P("mirror", "section", "tp", None),
        P("mirror", "section", "tp", None),
        P("mirror", "section", "tp", None),
        P("mirror", "section", None, "tp", None),
        P("mirror", None, "tp", None),
    )
    out_specs = (
        P("mirror", "section", None, "tp", None),
        P("mirror", "section", None, "tp", None),
        P("mirror", "section", None, None, "tp"),
        P("mirror", "section", "tp", None),
    )
    return jax.shard_map(shards, mesh=mesh, in_specs=in_specs, out_specs=out_specs, check_vma=False)
```

```python
import math

import numpy as np

import jax
import jax.numpy as jnp
from jax import lax
from jax.sharding import PartitionSpec as P

HD = 128


def passed_along(block, axis, distance):
    devices = range(lax.axis_size(axis))
    route = [(i - distance, i) for i in devices if i - distance in devices]
    return lax.ppermute(block, axis, route)


def flipped(value, axis, mask):
    return lax.ppermute(value, axis, [(i, i ^ mask) for i in range(lax.axis_size(axis))])


def normalize(values, gain_row):
    mean_square = jnp.mean(values * values, axis=-1, keepdims=True)
    return values * lax.rsqrt(mean_square + 1e-05) * gain_row


def segment_mask(segment_ids):
    position = jnp.arange(segment_ids.shape[0], dtype=jnp.int32)
    causal = position[None, :] <= position[:, None]
    return causal & (segment_ids[:, None] == segment_ids[None, :])


def attend(queries, keys_all, values_all, seg_mask):
    scores = jnp.einsum(
        "ihd,jhd->hij", queries, keys_all, preferred_element_type=jnp.float32
    ) / math.sqrt(queries.shape[-1])
    scores = jnp.where(seg_mask[None], scores, -1e30)
    highest = lax.stop_gradient(jnp.max(scores, axis=-1, keepdims=True))
    expo = jnp.exp(scores - highest)
    probs = (expo / jnp.sum(expo, axis=-1, keepdims=True)).astype(values_all.dtype)
    return jnp.einsum("hij,jhd->ihd", probs, values_all, preferred_element_type=jnp.float32)


def embedding(feat_rows, type_rows, type_table):
    onehot = (
        type_rows[:, None] == jnp.arange(type_table.shape[0], dtype=jnp.int32)[None, :]
    ).astype(jnp.bfloat16)
    looked = jnp.dot(onehot, type_table, preferred_element_type=jnp.float32)
    return (feat_rows.astype(jnp.float32) + looked).astype(jnp.bfloat16)


def gathered(blocks):
    full = lax.all_gather(jnp.stack(blocks), "tp", axis=1, tiled=True)
    return [full[i] for i in range(len(blocks))]


def scattered(blocks):
    part = lax.psum_scatter(jnp.stack(blocks), "tp", scatter_dimension=1, tiled=True)
    return [part[i] for i in range(len(blocks))]


def shards(
    feats, types, segs, type_table, gains, w_qkv, w_out, carry_acts, grad_in, saved, cotangent
):
    sections = lax.axis_size("section")
    section_index = lax.axis_index("section")
    on_first_pipe = lax.axis_index("mirror") == 0
    position = jnp.where(on_first_pipe, section_index, sections - 1 - section_index)
    gain_row = gains[0, 0]
    qkv_weight = w_qkv[0, 0]
    out_weight = w_out[0, 0]
    window_steps = feats.shape[1]
    seq_len = segs.shape[3]
    model_width = qkv_weight.shape[1]
    inner_here = qkv_weight.shape[-1]
    heads_here = inner_here // HD

    def mask_for(which, index):
        return segment_mask(lax.dynamic_index_in_dim(segs[0, which], index, 0, keepdims=False))

    def normed_rows(rows):
        return normalize(rows.astype(jnp.float32), gain_row).astype(jnp.bfloat16)

    def heads_of(normed_full):
        projected = jnp.einsum(
            "sd,cdn->csn", normed_full, qkv_weight, preferred_element_type=jnp.float32
        ).astype(jnp.bfloat16)
        return projected.reshape(3, seq_len, heads_here, HD)

    def forward_part(normed_full, seg_mask):
        heads_view = heads_of(normed_full)
        mixed = (
            attend(heads_view[0], heads_view[1], heads_view[2], seg_mask)
            .reshape(seq_len, inner_here)
            .astype(jnp.bfloat16)
        )
        return mixed

    def backward_part(normed_full, upstream_full, seg_mask):
        heads_view = heads_of(normed_full)
        primal, pull_attend = jax.vjp(
            lambda query_part, key_part, value_part: attend(
                query_part, key_part, value_part, seg_mask
            ),
            heads_view[0],
            heads_view[1],
            heads_view[2],
        )
        mixed = primal.reshape(seq_len, inner_here).astype(jnp.bfloat16)
        d_mixed = jnp.einsum(
            "sd,nd->sn", upstream_full, out_weight, preferred_element_type=jnp.float32
        ).astype(jnp.bfloat16)
        pulled = pull_attend(d_mixed.astype(jnp.float32).reshape(seq_len, heads_here, HD))
        d_projected = jnp.stack(pulled).reshape(3, seq_len, inner_here)
        return d_projected, mixed

    qkv_rows = jnp.transpose(qkv_weight, (0, 2, 1)).reshape(3 * inner_here, model_width)
    padded_out = jnp.concatenate(
        [out_weight, jnp.zeros((2 * inner_here, model_width), out_weight.dtype)], axis=0
    )
    block_weight = jnp.stack([qkv_rows, padded_out])

    def projected_back(d_projected, forward_mixed):
        lhs = jnp.stack(
            [
                jnp.transpose(d_projected, (1, 0, 2)).reshape(seq_len, 3 * inner_here),
                jnp.concatenate(
                    [forward_mixed, jnp.zeros((seq_len, 2 * inner_here), forward_mixed.dtype)],
                    axis=1,
                ),
            ]
        )
        return jnp.einsum(
            "tsk,tkd->tsd", lhs, block_weight, preferred_element_type=jnp.float32
        ).astype(jnp.bfloat16)

    def weight_terms(normed_fulls, d_projecteds, mixeds, upstream_fulls):
        qkv_sum = None
        out_sum = None
        for normed_full, d_projected, mixed, upstream_full in zip(
            normed_fulls, d_projecteds, mixeds, upstream_fulls
        ):
            qkv_term = jnp.einsum(
                "sd,csn->cdn", normed_full, d_projected, preferred_element_type=jnp.float32
            )
            out_term = jnp.einsum(
                "sn,sd->nd", mixed, upstream_full, preferred_element_type=jnp.float32
            )
            qkv_sum = qkv_term if qkv_sum is None else qkv_sum + qkv_term
            out_sum = out_term if out_sum is None else out_sum + out_term
        return qkv_sum.astype(jnp.bfloat16), out_sum.astype(jnp.bfloat16)

    def input_grad(layer_in, upstream, d_normed):
        unused_norm, pull_norm = jax.vjp(
            lambda inputs: normalize(inputs, gain_row), layer_in.astype(jnp.float32)
        )
        d_input = pull_norm(d_normed.astype(jnp.float32))[0]
        return (upstream.astype(jnp.float32) + d_input).astype(jnp.bfloat16)

    pair_axes = ("section", "mirror")
    mirror_size = lax.axis_size("mirror")
    up_pairs = []
    down_pairs = []
    for section in range(sections):
        for mirror in range(mirror_size):
            ahead = 1 if mirror == 0 else -1
            if 0 <= section + ahead < sections:
                up_pairs.append((section * mirror_size + mirror, (section + ahead) * mirror_size + mirror))
            if 0 <= section - ahead < sections:
                down_pairs.append((section * mirror_size + mirror, (section - ahead) * mirror_size + mirror))

    bit_count = lax.axis_size(pair_axes).bit_length() - 1
    section_bits = list(range(1, bit_count))
    if section_bits:
        routes = []
        for start in range(len(section_bits)):
            order = section_bits[start:] + section_bits[:start]
            routes.append([1 | (1 << order[0])] + [1 << bit for bit in order[1:]])
    else:
        routes = [[1]]

    def to_partner(value):
        return flipped(value, pair_axes, (1 << bit_count) - 1)

    last_step = window_steps - 1
    saved_normed = [normed_rows(saved[0, 0, t]) for t in range(window_steps)]
    backward_normed_full = [None] * window_steps
    upstream_fulls = []
    d_projecteds = []
    mixeds = []
    partner_normed = [None] * window_steps
    partner_upstream = []
    partner_d_projected = []
    partner_mixed = []
    forward_outs = []
    backward_outs = []
    forward_in = carry_acts[0, 0]
    backward_in = grad_in[0, 0]
    inbox = {}
    deferred = {}
    tie_scatter = {}
    for step_index in range(window_steps):
        embedded = embedding(feats[0, step_index], types[0, step_index], type_table)
        current = jnp.where(position == 0, embedded, forward_in)
        upstream = jnp.where(position == sections - 1, cotangent[0, step_index], backward_in)
        if step_index == 0:
            upstream_full, backward_normed_full[0] = gathered([upstream, saved_normed[0]])
            first_sent = to_partner(jnp.stack([upstream_full, backward_normed_full[0]]))
            forward_normed, upstream_full = lax.optimization_barrier(
                (normed_rows(current), upstream_full)
            )
            forward_normed_full = gathered([forward_normed])[0]
        else:
            upstream_full, forward_normed_full = gathered([upstream, normed_rows(current)])
            inbox[f"rows{step_index}"] = to_partner(upstream_full)
        d_projected, mixed = backward_part(
            backward_normed_full[step_index], upstream_full, mask_for(1, step_index + position)
        )
        upstream_fulls.append(upstream_full)
        d_projecteds.append(d_projected)
        mixeds.append(mixed)
        small = jnp.concatenate([d_projected, mixed[None]])
        if step_index < last_step:
            deferred[f"small{step_index}"] = small
        else:
            inbox[f"small{step_index}"] = to_partner(small)
        forward_mixed = forward_part(
            forward_normed_full, mask_for(0, step_index - position + sections - 1)
        )
        both_parts, tie_scatter = lax.optimization_barrier(
            (projected_back(d_projected, forward_mixed), tie_scatter)
        )
        inbox.update(tie_scatter)
        tie_scatter = {}
        both_rows = lax.psum_scatter(both_parts, "tp", scatter_dimension=1, tiled=True)
        d_normed, attn_rows = both_rows[0], both_rows[1]
        if step_index == 0 and window_steps > 1:
            later_rows, d_normed = lax.optimization_barrier((saved_normed[1:], d_normed))
            later = gathered(later_rows)
            backward_normed_full[1:] = later
            deferred["later"] = jnp.stack(later)
        backward_out = input_grad(saved[0, 0, step_index], upstream, d_normed)
        forward_out = (current.astype(jnp.float32) + attn_rows.astype(jnp.float32)).astype(
            jnp.bfloat16
        )
        forward_outs.append(forward_out)
        backward_outs.append(backward_out)
        if step_index < last_step:
            backward_in = lax.ppermute(backward_out, pair_axes, down_pairs)
            forward_in = lax.ppermute(forward_out, pair_axes, up_pairs)
            if step_index == 0:
                deferred, first_sent, backward_in, forward_in = lax.optimization_barrier(
                    (deferred, first_sent, backward_in, forward_in)
                )
                inbox["first"] = first_sent
            else:
                deferred, backward_in, forward_in = lax.optimization_barrier(
                    (deferred, backward_in, forward_in)
                )
            tie_scatter = {key: to_partner(value) for key, value in deferred.items()}
            deferred = {}

    partner_upstream = [inbox["first"][0]] + [inbox[f"rows{t}"] for t in range(1, window_steps)]
    partner_normed = [inbox["first"][1]] + (
        [inbox["later"][t] for t in range(window_steps - 1)] if window_steps > 1 else []
    )
    partner_d_projected = [inbox[f"small{t}"][:3] for t in range(window_steps)]
    partner_mixed = [inbox[f"small{t}"][3] for t in range(window_steps)]
    own_qkv, own_out = weight_terms(backward_normed_full, d_projecteds, mixeds, upstream_fulls)
    other_qkv, other_out = weight_terms(
        partner_normed, partner_d_projected, partner_mixed, partner_upstream
    )
    grad_qkv = (own_qkv.astype(jnp.float32) + other_qkv.astype(jnp.float32)).astype(jnp.bfloat16)
    grad_out = (own_out.astype(jnp.float32) + other_out.astype(jnp.float32)).astype(jnp.bfloat16)
    acts_block = jnp.stack(forward_outs)[None, None]
    grads_block = jnp.stack(backward_outs)[None, None]
    return (acts_block, grads_block, grad_qkv[None, None], grad_out[None, None])


def solution(mesh):
    in_specs = (
        P("mirror", None, "tp", None),
        P("mirror", None, "tp"),
        P("mirror", None, None, None),
        P(),
        P("mirror", "section", None),
        P("mirror", "section", None, None, "tp"),
        P("mirror", "section", "tp", None),
        P("mirror", "section", "tp", None),
        P("mirror", "section", "tp", None),
        P("mirror", "section", None, "tp", None),
        P("mirror", None, "tp", None),
    )
    out_specs = (
        P("mirror", "section", None, "tp", None),
        P("mirror", "section", None, "tp", None),
        P("mirror", "section", None, None, "tp"),
        P("mirror", "section", "tp", None),
    )
    return jax.shard_map(shards, mesh=mesh, in_specs=in_specs, out_specs=out_specs, check_vma=False)
```

```python
import math

import numpy as np

import jax
import jax.numpy as jnp
from jax import lax
from jax.sharding import PartitionSpec as P

HD = 128


def passed_along(block, axis, distance):
    devices = range(lax.axis_size(axis))
    route = [(i - distance, i) for i in devices if i - distance in devices]
    return lax.ppermute(block, axis, route)


def flipped(value, axis, mask):
    return lax.ppermute(value, axis, [(i, i ^ mask) for i in range(lax.axis_size(axis))])


def normalize(values, gain_row):
    mean_square = jnp.mean(values * values, axis=-1, keepdims=True)
    return values * lax.rsqrt(mean_square + 1e-05) * gain_row


def segment_mask(segment_ids):
    position = jnp.arange(segment_ids.shape[0], dtype=jnp.int32)
    causal = position[None, :] <= position[:, None]
    return causal & (segment_ids[:, None] == segment_ids[None, :])


def attend(queries, keys_all, values_all, seg_mask):
    scores = jnp.einsum(
        "ihd,jhd->hij", queries, keys_all, preferred_element_type=jnp.float32
    ) / math.sqrt(queries.shape[-1])
    scores = jnp.where(seg_mask[None], scores, -1e30)
    highest = lax.stop_gradient(jnp.max(scores, axis=-1, keepdims=True))
    expo = jnp.exp(scores - highest)
    probs = (expo / jnp.sum(expo, axis=-1, keepdims=True)).astype(values_all.dtype)
    return jnp.einsum("hij,jhd->ihd", probs, values_all, preferred_element_type=jnp.float32)


def embedding(feat_rows, type_rows, type_table):
    onehot = (
        type_rows[:, None] == jnp.arange(type_table.shape[0], dtype=jnp.int32)[None, :]
    ).astype(jnp.bfloat16)
    looked = jnp.dot(onehot, type_table, preferred_element_type=jnp.float32)
    return (feat_rows.astype(jnp.float32) + looked).astype(jnp.bfloat16)


def gathered(blocks):
    full = lax.all_gather(jnp.stack(blocks), "tp", axis=1, tiled=True)
    return [full[i] for i in range(len(blocks))]


def scattered(blocks):
    part = lax.psum_scatter(jnp.stack(blocks), "tp", scatter_dimension=1, tiled=True)
    return [part[i] for i in range(len(blocks))]


def shards(
    feats, types, segs, type_table, gains, w_qkv, w_out, carry_acts, grad_in, saved, cotangent
):
    sections = lax.axis_size("section")
    section_index = lax.axis_index("section")
    on_first_pipe = lax.axis_index("mirror") == 0
    position = jnp.where(on_first_pipe, section_index, sections - 1 - section_index)
    gain_row = gains[0, 0]
    qkv_weight = w_qkv[0, 0]
    out_weight = w_out[0, 0]
    window_steps = feats.shape[1]
    seq_len = segs.shape[3]
    model_width = qkv_weight.shape[1]
    inner_here = qkv_weight.shape[-1]
    heads_here = inner_here // HD

    def mask_for(which, index):
        return segment_mask(lax.dynamic_index_in_dim(segs[0, which], index, 0, keepdims=False))

    def normed_rows(rows):
        return normalize(rows.astype(jnp.float32), gain_row).astype(jnp.bfloat16)

    def heads_of(normed_full):
        projected = jnp.einsum(
            "sd,cdn->csn", normed_full, qkv_weight, preferred_element_type=jnp.float32
        ).astype(jnp.bfloat16)
        return projected.reshape(3, seq_len, heads_here, HD)

    def forward_part(normed_full, seg_mask):
        heads_view = heads_of(normed_full)
        mixed = (
            attend(heads_view[0], heads_view[1], heads_view[2], seg_mask)
            .reshape(seq_len, inner_here)
            .astype(jnp.bfloat16)
        )
        return mixed

    def backward_part(normed_full, upstream_full, seg_mask):
        heads_view = heads_of(normed_full)
        primal, pull_attend = jax.vjp(
            lambda query_part, key_part, value_part: attend(
                query_part, key_part, value_part, seg_mask
            ),
            heads_view[0],
            heads_view[1],
            heads_view[2],
        )
        mixed = primal.reshape(seq_len, inner_here).astype(jnp.bfloat16)
        d_mixed = jnp.einsum(
            "sd,nd->sn", upstream_full, out_weight, preferred_element_type=jnp.float32
        ).astype(jnp.bfloat16)
        pulled = pull_attend(d_mixed.astype(jnp.float32).reshape(seq_len, heads_here, HD))
        d_projected = jnp.stack(pulled).reshape(3, seq_len, inner_here)
        return d_projected, mixed

    qkv_rows = jnp.transpose(qkv_weight, (0, 2, 1)).reshape(3 * inner_here, model_width)
    padded_out = jnp.concatenate(
        [out_weight, jnp.zeros((2 * inner_here, model_width), out_weight.dtype)], axis=0
    )
    block_weight = jnp.stack([qkv_rows, padded_out])

    def projected_back(d_projected, forward_mixed):
        lhs = jnp.stack(
            [
                jnp.transpose(d_projected, (1, 0, 2)).reshape(seq_len, 3 * inner_here),
                jnp.concatenate(
                    [forward_mixed, jnp.zeros((seq_len, 2 * inner_here), forward_mixed.dtype)],
                    axis=1,
                ),
            ]
        )
        return jnp.einsum(
            "tsk,tkd->tsd", lhs, block_weight, preferred_element_type=jnp.float32
        ).astype(jnp.bfloat16)

    def weight_terms(normed_fulls, d_projecteds, mixeds, upstream_fulls):
        qkv_sum = None
        out_sum = None
        for normed_full, d_projected, mixed, upstream_full in zip(
            normed_fulls, d_projecteds, mixeds, upstream_fulls
        ):
            qkv_term = jnp.einsum(
                "sd,csn->cdn", normed_full, d_projected, preferred_element_type=jnp.float32
            )
            out_term = jnp.einsum(
                "sn,sd->nd", mixed, upstream_full, preferred_element_type=jnp.float32
            )
            qkv_sum = qkv_term if qkv_sum is None else qkv_sum + qkv_term
            out_sum = out_term if out_sum is None else out_sum + out_term
        return qkv_sum.astype(jnp.bfloat16), out_sum.astype(jnp.bfloat16)

    def input_grad(layer_in, upstream, d_normed):
        unused_norm, pull_norm = jax.vjp(
            lambda inputs: normalize(inputs, gain_row), layer_in.astype(jnp.float32)
        )
        d_input = pull_norm(d_normed.astype(jnp.float32))[0]
        return (upstream.astype(jnp.float32) + d_input).astype(jnp.bfloat16)

    pair_axes = ("section", "mirror")
    mirror_size = lax.axis_size("mirror")
    up_pairs = []
    down_pairs = []
    for section in range(sections):
        for mirror in range(mirror_size):
            ahead = 1 if mirror == 0 else -1
            if 0 <= section + ahead < sections:
                up_pairs.append((section * mirror_size + mirror, (section + ahead) * mirror_size + mirror))
            if 0 <= section - ahead < sections:
                down_pairs.append((section * mirror_size + mirror, (section - ahead) * mirror_size + mirror))

    bit_count = lax.axis_size(pair_axes).bit_length() - 1
    section_bits = list(range(1, bit_count))
    if section_bits:
        routes = []
        for start in range(len(section_bits)):
            order = section_bits[start:] + section_bits[:start]
            routes.append([1 | (1 << order[0])] + [1 << bit for bit in order[1:]])
    else:
        routes = [[1]]

    def to_partner(value):
        return flipped(value, pair_axes, (1 << bit_count) - 1)

    last_step = window_steps - 1
    saved_normed = [normed_rows(saved[0, 0, t]) for t in range(window_steps)]
    backward_normed_full = [None] * window_steps
    upstream_fulls = []
    d_projecteds = []
    mixeds = []
    partner_normed = [None] * window_steps
    partner_upstream = []
    partner_d_projected = []
    partner_mixed = []
    forward_outs = []
    backward_outs = []
    forward_in = carry_acts[0, 0]
    backward_in = grad_in[0, 0]
    inbox = {}
    deferred = {}
    tie_scatter = {}
    for step_index in range(window_steps):
        embedded = embedding(feats[0, step_index], types[0, step_index], type_table)
        current = jnp.where(position == 0, embedded, forward_in)
        upstream = jnp.where(position == sections - 1, cotangent[0, step_index], backward_in)
        if step_index == 0:
            upstream_full, backward_normed_full[0], forward_normed_full = gathered(
                [upstream, saved_normed[0], normed_rows(current)]
            )
            first_sent = to_partner(jnp.stack([upstream_full, backward_normed_full[0]]))
        else:
            upstream_full, forward_normed_full = gathered([upstream, normed_rows(current)])
            inbox[f"rows{step_index}"] = to_partner(upstream_full)
        d_projected, mixed = backward_part(
            backward_normed_full[step_index], upstream_full, mask_for(1, step_index + position)
        )
        upstream_fulls.append(upstream_full)
        d_projecteds.append(d_projected)
        mixeds.append(mixed)
        small = jnp.concatenate([d_projected, mixed[None]])
        if step_index < last_step:
            deferred[f"small{step_index}"] = small
        else:
            inbox[f"small{step_index}"] = to_partner(small)
        forward_mixed = forward_part(
            forward_normed_full, mask_for(0, step_index - position + sections - 1)
        )
        both_parts, tie_scatter = lax.optimization_barrier(
            (projected_back(d_projected, forward_mixed), tie_scatter)
        )
        inbox.update(tie_scatter)
        tie_scatter = {}
        both_rows = lax.psum_scatter(both_parts, "tp", scatter_dimension=1, tiled=True)
        d_normed, attn_rows = both_rows[0], both_rows[1]
        if step_index == 0 and window_steps > 1:
            later_rows, d_normed = lax.optimization_barrier((saved_normed[1:], d_normed))
            later = gathered(later_rows)
            backward_normed_full[1:] = later
            deferred["later"] = jnp.stack(later)
        backward_out = input_grad(saved[0, 0, step_index], upstream, d_normed)
        forward_out = (current.astype(jnp.float32) + attn_rows.astype(jnp.float32)).astype(
            jnp.bfloat16
        )
        forward_outs.append(forward_out)
        backward_outs.append(backward_out)
        if step_index < last_step:
            backward_in = lax.ppermute(backward_out, pair_axes, down_pairs)
            forward_in = lax.ppermute(forward_out, pair_axes, up_pairs)
            if step_index == 0:
                deferred, first_sent, backward_in, forward_in = lax.optimization_barrier(
                    (deferred, first_sent, backward_in, forward_in)
                )
                inbox["first"] = first_sent
            else:
                deferred, backward_in, forward_in = lax.optimization_barrier(
                    (deferred, backward_in, forward_in)
                )
            tie_scatter = {key: to_partner(value) for key, value in deferred.items()}
            deferred = {}

    partner_upstream = [inbox["first"][0]] + [inbox[f"rows{t}"] for t in range(1, window_steps)]
    partner_normed = [inbox["first"][1]] + (
        [inbox["later"][t] for t in range(window_steps - 1)] if window_steps > 1 else []
    )
    partner_d_projected = [inbox[f"small{t}"][:3] for t in range(window_steps)]
    partner_mixed = [inbox[f"small{t}"][3] for t in range(window_steps)]
    own_qkv, own_out = weight_terms(backward_normed_full, d_projecteds, mixeds, upstream_fulls)
    other_qkv, other_out = weight_terms(
        partner_normed, partner_d_projected, partner_mixed, partner_upstream
    )
    grad_qkv = (own_qkv.astype(jnp.float32) + other_qkv.astype(jnp.float32)).astype(jnp.bfloat16)
    grad_out = (own_out.astype(jnp.float32) + other_out.astype(jnp.float32)).astype(jnp.bfloat16)
    acts_block = jnp.stack(forward_outs)[None, None]
    grads_block = jnp.stack(backward_outs)[None, None]
    return (acts_block, grads_block, grad_qkv[None, None], grad_out[None, None])


def solution(mesh):
    in_specs = (
        P("mirror", None, "tp", None),
        P("mirror", None, "tp"),
        P("mirror", None, None, None),
        P(),
        P("mirror", "section", None),
        P("mirror", "section", None, None, "tp"),
        P("mirror", "section", "tp", None),
        P("mirror", "section", "tp", None),
        P("mirror", "section", "tp", None),
        P("mirror", "section", None, "tp", None),
        P("mirror", None, "tp", None),
    )
    out_specs = (
        P("mirror", "section", None, "tp", None),
        P("mirror", "section", None, "tp", None),
        P("mirror", "section", None, None, "tp"),
        P("mirror", "section", "tp", None),
    )
    return jax.shard_map(shards, mesh=mesh, in_specs=in_specs, out_specs=out_specs, check_vma=False)
```

```python
import math

import numpy as np

import jax
import jax.numpy as jnp
from jax import lax
from jax.sharding import PartitionSpec as P

HD = 128


def passed_along(block, axis, distance):
    devices = range(lax.axis_size(axis))
    route = [(i - distance, i) for i in devices if i - distance in devices]
    return lax.ppermute(block, axis, route)


def flipped(value, axis, mask):
    return lax.ppermute(value, axis, [(i, i ^ mask) for i in range(lax.axis_size(axis))])


def normalize(values, gain_row):
    mean_square = jnp.mean(values * values, axis=-1, keepdims=True)
    return values * lax.rsqrt(mean_square + 1e-05) * gain_row


def segment_mask(segment_ids):
    position = jnp.arange(segment_ids.shape[0], dtype=jnp.int32)
    causal = position[None, :] <= position[:, None]
    return causal & (segment_ids[:, None] == segment_ids[None, :])


def attend(queries, keys_all, values_all, seg_mask):
    scores = jnp.einsum(
        "ihd,jhd->hij", queries, keys_all, preferred_element_type=jnp.float32
    ) / math.sqrt(queries.shape[-1])
    scores = jnp.where(seg_mask[None], scores, -1e30)
    highest = lax.stop_gradient(jnp.max(scores, axis=-1, keepdims=True))
    expo = jnp.exp(scores - highest)
    probs = (expo / jnp.sum(expo, axis=-1, keepdims=True)).astype(values_all.dtype)
    return jnp.einsum("hij,jhd->ihd", probs, values_all, preferred_element_type=jnp.float32)


def embedding(feat_rows, type_rows, type_table):
    onehot = (
        type_rows[:, None] == jnp.arange(type_table.shape[0], dtype=jnp.int32)[None, :]
    ).astype(jnp.bfloat16)
    looked = jnp.dot(onehot, type_table, preferred_element_type=jnp.float32)
    return (feat_rows.astype(jnp.float32) + looked).astype(jnp.bfloat16)


def gathered(blocks):
    full = lax.all_gather(jnp.stack(blocks), "tp", axis=1, tiled=True)
    return [full[i] for i in range(len(blocks))]


def scattered(blocks):
    part = lax.psum_scatter(jnp.stack(blocks), "tp", scatter_dimension=1, tiled=True)
    return [part[i] for i in range(len(blocks))]


def shards(
    feats, types, segs, type_table, gains, w_qkv, w_out, carry_acts, grad_in, saved, cotangent
):
    sections = lax.axis_size("section")
    section_index = lax.axis_index("section")
    on_first_pipe = lax.axis_index("mirror") == 0
    position = jnp.where(on_first_pipe, section_index, sections - 1 - section_index)
    gain_row = gains[0, 0]
    qkv_weight = w_qkv[0, 0]
    out_weight = w_out[0, 0]
    window_steps = feats.shape[1]
    seq_len = segs.shape[3]
    model_width = qkv_weight.shape[1]
    inner_here = qkv_weight.shape[-1]
    heads_here = inner_here // HD

    def mask_for(which, index):
        return segment_mask(lax.dynamic_index_in_dim(segs[0, which], index, 0, keepdims=False))

    def normed_rows(rows):
        return normalize(rows.astype(jnp.float32), gain_row).astype(jnp.bfloat16)

    def heads_of(normed_full):
        projected = jnp.einsum(
            "sd,cdn->csn", normed_full, qkv_weight, preferred_element_type=jnp.float32
        ).astype(jnp.bfloat16)
        return projected.reshape(3, seq_len, heads_here, HD)

    def forward_part(normed_full, seg_mask, heads_view=None):
        if heads_view is None:
            heads_view = heads_of(normed_full)
        mixed = (
            attend(heads_view[0], heads_view[1], heads_view[2], seg_mask)
            .reshape(seq_len, inner_here)
            .astype(jnp.bfloat16)
        )
        return mixed

    def backward_part(normed_full, upstream_full, seg_mask, heads_view=None):
        if heads_view is None:
            heads_view = heads_of(normed_full)
        primal, pull_attend = jax.vjp(
            lambda query_part, key_part, value_part: attend(
                query_part, key_part, value_part, seg_mask
            ),
            heads_view[0],
            heads_view[1],
            heads_view[2],
        )
        mixed = primal.reshape(seq_len, inner_here).astype(jnp.bfloat16)
        d_mixed = jnp.einsum(
            "sd,nd->sn", upstream_full, out_weight, preferred_element_type=jnp.float32
        ).astype(jnp.bfloat16)
        pulled = pull_attend(d_mixed.astype(jnp.float32).reshape(seq_len, heads_here, HD))
        d_projected = jnp.stack(pulled).reshape(3, seq_len, inner_here)
        return d_projected, mixed

    qkv_rows = jnp.transpose(qkv_weight, (0, 2, 1)).reshape(3 * inner_here, model_width)
    padded_out = jnp.concatenate(
        [out_weight, jnp.zeros((2 * inner_here, model_width), out_weight.dtype)], axis=0
    )
    block_weight = jnp.stack([qkv_rows, padded_out])

    def projected_back(d_projected, forward_mixed):
        lhs = jnp.stack(
            [
                jnp.transpose(d_projected, (1, 0, 2)).reshape(seq_len, 3 * inner_here),
                jnp.concatenate(
                    [forward_mixed, jnp.zeros((seq_len, 2 * inner_here), forward_mixed.dtype)],
                    axis=1,
                ),
            ]
        )
        return jnp.einsum(
            "tsk,tkd->tsd", lhs, block_weight, preferred_element_type=jnp.float32
        ).astype(jnp.bfloat16)

    def weight_terms(normed_fulls, d_projecteds, mixeds, upstream_fulls):
        qkv_sum = None
        out_sum = None
        for normed_full, d_projected, mixed, upstream_full in zip(
            normed_fulls, d_projecteds, mixeds, upstream_fulls
        ):
            qkv_term = jnp.einsum(
                "sd,csn->cdn", normed_full, d_projected, preferred_element_type=jnp.float32
            )
            out_term = jnp.einsum(
                "sn,sd->nd", mixed, upstream_full, preferred_element_type=jnp.float32
            )
            qkv_sum = qkv_term if qkv_sum is None else qkv_sum + qkv_term
            out_sum = out_term if out_sum is None else out_sum + out_term
        return qkv_sum.astype(jnp.bfloat16), out_sum.astype(jnp.bfloat16)

    def input_grad(layer_in, upstream, d_normed):
        unused_norm, pull_norm = jax.vjp(
            lambda inputs: normalize(inputs, gain_row), layer_in.astype(jnp.float32)
        )
        d_input = pull_norm(d_normed.astype(jnp.float32))[0]
        return (upstream.astype(jnp.float32) + d_input).astype(jnp.bfloat16)

    pair_axes = ("section", "mirror")
    mirror_size = lax.axis_size("mirror")
    up_pairs = []
    down_pairs = []
    for section in range(sections):
        for mirror in range(mirror_size):
            ahead = 1 if mirror == 0 else -1
            if 0 <= section + ahead < sections:
                up_pairs.append((section * mirror_size + mirror, (section + ahead) * mirror_size + mirror))
            if 0 <= section - ahead < sections:
                down_pairs.append((section * mirror_size + mirror, (section - ahead) * mirror_size + mirror))

    bit_count = lax.axis_size(pair_axes).bit_length() - 1
    section_bits = list(range(1, bit_count))
    if section_bits:
        routes = []
        for start in range(len(section_bits)):
            order = section_bits[start:] + section_bits[:start]
            routes.append([1 | (1 << order[0])] + [1 << bit for bit in order[1:]])
    else:
        routes = [[1]]

    def to_partner(value):
        return flipped(value, pair_axes, (1 << bit_count) - 1)

    last_step = window_steps - 1
    saved_normed = [normed_rows(saved[0, 0, t]) for t in range(window_steps)]
    backward_normed_full = [None] * window_steps
    upstream_fulls = []
    d_projecteds = []
    mixeds = []
    partner_normed = [None] * window_steps
    partner_upstream = []
    partner_d_projected = []
    partner_mixed = []
    forward_outs = []
    backward_outs = []
    forward_in = carry_acts[0, 0]
    backward_in = grad_in[0, 0]
    inbox = {}
    deferred = {}
    tie_scatter = {}
    for step_index in range(window_steps):
        embedded = embedding(feats[0, step_index], types[0, step_index], type_table)
        current = jnp.where(position == 0, embedded, forward_in)
        upstream = jnp.where(position == sections - 1, cotangent[0, step_index], backward_in)
        if step_index == 0:
            upstream_full, backward_normed_full[0], forward_normed_full = gathered(
                [upstream, saved_normed[0], normed_rows(current)]
            )
            first_sent = to_partner(jnp.stack([upstream_full, backward_normed_full[0]]))
            paired = jnp.einsum(
                "tsd,cdn->tcsn",
                jnp.stack([backward_normed_full[0], forward_normed_full]),
                qkv_weight,
                preferred_element_type=jnp.float32,
            ).astype(jnp.bfloat16)
            step_heads = [paired[t].reshape(3, seq_len, heads_here, HD) for t in range(2)]
        else:
            step_heads = [None, None]
            upstream_full, forward_normed_full = gathered([upstream, normed_rows(current)])
            inbox[f"rows{step_index}"] = to_partner(upstream_full)
        d_projected, mixed = backward_part(
            backward_normed_full[step_index],
            upstream_full,
            mask_for(1, step_index + position),
            step_heads[0],
        )
        upstream_fulls.append(upstream_full)
        d_projecteds.append(d_projected)
        mixeds.append(mixed)
        small = jnp.concatenate([d_projected, mixed[None]])
        if step_index < last_step:
            deferred[f"small{step_index}"] = small
        else:
            inbox[f"small{step_index}"] = to_partner(small)
        forward_mixed = forward_part(
            forward_normed_full, mask_for(0, step_index - position + sections - 1), step_heads[1]
        )
        both_parts, tie_scatter = lax.optimization_barrier(
            (projected_back(d_projected, forward_mixed), tie_scatter)
        )
        inbox.update(tie_scatter)
        tie_scatter = {}
        both_rows = lax.psum_scatter(both_parts, "tp", scatter_dimension=1, tiled=True)
        d_normed, attn_rows = both_rows[0], both_rows[1]
        if step_index == 0 and window_steps > 1:
            later_rows, d_normed = lax.optimization_barrier((saved_normed[1:], d_normed))
            later = gathered(later_rows)
            backward_normed_full[1:] = later
            deferred["later"] = jnp.stack(later)
        backward_out = input_grad(saved[0, 0, step_index], upstream, d_normed)
        forward_out = (current.astype(jnp.float32) + attn_rows.astype(jnp.float32)).astype(
            jnp.bfloat16
        )
        forward_outs.append(forward_out)
        backward_outs.append(backward_out)
        if step_index < last_step:
            backward_in = lax.ppermute(backward_out, pair_axes, down_pairs)
            forward_in = lax.ppermute(forward_out, pair_axes, up_pairs)
            if step_index == 0:
                deferred, first_sent, backward_in, forward_in = lax.optimization_barrier(
                    (deferred, first_sent, backward_in, forward_in)
                )
                inbox["first"] = first_sent
            else:
                deferred, backward_in, forward_in = lax.optimization_barrier(
                    (deferred, backward_in, forward_in)
                )
            tie_scatter = {key: to_partner(value) for key, value in deferred.items()}
            deferred = {}

    partner_upstream = [inbox["first"][0]] + [inbox[f"rows{t}"] for t in range(1, window_steps)]
    partner_normed = [inbox["first"][1]] + (
        [inbox["later"][t] for t in range(window_steps - 1)] if window_steps > 1 else []
    )
    partner_d_projected = [inbox[f"small{t}"][:3] for t in range(window_steps)]
    partner_mixed = [inbox[f"small{t}"][3] for t in range(window_steps)]
    own_qkv, own_out = weight_terms(backward_normed_full, d_projecteds, mixeds, upstream_fulls)
    other_qkv, other_out = weight_terms(
        partner_normed, partner_d_projected, partner_mixed, partner_upstream
    )
    grad_qkv = (own_qkv.astype(jnp.float32) + other_qkv.astype(jnp.float32)).astype(jnp.bfloat16)
    grad_out = (own_out.astype(jnp.float32) + other_out.astype(jnp.float32)).astype(jnp.bfloat16)
    acts_block = jnp.stack(forward_outs)[None, None]
    grads_block = jnp.stack(backward_outs)[None, None]
    return (acts_block, grads_block, grad_qkv[None, None], grad_out[None, None])


def solution(mesh):
    in_specs = (
        P("mirror", None, "tp", None),
        P("mirror", None, "tp"),
        P("mirror", None, None, None),
        P(),
        P("mirror", "section", None),
        P("mirror", "section", None, None, "tp"),
        P("mirror", "section", "tp", None),
        P("mirror", "section", "tp", None),
        P("mirror", "section", "tp", None),
        P("mirror", "section", None, "tp", None),
        P("mirror", None, "tp", None),
    )
    out_specs = (
        P("mirror", "section", None, "tp", None),
        P("mirror", "section", None, "tp", None),
        P("mirror", "section", None, None, "tp"),
        P("mirror", "section", "tp", None),
    )
    return jax.shard_map(shards, mesh=mesh, in_specs=in_specs, out_specs=out_specs, check_vma=False)
```

```python
import math

import numpy as np

import jax
import jax.numpy as jnp
from jax import lax
from jax.sharding import PartitionSpec as P

HD = 128


def passed_along(block, axis, distance):
    devices = range(lax.axis_size(axis))
    route = [(i - distance, i) for i in devices if i - distance in devices]
    return lax.ppermute(block, axis, route)


def flipped(value, axis, mask):
    return lax.ppermute(value, axis, [(i, i ^ mask) for i in range(lax.axis_size(axis))])


def normalize(values, gain_row):
    mean_square = jnp.mean(values * values, axis=-1, keepdims=True)
    return values * lax.rsqrt(mean_square + 1e-05) * gain_row


def segment_mask(segment_ids):
    position = jnp.arange(segment_ids.shape[0], dtype=jnp.int32)
    causal = position[None, :] <= position[:, None]
    return causal & (segment_ids[:, None] == segment_ids[None, :])


def attend(queries, keys_all, values_all, seg_mask):
    scores = jnp.einsum(
        "ihd,jhd->hij", queries, keys_all, preferred_element_type=jnp.float32
    ) / math.sqrt(queries.shape[-1])
    scores = jnp.where(seg_mask[None], scores, -1e30)
    highest = lax.stop_gradient(jnp.max(scores, axis=-1, keepdims=True))
    expo = jnp.exp(scores - highest)
    probs = (expo / jnp.sum(expo, axis=-1, keepdims=True)).astype(values_all.dtype)
    return jnp.einsum("hij,jhd->ihd", probs, values_all, preferred_element_type=jnp.float32)


def embedding(feat_rows, type_rows, type_table):
    onehot = (
        type_rows[:, None] == jnp.arange(type_table.shape[0], dtype=jnp.int32)[None, :]
    ).astype(jnp.bfloat16)
    looked = jnp.dot(onehot, type_table, preferred_element_type=jnp.float32)
    return (feat_rows.astype(jnp.float32) + looked).astype(jnp.bfloat16)


def gathered(blocks):
    full = lax.all_gather(jnp.stack(blocks), "tp", axis=1, tiled=True)
    return [full[i] for i in range(len(blocks))]


def scattered(blocks):
    part = lax.psum_scatter(jnp.stack(blocks), "tp", scatter_dimension=1, tiled=True)
    return [part[i] for i in range(len(blocks))]


def shards(
    feats, types, segs, type_table, gains, w_qkv, w_out, carry_acts, grad_in, saved, cotangent
):
    sections = lax.axis_size("section")
    section_index = lax.axis_index("section")
    on_first_pipe = lax.axis_index("mirror") == 0
    position = jnp.where(on_first_pipe, section_index, sections - 1 - section_index)
    gain_row = gains[0, 0]
    qkv_weight = w_qkv[0, 0]
    out_weight = w_out[0, 0]
    window_steps = feats.shape[1]
    seq_len = segs.shape[3]
    model_width = qkv_weight.shape[1]
    inner_here = qkv_weight.shape[-1]
    heads_here = inner_here // HD

    def mask_for(which, index):
        return segment_mask(lax.dynamic_index_in_dim(segs[0, which], index, 0, keepdims=False))

    def normed_rows(rows):
        return normalize(rows.astype(jnp.float32), gain_row).astype(jnp.bfloat16)

    def heads_of(normed_full):
        projected = jnp.einsum(
            "sd,cdn->csn", normed_full, qkv_weight, preferred_element_type=jnp.float32
        ).astype(jnp.bfloat16)
        return projected.reshape(3, seq_len, heads_here, HD)

    def forward_part(normed_full, seg_mask, heads_view=None):
        if heads_view is None:
            heads_view = heads_of(normed_full)
        mixed = (
            attend(heads_view[0], heads_view[1], heads_view[2], seg_mask)
            .reshape(seq_len, inner_here)
            .astype(jnp.bfloat16)
        )
        return mixed

    def backward_part(normed_full, upstream_full, seg_mask, heads_view=None):
        if heads_view is None:
            heads_view = heads_of(normed_full)
        primal, pull_attend = jax.vjp(
            lambda query_part, key_part, value_part: attend(
                query_part, key_part, value_part, seg_mask
            ),
            heads_view[0],
            heads_view[1],
            heads_view[2],
        )
        mixed = primal.reshape(seq_len, inner_here).astype(jnp.bfloat16)
        d_mixed = jnp.einsum(
            "sd,nd->sn", upstream_full, out_weight, preferred_element_type=jnp.float32
        ).astype(jnp.bfloat16)
        pulled = pull_attend(d_mixed.astype(jnp.float32).reshape(seq_len, heads_here, HD))
        d_projected = jnp.stack(pulled).reshape(3, seq_len, inner_here)
        return d_projected, mixed

    qkv_rows = jnp.transpose(qkv_weight, (0, 2, 1)).reshape(3 * inner_here, model_width)
    padded_out = jnp.concatenate(
        [out_weight, jnp.zeros((2 * inner_here, model_width), out_weight.dtype)], axis=0
    )
    block_weight = jnp.stack([qkv_rows, padded_out])

    def projected_back(d_projected, forward_mixed):
        lhs = jnp.stack(
            [
                jnp.transpose(d_projected, (1, 0, 2)).reshape(seq_len, 3 * inner_here),
                jnp.concatenate(
                    [forward_mixed, jnp.zeros((seq_len, 2 * inner_here), forward_mixed.dtype)],
                    axis=1,
                ),
            ]
        )
        return jnp.einsum(
            "tsk,tkd->tsd", lhs, block_weight, preferred_element_type=jnp.float32
        ).astype(jnp.bfloat16)

    def weight_terms(normed_fulls, d_projecteds, mixeds, upstream_fulls):
        qkv_sum = None
        out_sum = None
        for normed_full, d_projected, mixed, upstream_full in zip(
            normed_fulls, d_projecteds, mixeds, upstream_fulls
        ):
            qkv_term = jnp.einsum(
                "sd,csn->cdn", normed_full, d_projected, preferred_element_type=jnp.float32
            )
            out_term = jnp.einsum(
                "sn,sd->nd", mixed, upstream_full, preferred_element_type=jnp.float32
            )
            qkv_sum = qkv_term if qkv_sum is None else qkv_sum + qkv_term
            out_sum = out_term if out_sum is None else out_sum + out_term
        return qkv_sum.astype(jnp.bfloat16), out_sum.astype(jnp.bfloat16)

    def input_grad(layer_in, upstream, d_normed):
        unused_norm, pull_norm = jax.vjp(
            lambda inputs: normalize(inputs, gain_row), layer_in.astype(jnp.float32)
        )
        d_input = pull_norm(d_normed.astype(jnp.float32))[0]
        return (upstream.astype(jnp.float32) + d_input).astype(jnp.bfloat16)

    pair_axes = ("section", "mirror")
    mirror_size = lax.axis_size("mirror")
    up_pairs = []
    down_pairs = []
    for section in range(sections):
        for mirror in range(mirror_size):
            ahead = 1 if mirror == 0 else -1
            if 0 <= section + ahead < sections:
                up_pairs.append((section * mirror_size + mirror, (section + ahead) * mirror_size + mirror))
            if 0 <= section - ahead < sections:
                down_pairs.append((section * mirror_size + mirror, (section - ahead) * mirror_size + mirror))

    bit_count = lax.axis_size(pair_axes).bit_length() - 1
    section_bits = list(range(1, bit_count))
    if section_bits:
        routes = []
        for start in range(len(section_bits)):
            order = section_bits[start:] + section_bits[:start]
            routes.append([1 | (1 << order[0])] + [1 << bit for bit in order[1:]])
    else:
        routes = [[1]]

    def to_partner(value):
        return flipped(value, pair_axes, (1 << bit_count) - 1)

    last_step = window_steps - 1
    saved_normed = [normed_rows(saved[0, 0, t]) for t in range(window_steps)]
    backward_normed_full = [None] * window_steps
    upstream_fulls = []
    d_projecteds = []
    mixeds = []
    partner_normed = [None] * window_steps
    partner_upstream = []
    partner_d_projected = []
    partner_mixed = []
    forward_outs = []
    backward_outs = []
    forward_in = carry_acts[0, 0]
    backward_in = grad_in[0, 0]
    inbox = {}
    deferred = {}
    tie_scatter = {}
    for step_index in range(window_steps):
        embedded = embedding(feats[0, step_index], types[0, step_index], type_table)
        current = jnp.where(position == 0, embedded, forward_in)
        upstream = jnp.where(position == sections - 1, cotangent[0, step_index], backward_in)
        if step_index == 0:
            first_rows = lax.all_gather(
                jnp.stack([upstream, saved_normed[0], normed_rows(current)]),
                "tp",
                axis=1,
                tiled=True,
            )
            upstream_full, backward_normed_full[0], forward_normed_full = (
                first_rows[0],
                first_rows[1],
                first_rows[2],
            )
            first_sent = to_partner(first_rows)
            paired = jnp.einsum(
                "tsd,cdn->tcsn",
                jnp.stack([backward_normed_full[0], forward_normed_full]),
                qkv_weight,
                preferred_element_type=jnp.float32,
            ).astype(jnp.bfloat16)
            step_heads = [paired[t].reshape(3, seq_len, heads_here, HD) for t in range(2)]
        else:
            step_heads = [None, None]
            upstream_full, forward_normed_full = gathered([upstream, normed_rows(current)])
            inbox[f"rows{step_index}"] = to_partner(upstream_full)
        d_projected, mixed = backward_part(
            backward_normed_full[step_index],
            upstream_full,
            mask_for(1, step_index + position),
            step_heads[0],
        )
        upstream_fulls.append(upstream_full)
        d_projecteds.append(d_projected)
        mixeds.append(mixed)
        small = jnp.concatenate([d_projected, mixed[None]])
        if step_index < last_step:
            deferred[f"small{step_index}"] = small
        else:
            inbox[f"small{step_index}"] = to_partner(small)
        forward_mixed = forward_part(
            forward_normed_full, mask_for(0, step_index - position + sections - 1), step_heads[1]
        )
        both_parts, tie_scatter = lax.optimization_barrier(
            (projected_back(d_projected, forward_mixed), tie_scatter)
        )
        inbox.update(tie_scatter)
        tie_scatter = {}
        both_rows = lax.psum_scatter(both_parts, "tp", scatter_dimension=1, tiled=True)
        d_normed, attn_rows = both_rows[0], both_rows[1]
        if step_index == 0 and window_steps > 1:
            later_rows, d_normed = lax.optimization_barrier((saved_normed[1:], d_normed))
            later = gathered(later_rows)
            backward_normed_full[1:] = later
            deferred["later"] = jnp.stack(later)
        backward_out = input_grad(saved[0, 0, step_index], upstream, d_normed)
        forward_out = (current.astype(jnp.float32) + attn_rows.astype(jnp.float32)).astype(
            jnp.bfloat16
        )
        forward_outs.append(forward_out)
        backward_outs.append(backward_out)
        if step_index < last_step:
            backward_in = lax.ppermute(backward_out, pair_axes, down_pairs)
            forward_in = lax.ppermute(forward_out, pair_axes, up_pairs)
            if step_index == 0:
                deferred, first_sent, backward_in, forward_in = lax.optimization_barrier(
                    (deferred, first_sent, backward_in, forward_in)
                )
                inbox["first"] = first_sent
            else:
                deferred, backward_in, forward_in = lax.optimization_barrier(
                    (deferred, backward_in, forward_in)
                )
            tie_scatter = {key: to_partner(value) for key, value in deferred.items()}
            deferred = {}

    partner_upstream = [inbox["first"][0]] + [inbox[f"rows{t}"] for t in range(1, window_steps)]
    partner_normed = [inbox["first"][1]] + (
        [inbox["later"][t] for t in range(window_steps - 1)] if window_steps > 1 else []
    )
    partner_d_projected = [inbox[f"small{t}"][:3] for t in range(window_steps)]
    partner_mixed = [inbox[f"small{t}"][3] for t in range(window_steps)]
    own_qkv, own_out = weight_terms(backward_normed_full, d_projecteds, mixeds, upstream_fulls)
    other_qkv, other_out = weight_terms(
        partner_normed, partner_d_projected, partner_mixed, partner_upstream
    )
    grad_qkv = (own_qkv.astype(jnp.float32) + other_qkv.astype(jnp.float32)).astype(jnp.bfloat16)
    grad_out = (own_out.astype(jnp.float32) + other_out.astype(jnp.float32)).astype(jnp.bfloat16)
    acts_block = jnp.stack(forward_outs)[None, None]
    grads_block = jnp.stack(backward_outs)[None, None]
    return (acts_block, grads_block, grad_qkv[None, None], grad_out[None, None])


def solution(mesh):
    in_specs = (
        P("mirror", None, "tp", None),
        P("mirror", None, "tp"),
        P("mirror", None, None, None),
        P(),
        P("mirror", "section", None),
        P("mirror", "section", None, None, "tp"),
        P("mirror", "section", "tp", None),
        P("mirror", "section", "tp", None),
        P("mirror", "section", "tp", None),
        P("mirror", "section", None, "tp", None),
        P("mirror", None, "tp", None),
    )
    out_specs = (
        P("mirror", "section", None, "tp", None),
        P("mirror", "section", None, "tp", None),
        P("mirror", "section", None, None, "tp"),
        P("mirror", "section", "tp", None),
    )
    return jax.shard_map(shards, mesh=mesh, in_specs=in_specs, out_specs=out_specs, check_vma=False)
```

```python
import math

import numpy as np

import jax
import jax.numpy as jnp
from jax import lax
from jax.sharding import PartitionSpec as P

HD = 128


def passed_along(block, axis, distance):
    devices = range(lax.axis_size(axis))
    route = [(i - distance, i) for i in devices if i - distance in devices]
    return lax.ppermute(block, axis, route)


def flipped(value, axis, mask):
    return lax.ppermute(value, axis, [(i, i ^ mask) for i in range(lax.axis_size(axis))])


def normalize(values, gain_row):
    mean_square = jnp.mean(values * values, axis=-1, keepdims=True)
    return values * lax.rsqrt(mean_square + 1e-05) * gain_row


def segment_mask(segment_ids):
    position = jnp.arange(segment_ids.shape[0], dtype=jnp.int32)
    causal = position[None, :] <= position[:, None]
    return causal & (segment_ids[:, None] == segment_ids[None, :])


def attend(queries, keys_all, values_all, seg_mask):
    scores = jnp.einsum(
        "ihd,jhd->hij", queries, keys_all, preferred_element_type=jnp.float32
    ) / math.sqrt(queries.shape[-1])
    scores = jnp.where(seg_mask[None], scores, -1e30)
    highest = lax.stop_gradient(jnp.max(scores, axis=-1, keepdims=True))
    expo = jnp.exp(scores - highest)
    probs = (expo / jnp.sum(expo, axis=-1, keepdims=True)).astype(values_all.dtype)
    return jnp.einsum("hij,jhd->ihd", probs, values_all, preferred_element_type=jnp.float32)


def embedding(feat_rows, type_rows, type_table):
    onehot = (
        type_rows[:, None] == jnp.arange(type_table.shape[0], dtype=jnp.int32)[None, :]
    ).astype(jnp.bfloat16)
    looked = jnp.dot(onehot, type_table, preferred_element_type=jnp.float32)
    return (feat_rows.astype(jnp.float32) + looked).astype(jnp.bfloat16)


def gathered(blocks):
    full = lax.all_gather(jnp.stack(blocks), "tp", axis=1, tiled=True)
    return [full[i] for i in range(len(blocks))]


def scattered(blocks):
    part = lax.psum_scatter(jnp.stack(blocks), "tp", scatter_dimension=1, tiled=True)
    return [part[i] for i in range(len(blocks))]


def shards(
    feats, types, segs, type_table, gains, w_qkv, w_out, carry_acts, grad_in, saved, cotangent
):
    sections = lax.axis_size("section")
    section_index = lax.axis_index("section")
    on_first_pipe = lax.axis_index("mirror") == 0
    position = jnp.where(on_first_pipe, section_index, sections - 1 - section_index)
    gain_row = gains[0, 0]
    qkv_weight = w_qkv[0, 0]
    out_weight = w_out[0, 0]
    window_steps = feats.shape[1]
    seq_len = segs.shape[3]
    model_width = qkv_weight.shape[1]
    inner_here = qkv_weight.shape[-1]
    heads_here = inner_here // HD

    def mask_for(which, index):
        return segment_mask(lax.dynamic_index_in_dim(segs[0, which], index, 0, keepdims=False))

    def normed_rows(rows):
        return normalize(rows.astype(jnp.float32), gain_row).astype(jnp.bfloat16)

    def heads_of(normed_full):
        projected = jnp.einsum(
            "sd,cdn->csn", normed_full, qkv_weight, preferred_element_type=jnp.float32
        ).astype(jnp.bfloat16)
        return projected.reshape(3, seq_len, heads_here, HD)

    def forward_part(normed_full, seg_mask, heads_view=None):
        if heads_view is None:
            heads_view = heads_of(normed_full)
        mixed = (
            attend(heads_view[0], heads_view[1], heads_view[2], seg_mask)
            .reshape(seq_len, inner_here)
            .astype(jnp.bfloat16)
        )
        return mixed

    def backward_part(normed_full, upstream_full, seg_mask, heads_view=None):
        if heads_view is None:
            heads_view = heads_of(normed_full)
        primal, pull_attend = jax.vjp(
            lambda query_part, key_part, value_part: attend(
                query_part, key_part, value_part, seg_mask
            ),
            heads_view[0],
            heads_view[1],
            heads_view[2],
        )
        mixed = primal.reshape(seq_len, inner_here).astype(jnp.bfloat16)
        d_mixed = jnp.einsum(
            "sd,nd->sn", upstream_full, out_weight, preferred_element_type=jnp.float32
        ).astype(jnp.bfloat16)
        pulled = pull_attend(d_mixed.astype(jnp.float32).reshape(seq_len, heads_here, HD))
        d_projected = jnp.stack(pulled).reshape(3, seq_len, inner_here)
        return d_projected, mixed

    qkv_rows = jnp.transpose(qkv_weight, (0, 2, 1)).reshape(3 * inner_here, model_width)
    padded_out = jnp.concatenate(
        [out_weight, jnp.zeros((2 * inner_here, model_width), out_weight.dtype)], axis=0
    )
    block_weight = jnp.stack([qkv_rows, padded_out])

    def projected_back(d_projected, forward_mixed):
        lhs = jnp.stack(
            [
                jnp.transpose(d_projected, (1, 0, 2)).reshape(seq_len, 3 * inner_here),
                jnp.concatenate(
                    [forward_mixed, jnp.zeros((seq_len, 2 * inner_here), forward_mixed.dtype)],
                    axis=1,
                ),
            ]
        )
        return jnp.einsum(
            "tsk,tkd->tsd", lhs, block_weight, preferred_element_type=jnp.float32
        ).astype(jnp.bfloat16)

    def weight_terms(normed_fulls, d_projecteds, mixeds, upstream_fulls):
        qkv_sum = None
        out_sum = None
        for normed_full, d_projected, mixed, upstream_full in zip(
            normed_fulls, d_projecteds, mixeds, upstream_fulls
        ):
            qkv_term = jnp.einsum(
                "sd,csn->cdn", normed_full, d_projected, preferred_element_type=jnp.float32
            )
            out_term = jnp.einsum(
                "sn,sd->nd", mixed, upstream_full, preferred_element_type=jnp.float32
            )
            qkv_sum = qkv_term if qkv_sum is None else qkv_sum + qkv_term
            out_sum = out_term if out_sum is None else out_sum + out_term
        return qkv_sum.astype(jnp.bfloat16), out_sum.astype(jnp.bfloat16)

    def input_grad(layer_in, upstream, d_normed):
        unused_norm, pull_norm = jax.vjp(
            lambda inputs: normalize(inputs, gain_row), layer_in.astype(jnp.float32)
        )
        d_input = pull_norm(d_normed.astype(jnp.float32))[0]
        return (upstream.astype(jnp.float32) + d_input).astype(jnp.bfloat16)

    pair_axes = ("section", "mirror")
    mirror_size = lax.axis_size("mirror")
    up_pairs = []
    down_pairs = []
    for section in range(sections):
        for mirror in range(mirror_size):
            ahead = 1 if mirror == 0 else -1
            if 0 <= section + ahead < sections:
                up_pairs.append((section * mirror_size + mirror, (section + ahead) * mirror_size + mirror))
            if 0 <= section - ahead < sections:
                down_pairs.append((section * mirror_size + mirror, (section - ahead) * mirror_size + mirror))

    bit_count = lax.axis_size(pair_axes).bit_length() - 1
    section_bits = list(range(1, bit_count))
    if section_bits:
        routes = []
        for start in range(len(section_bits)):
            order = section_bits[start:] + section_bits[:start]
            routes.append([1 | (1 << order[0])] + [1 << bit for bit in order[1:]])
    else:
        routes = [[1]]

    def to_partner(value):
        return flipped(value, pair_axes, (1 << bit_count) - 1)

    last_step = window_steps - 1
    saved_normed = [normed_rows(saved[0, 0, t]) for t in range(window_steps)]
    backward_normed_full = [None] * window_steps
    upstream_fulls = []
    d_projecteds = []
    mixeds = []
    partner_normed = [None] * window_steps
    partner_upstream = []
    partner_d_projected = []
    partner_mixed = []
    forward_outs = []
    backward_outs = []
    forward_in = carry_acts[0, 0]
    backward_in = grad_in[0, 0]
    inbox = {}
    deferred = {}
    tie_scatter = {}
    for step_index in range(window_steps):
        embedded = embedding(feats[0, step_index], types[0, step_index], type_table)
        current = jnp.where(position == 0, embedded, forward_in)
        upstream = jnp.where(position == sections - 1, cotangent[0, step_index], backward_in)
        if step_index == 0:
            upstream_full, backward_normed_full[0], forward_normed_full = gathered(
                [upstream, saved_normed[0], normed_rows(current)]
            )
            first_sent = to_partner(upstream_full)
            deferred["normed0"] = backward_normed_full[0]
            paired = jnp.einsum(
                "tsd,cdn->tcsn",
                jnp.stack([backward_normed_full[0], forward_normed_full]),
                qkv_weight,
                preferred_element_type=jnp.float32,
            ).astype(jnp.bfloat16)
            step_heads = [paired[t].reshape(3, seq_len, heads_here, HD) for t in range(2)]
        else:
            step_heads = [None, None]
            upstream_full, forward_normed_full = gathered([upstream, normed_rows(current)])
            inbox[f"rows{step_index}"] = to_partner(upstream_full)
        d_projected, mixed = backward_part(
            backward_normed_full[step_index],
            upstream_full,
            mask_for(1, step_index + position),
            step_heads[0],
        )
        upstream_fulls.append(upstream_full)
        d_projecteds.append(d_projected)
        mixeds.append(mixed)
        small = jnp.concatenate([d_projected, mixed[None]])
        if step_index < last_step:
            deferred[f"small{step_index}"] = small
        else:
            inbox[f"small{step_index}"] = to_partner(small)
        forward_mixed = forward_part(
            forward_normed_full, mask_for(0, step_index - position + sections - 1), step_heads[1]
        )
        both_parts, tie_scatter = lax.optimization_barrier(
            (projected_back(d_projected, forward_mixed), tie_scatter)
        )
        inbox.update(tie_scatter)
        tie_scatter = {}
        both_rows = lax.psum_scatter(both_parts, "tp", scatter_dimension=1, tiled=True)
        d_normed, attn_rows = both_rows[0], both_rows[1]
        if step_index == 0 and window_steps > 1:
            later_rows, d_normed = lax.optimization_barrier((saved_normed[1:], d_normed))
            later = gathered(later_rows)
            backward_normed_full[1:] = later
            deferred["later"] = jnp.stack(later)
        backward_out = input_grad(saved[0, 0, step_index], upstream, d_normed)
        forward_out = (current.astype(jnp.float32) + attn_rows.astype(jnp.float32)).astype(
            jnp.bfloat16
        )
        forward_outs.append(forward_out)
        backward_outs.append(backward_out)
        if step_index < last_step:
            backward_in = lax.ppermute(backward_out, pair_axes, down_pairs)
            forward_in = lax.ppermute(forward_out, pair_axes, up_pairs)
            if step_index == 0:
                deferred, first_sent, backward_in, forward_in = lax.optimization_barrier(
                    (deferred, first_sent, backward_in, forward_in)
                )
                inbox["first"] = first_sent
            else:
                deferred, backward_in, forward_in = lax.optimization_barrier(
                    (deferred, backward_in, forward_in)
                )
            tie_scatter = {key: to_partner(value) for key, value in deferred.items()}
            deferred = {}

    partner_upstream = [inbox["first"]] + [inbox[f"rows{t}"] for t in range(1, window_steps)]
    partner_normed = [inbox["normed0"]] + (
        [inbox["later"][t] for t in range(window_steps - 1)] if window_steps > 1 else []
    )
    partner_d_projected = [inbox[f"small{t}"][:3] for t in range(window_steps)]
    partner_mixed = [inbox[f"small{t}"][3] for t in range(window_steps)]
    own_qkv, own_out = weight_terms(backward_normed_full, d_projecteds, mixeds, upstream_fulls)
    other_qkv, other_out = weight_terms(
        partner_normed, partner_d_projected, partner_mixed, partner_upstream
    )
    grad_qkv = (own_qkv.astype(jnp.float32) + other_qkv.astype(jnp.float32)).astype(jnp.bfloat16)
    grad_out = (own_out.astype(jnp.float32) + other_out.astype(jnp.float32)).astype(jnp.bfloat16)
    acts_block = jnp.stack(forward_outs)[None, None]
    grads_block = jnp.stack(backward_outs)[None, None]
    return (acts_block, grads_block, grad_qkv[None, None], grad_out[None, None])


def solution(mesh):
    in_specs = (
        P("mirror", None, "tp", None),
        P("mirror", None, "tp"),
        P("mirror", None, None, None),
        P(),
        P("mirror", "section", None),
        P("mirror", "section", None, None, "tp"),
        P("mirror", "section", "tp", None),
        P("mirror", "section", "tp", None),
        P("mirror", "section", "tp", None),
        P("mirror", "section", None, "tp", None),
        P("mirror", None, "tp", None),
    )
    out_specs = (
        P("mirror", "section", None, "tp", None),
        P("mirror", "section", None, "tp", None),
        P("mirror", "section", None, None, "tp"),
        P("mirror", "section", "tp", None),
    )
    return jax.shard_map(shards, mesh=mesh, in_specs=in_specs, out_specs=out_specs, check_vma=False)
```
